32 devices in a mesh: slab: 4 (over x, core), ctx: 8 (over z, y).
Axes of the slice: x: 2, y: 2, z: 4, core: 2. Of those that a mesh axis runs over, the one named last changes fastest.
Arguments:
- queries: bfloat16 [32768, 2048], P(('slab', 'ctx'))
- keys: bfloat16 [32768, 1024], P(('slab', 'ctx'))
- values: bfloat16 [32768, 1024], P(('slab', 'ctx')), may hold values from -6 to 6
- output_gradient: bfloat16 [32768, 2048], P(('slab', 'ctx')), may hold values from -6 to 6
- reach: int32 [32768], P(('slab', 'ctx')), may hold values from 1 to 1024, as said below
Outputs:
- grad_queries: bfloat16 [32768, 2048], P(('slab', 'ctx'))
- grad_keys: bfloat16 [32768, 1024], P(('slab', 'ctx'))
- grad_values: bfloat16 [32768, 1024], P(('slab', 'ctx'))
The draws below stay inside these ranges and needn't reach their ends.
Inputs may be any that keep to these rules, and one draw needn't show every extreme that they name: reach[i] is the smaller of 1024 and i + 1 - (the first token of the document that holds token i); documents begin at token 0 and at most once in every aligned block of 1024 tokens.
All inputs are finite; a program needn't handle non-finite values.
Results may differ from the reference program's by a relative error of at most 0.005.
Values may be sent and summed in bfloat16 or wider, within the bound.
No kernel may reach another device: no remote copies, remote signals or barrier semaphores. Data moves between devices by JAX's collectives and lax.ppermute only.
A program may use at most 192 MiB of HBM per device.

```python
import jax
import jax.numpy as jnp
from jax import lax

HEAD_DIMENSION = 128
QUERY_HEADS = 16
KEY_VALUE_HEADS = 8
WINDOW_TOKENS = 1024
QPRE = 168
TOK_DEV = 1024
DOCUMENT_TOKENS = 32768


def paired_draw(key):
    base_q = jax.random.normal(jax.random.fold_in(key, 11), (DOCUMENT_TOKENS, QUERY_HEADS * HEAD_DIMENSION), jnp.float32)
    key_offset = jax.random.normal(jax.random.fold_in(key, 12), (DOCUMENT_TOKENS, KEY_VALUE_HEADS * HEAD_DIMENSION), jnp.float32)
    return (base_q, key_offset)


def draw_queries(key, part):
    return paired_draw(key)[0].astype(jnp.bfloat16)


def draw_keys(key, part):
    return paired_draw(key)[1].astype(jnp.bfloat16)


def draw_reach(key, part):
    blocks = DOCUMENT_TOKENS // TOK_DEV
    starts_here = jax.random.randint(jax.random.fold_in(key, 21), (blocks,), 0, 2, dtype=jnp.int32)
    offsets = jax.random.randint(jax.random.fold_in(key, 22), (blocks,), 0, TOK_DEV, dtype=jnp.int32)
    starts_here = starts_here.at[0].set(1)
    offsets = offsets.at[0].set(0)
    where_at = jnp.arange(blocks, dtype=jnp.int32) * TOK_DEV + offsets
    marks = jnp.zeros((DOCUMENT_TOKENS,), jnp.int32).at[where_at].max(where_at * starts_here)
    doc_first = lax.cummax(marks)
    position = jnp.arange(DOCUMENT_TOKENS, dtype=jnp.int32)
    return jnp.minimum(WINDOW_TOKENS, position - doc_first + 1).astype(jnp.int32)


def shard_levels(stream_key, dims, pieces, low, largest):
    factor_of = 1.0
    for dim, parts in pieces:
        heights = jax.random.uniform(jax.random.fold_in(jax.random.fold_in(stream_key, 6), dim), (parts,), jnp.float32, low / len(pieces), largest / len(pieces))
        factor_of = factor_of * jnp.repeat(jnp.exp(heights), dims[dim] // parts).reshape((-1,) + (1,) * (len(dims) - 1 - dim))
    return factor_of


def noise(stream_key, shape, scale, limit, split=(), kind=jnp.bfloat16):
    result = scale * jax.random.normal(stream_key, shape, jnp.float32)
    if split:
        result = result * shard_levels(stream_key, shape, split, -0.22, 0.18)
    return jnp.clip(result, -limit, limit).astype(kind)


def setup_inputs(seed: int = 0) -> dict:
    splits = jax.random.split(jax.random.key(seed), 6)
    queries = draw_queries(jax.random.fold_in(splits[5], 71), 0)
    keys = draw_keys(jax.random.fold_in(splits[5], 71), 0)
    values = noise(splits[2], (DOCUMENT_TOKENS, KEY_VALUE_HEADS * HEAD_DIMENSION), 1.0, 6.0, ((0, 32),))
    output_gradient = noise(splits[3], (DOCUMENT_TOKENS, QUERY_HEADS * HEAD_DIMENSION), 1.0, 6.0, ((0, 32),))
    reach = draw_reach(jax.random.fold_in(splits[5], 71), 0)
    return {"queries": queries, "keys": keys, "values": values, "output_gradient": output_gradient, "reach": reach}


def reference(queries, keys, values, output_gradient, reach):
    scale = jnp.float32(QPRE ** -0.5)
    block_rows = min(256, TOK_DEV)
    window_extent = WINDOW_TOKENS + block_rows
    padding_rows = jnp.zeros((WINDOW_TOKENS, KEY_VALUE_HEADS * HEAD_DIMENSION), keys.dtype)
    extended_keys = jnp.concatenate([padding_rows, keys], axis=0)
    extended_values = jnp.concatenate([padding_rows, values], axis=0)
    extended_key_gradient = jnp.zeros((DOCUMENT_TOKENS + WINDOW_TOKENS, KEY_VALUE_HEADS * HEAD_DIMENSION), jnp.float32)
    extended_value_gradient = jnp.zeros((DOCUMENT_TOKENS + WINDOW_TOKENS, KEY_VALUE_HEADS * HEAD_DIMENSION), jnp.float32)

    def step(carry, index):
        acc_keys, acc_values = carry
        leading_index = (index * block_rows).astype(jnp.int32)
        query_portion = lax.dynamic_slice_in_dim(queries, leading_index, block_rows, 0).astype(jnp.float32).reshape(block_rows, KEY_VALUE_HEADS, 2, HEAD_DIMENSION)
        gradient_portion = lax.dynamic_slice_in_dim(output_gradient, leading_index, block_rows, 0).astype(jnp.float32).reshape(block_rows, KEY_VALUE_HEADS, 2, HEAD_DIMENSION)
        key_portion = lax.dynamic_slice_in_dim(extended_keys, leading_index, window_extent, 0).astype(jnp.float32).reshape(window_extent, KEY_VALUE_HEADS, HEAD_DIMENSION)
        value_portion = lax.dynamic_slice_in_dim(extended_values, leading_index, window_extent, 0).astype(jnp.float32).reshape(window_extent, KEY_VALUE_HEADS, HEAD_DIMENSION)
        r_part = lax.dynamic_slice_in_dim(reach, leading_index, block_rows, 0)
        q_pos = leading_index + jnp.arange(block_rows, dtype=jnp.int32)
        k_pos = leading_index - WINDOW_TOKENS + jnp.arange(window_extent, dtype=jnp.int32)
        visible = (k_pos[None, :] <= q_pos[:, None]) & (k_pos[None, :] > q_pos[:, None] - r_part[:, None])
        scores = jnp.einsum('qhgd,khd->hgqk', query_portion, key_portion) * scale
        scores = jnp.where(visible, scores, jnp.float32(-1e30))
        top = jnp.max(scores, axis=-1, keepdims=True)
        expo = jnp.where(visible, jnp.exp(scores - top), jnp.float32(0.0))
        probs = expo / jnp.sum(expo, axis=-1, keepdims=True)
        probability_lowprecision = lax.optimization_barrier(probs.astype(jnp.bfloat16)).astype(jnp.float32)
        dprobs = jnp.einsum('qhgd,khd->hgqk', gradient_portion, value_portion)
        delta = jnp.sum(probs * dprobs, axis=-1, keepdims=True)
        score_gradient = lax.optimization_barrier((scale * probs * (dprobs - delta)).astype(jnp.bfloat16)).astype(jnp.float32)
        dq_block = jnp.einsum('hgqk,khd->qhgd', score_gradient, key_portion).reshape(block_rows, QUERY_HEADS * HEAD_DIMENSION).astype(jnp.bfloat16)
        key_gradient_block = jnp.einsum('lwim,ilwr->mlr', score_gradient, query_portion).reshape(window_extent, KEY_VALUE_HEADS * HEAD_DIMENSION)
        value_gradient_block = jnp.einsum('lwim,ilwr->mlr', probability_lowprecision, gradient_portion).reshape(window_extent, KEY_VALUE_HEADS * HEAD_DIMENSION)
        acc_keys = lax.dynamic_update_slice_in_dim(acc_keys, lax.dynamic_slice_in_dim(acc_keys, leading_index, window_extent, 0) + key_gradient_block, leading_index, 0)
        acc_values = lax.dynamic_update_slice_in_dim(acc_values, lax.dynamic_slice_in_dim(acc_values, leading_index, window_extent, 0) + value_gradient_block, leading_index, 0)
        return (acc_keys, acc_values), dq_block

    (extended_key_gradient, extended_value_gradient), dq_blocks = lax.scan(step, (extended_key_gradient, extended_value_gradient), jnp.arange(DOCUMENT_TOKENS // block_rows, dtype=jnp.int32))
    grad_queries = dq_blocks.reshape(DOCUMENT_TOKENS, QUERY_HEADS * HEAD_DIMENSION)
    grad_keys = extended_key_gradient[WINDOW_TOKENS:].astype(jnp.bfloat16)
    grad_values = extended_value_gradient[WINDOW_TOKENS:].astype(jnp.bfloat16)
    return (grad_queries, grad_keys, grad_values)
```

```python
import functools

import jax
import jax.numpy as jnp
from jax import lax
from jax.experimental import pallas as pl
from jax.experimental.pallas import tpu as pltpu
from jax.sharding import PartitionSpec as P

HEAD_DIMENSION = 128
WINDOW_TOKENS = 1024
QPRE = 168
BLOCK_Q = 128

NT_DIMS = (((1,), (1,)), ((), ()))
TN_DIMS = (((0,), (0,)), ((), ()))


def doc_shift(x, by):
    count = lax.axis_size("slab") * lax.axis_size("ctx")
    pairs = [(i, i + by) for i in range(count) if 0 <= i + by < count]
    return lax.ppermute(x, ("slab", "ctx"), pairs)


def attention_kernel(reach_ref, q_ref, do_ref, kp_ref, vp_ref, ko_ref, vo_ref,
                     dq_ref, dko_ref, dvo_ref, dkp_ref, dvp_ref,
                     kext, vext, dkacc, dvacc):
    rows = q_ref.shape[0]
    d = HEAD_DIMENSION
    w = WINDOW_TOKENS
    span = BLOCK_Q + w
    scale = jnp.float32(QPRE ** (-0.5))

    kext[0:w, :] = kp_ref[...]
    kext[w:w + rows, :] = ko_ref[...]
    vext[0:w, :] = vp_ref[...]
    vext[w:w + rows, :] = vo_ref[...]
    dkacc[...] = jnp.zeros_like(dkacc)
    dvacc[...] = jnp.zeros_like(dvacc)

    offsets = (lax.broadcasted_iota(jnp.int32, (BLOCK_Q, span), 1)
               - lax.broadcasted_iota(jnp.int32, (BLOCK_Q, span), 0))

    def body(b, carry):
        r0 = pl.multiple_of(b * BLOCK_Q, BLOCK_Q)
        q = q_ref[pl.ds(r0, BLOCK_Q), :]
        do = do_ref[pl.ds(r0, BLOCK_Q), :]
        q2 = jnp.concatenate([q[:, :d], q[:, d:]], axis=0)
        do2 = jnp.concatenate([do[:, :d], do[:, d:]], axis=0)
        kw = kext[pl.ds(r0, span), :]
        vw = vext[pl.ds(r0, span), :]
        reach = reach_ref[pl.ds(r0, BLOCK_Q), :]
        visible = (offsets <= w) & (offsets > w - reach)
        visible = jnp.concatenate([visible, visible], axis=0)
        s = lax.dot_general(q2, kw, NT_DIMS, preferred_element_type=jnp.float32)
        s = jnp.where(visible, s, -jnp.inf)
        top = jnp.max(s, axis=-1, keepdims=True)
        e = jnp.exp((s - top) * scale)
        total = jnp.sum(e, axis=-1, keepdims=True)
        p = e * (1.0 / total)
        dp = lax.dot_general(do2, vw, NT_DIMS, preferred_element_type=jnp.float32)
        delta = jnp.sum(p * dp, axis=-1, keepdims=True)
        ds = (scale * p * (dp - delta)).astype(jnp.bfloat16)
        pb = p.astype(jnp.bfloat16)
        dq2 = jnp.dot(ds, kw, preferred_element_type=jnp.float32)
        dq_ref[pl.ds(r0, BLOCK_Q), :] = jnp.concatenate(
            [dq2[:BLOCK_Q], dq2[BLOCK_Q:]], axis=1).astype(dq_ref.dtype)
        dk = lax.dot_general(ds, q2, TN_DIMS, preferred_element_type=jnp.float32)
        dv = lax.dot_general(pb, do2, TN_DIMS, preferred_element_type=jnp.float32)
        dkacc[pl.ds(r0, span), :] += dk
        dvacc[pl.ds(r0, span), :] += dv
        return carry

    lax.fori_loop(0, rows // BLOCK_Q, body, 0)
    dko_ref[...] = dkacc[w:w + rows, :]
    dvo_ref[...] = dvacc[w:w + rows, :]
    dkp_ref[...] = dkacc[0:w, :].astype(dkp_ref.dtype)
    dvp_ref[...] = dvacc[0:w, :].astype(dvp_ref.dtype)


def attention_block(queries, output_gradient, keys_prev, values_prev, keys, values, reach):
    rows, q_width = queries.shape
    kv_width = keys.shape[1]
    heads = kv_width // HEAD_DIMENSION
    d = HEAD_DIMENSION
    w = WINDOW_TOKENS
    reach_col = reach.reshape(rows, 1)
    q_spec = pl.BlockSpec((rows, 2 * d), lambda g: (0, g))
    own_spec = pl.BlockSpec((rows, d), lambda g: (0, g))
    prev_spec = pl.BlockSpec((w, d), lambda g: (0, g))
    flops = heads * (rows // BLOCK_Q) * 5 * 2 * (2 * BLOCK_Q) * (BLOCK_Q + w) * d
    cost = pl.CostEstimate(
        flops=flops,
        transcendentals=heads * rows * 2 * (BLOCK_Q + w),
        bytes_accessed=2 * (2 * rows * q_width + 2 * (rows + w) * kv_width + rows * q_width)
        + 4 * 2 * rows * kv_width + 2 * 2 * w * kv_width,
    )
    return pl.pallas_call(
        attention_kernel,
        grid=(heads,),
        in_specs=[
            pl.BlockSpec((rows, 1), lambda g: (0, 0)),
            q_spec, q_spec, prev_spec, prev_spec, own_spec, own_spec,
        ],
        out_specs=[q_spec, own_spec, own_spec, prev_spec, prev_spec],
        out_shape=[
            jax.ShapeDtypeStruct((rows, q_width), jnp.bfloat16),
            jax.ShapeDtypeStruct((rows, kv_width), jnp.float32),
            jax.ShapeDtypeStruct((rows, kv_width), jnp.float32),
            jax.ShapeDtypeStruct((w, kv_width), jnp.bfloat16),
            jax.ShapeDtypeStruct((w, kv_width), jnp.bfloat16),
        ],
        scratch_shapes=[
            pltpu.VMEM((w + rows, d), jnp.bfloat16),
            pltpu.VMEM((w + rows, d), jnp.bfloat16),
            pltpu.VMEM((w + rows, d), jnp.float32),
            pltpu.VMEM((w + rows, d), jnp.float32),
        ],
        compiler_params=pltpu.CompilerParams(dimension_semantics=("arbitrary",)),
        cost_estimate=cost,
    )(reach_col, queries, output_gradient, keys_prev, values_prev, keys, values)


def on_device(queries, keys, values, output_gradient, reach):
    rows = queries.shape[0]
    w = WINDOW_TOKENS
    tail = jnp.stack([keys[rows - w:], values[rows - w:]])
    previous = doc_shift(tail, 1)
    grad_q, dk_own, dv_own, dk_prev, dv_prev = attention_block(
        queries, output_gradient, previous[0], previous[1], keys, values, reach)
    incoming = doc_shift(jnp.stack([dk_prev, dv_prev]), -1).astype(jnp.float32)
    grad_keys = dk_own.at[rows - w:].add(incoming[0]).astype(jnp.bfloat16)
    grad_values = dv_own.at[rows - w:].add(incoming[1]).astype(jnp.bfloat16)
    return (grad_q, grad_keys, grad_values)


def solution(mesh):
    placed = (
        P(("slab", "ctx"), None),
        P(("slab", "ctx"), None),
        P(("slab", "ctx"), None),
        P(("slab", "ctx"), None),
        P(("slab", "ctx")),
    )
    return jax.shard_map(
        on_device,
        mesh=mesh,
        in_specs=placed,
        out_specs=(P(("slab", "ctx"), None), P(("slab", "ctx"), None), P(("slab", "ctx"), None)),
        check_vma=False,
    )
```

```python
import functools

import jax
import jax.numpy as jnp
from jax import lax
from jax.experimental import pallas as pl
from jax.experimental.pallas import tpu as pltpu
from jax.sharding import PartitionSpec as P

HEAD_DIMENSION = 128
WINDOW_TOKENS = 1024
QPRE = 168
BLOCK_Q = 128

NT_DIMS = (((1,), (1,)), ((), ()))
TN_DIMS = (((0,), (0,)), ((), ()))


def doc_shift(x, by):
    count = lax.axis_size("slab") * lax.axis_size("ctx")
    pairs = [(i, i + by) for i in range(count) if 0 <= i + by < count]
    return lax.ppermute(x, ("slab", "ctx"), pairs)


def attention_kernel(reach_ref, q_ref, do_ref, ko_ref, vo_ref, prev_ref,
                     dq_in, dk_in, dv_in,
                     dq_ref, dko_ref, dvo_ref, dprev_ref,
                     kext, vext, dkacc, dvacc):
    rows = q_ref.shape[0]
    d = HEAD_DIMENSION
    w = WINDOW_TOKENS
    span = BLOCK_Q + w
    scale = jnp.float32(QPRE ** (-0.5))

    kext[0:w, :] = prev_ref[0]
    kext[w:w + rows, :] = ko_ref[...]
    vext[0:w, :] = prev_ref[1]
    vext[w:w + rows, :] = vo_ref[...]
    dkacc[...] = jnp.zeros_like(dkacc)
    dvacc[...] = jnp.zeros_like(dvacc)

    offsets = (lax.broadcasted_iota(jnp.int32, (BLOCK_Q, span), 1)
               - lax.broadcasted_iota(jnp.int32, (BLOCK_Q, span), 0))

    def body(b, carry):
        r0 = pl.multiple_of(b * BLOCK_Q, BLOCK_Q)
        q = q_ref[pl.ds(r0, BLOCK_Q), :]
        do = do_ref[pl.ds(r0, BLOCK_Q), :]
        q2 = jnp.concatenate([q[:, :d], q[:, d:]], axis=0)
        do2 = jnp.concatenate([do[:, :d], do[:, d:]], axis=0)
        kw = kext[pl.ds(r0, span), :]
        vw = vext[pl.ds(r0, span), :]
        reach = reach_ref[pl.ds(r0, BLOCK_Q), :]
        visible = (offsets <= w) & (offsets > w - reach)
        visible = jnp.concatenate([visible, visible], axis=0)
        s = lax.dot_general(q2, kw, NT_DIMS, preferred_element_type=jnp.float32)
        s = jnp.where(visible, s, -jnp.inf)
        top = jnp.max(s, axis=-1, keepdims=True)
        e = jnp.exp((s - top) * scale)
        total = jnp.sum(e, axis=-1, keepdims=True)
        p = e * (1.0 / total)
        dp = lax.dot_general(do2, vw, NT_DIMS, preferred_element_type=jnp.float32)
        delta = jnp.sum(p * dp, axis=-1, keepdims=True)
        ds = (scale * p * (dp - delta)).astype(jnp.bfloat16)
        pb = p.astype(jnp.bfloat16)
        dq2 = jnp.dot(ds, kw, preferred_element_type=jnp.float32)
        dq_ref[pl.ds(r0, BLOCK_Q), :] = jnp.concatenate(
            [dq2[:BLOCK_Q], dq2[BLOCK_Q:]], axis=1).astype(dq_ref.dtype)
        dk = lax.dot_general(ds, q2, TN_DIMS, preferred_element_type=jnp.float32)
        dv = lax.dot_general(pb, do2, TN_DIMS, preferred_element_type=jnp.float32)
        dkacc[pl.ds(r0, span), :] += dk
        dvacc[pl.ds(r0, span), :] += dv
        return carry

    lax.fori_loop(0, rows // BLOCK_Q, body, 0)
    dko_ref[...] = dkacc[w:w + rows, :]
    dvo_ref[...] = dvacc[w:w + rows, :]
    dprev_ref[0] = dkacc[0:w, :].astype(dprev_ref.dtype)
    dprev_ref[1] = dvacc[0:w, :].astype(dprev_ref.dtype)


def attention_head(g, reach_col, queries, output_gradient, keys, values, previous,
                   dq_buf, dk_buf, dv_buf):
    rows, q_width = queries.shape
    kv_width = keys.shape[1]
    d = HEAD_DIMENSION
    w = WINDOW_TOKENS
    q_spec = pl.BlockSpec((rows, 2 * d), lambda i: (0, g))
    own_spec = pl.BlockSpec((rows, d), lambda i: (0, g))
    prev_spec = pl.BlockSpec((2, w, d), lambda i: (0, 0, 0))
    any_spec = pl.BlockSpec(memory_space=pl.ANY)
    flops = (rows // BLOCK_Q) * 5 * 2 * (2 * BLOCK_Q) * (BLOCK_Q + w) * d
    cost = pl.CostEstimate(
        flops=flops,
        transcendentals=rows * 2 * (BLOCK_Q + w),
        bytes_accessed=2 * (3 * rows * 2 * d + 2 * rows * d + 4 * w * d) + 4 * 2 * rows * d,
    )
    return pl.pallas_call(
        attention_kernel,
        grid=(1,),
        in_specs=[
            pl.BlockSpec((rows, 1), lambda i: (0, 0)),
            q_spec, q_spec, own_spec, own_spec, prev_spec,
            any_spec, any_spec, any_spec,
        ],
        out_specs=[q_spec, own_spec, own_spec, prev_spec],
        out_shape=[
            jax.ShapeDtypeStruct((rows, q_width), jnp.bfloat16),
            jax.ShapeDtypeStruct((rows, kv_width), jnp.float32),
            jax.ShapeDtypeStruct((rows, kv_width), jnp.float32),
            jax.ShapeDtypeStruct((2, w, d), jnp.bfloat16),
        ],
        scratch_shapes=[
            pltpu.VMEM((w + rows, d), jnp.bfloat16),
            pltpu.VMEM((w + rows, d), jnp.bfloat16),
            pltpu.VMEM((w + rows, d), jnp.float32),
            pltpu.VMEM((w + rows, d), jnp.float32),
        ],
        input_output_aliases={6: 0, 7: 1, 8: 2},
        compiler_params=pltpu.CompilerParams(dimension_semantics=("arbitrary",)),
        cost_estimate=cost,
    )(reach_col, queries, output_gradient, keys, values, previous, dq_buf, dk_buf, dv_buf)


def on_device(queries, keys, values, output_gradient, reach):
    rows, q_width = queries.shape
    kv_width = keys.shape[1]
    heads = kv_width // HEAD_DIMENSION
    d = HEAD_DIMENSION
    w = WINDOW_TOKENS
    reach_col = reach.reshape(rows, 1)
    dq_buf = jnp.zeros((rows, q_width), jnp.bfloat16)
    dk_buf = jnp.zeros((rows, kv_width), jnp.float32)
    dv_buf = jnp.zeros((rows, kv_width), jnp.float32)
    returned = []
    for g in range(heads):
        cols = slice(g * d, (g + 1) * d)
        previous = doc_shift(jnp.stack([keys[rows - w:, cols], values[rows - w:, cols]]), 1)
        dq_buf, dk_buf, dv_buf, dprev = attention_head(
            g, reach_col, queries, output_gradient, keys, values, previous,
            dq_buf, dk_buf, dv_buf)
        returned.append(doc_shift(dprev, -1))
    incoming = jnp.concatenate(returned, axis=-1).astype(jnp.float32)
    grad_keys = dk_buf.at[rows - w:].add(incoming[0]).astype(jnp.bfloat16)
    grad_values = dv_buf.at[rows - w:].add(incoming[1]).astype(jnp.bfloat16)
    return (dq_buf, grad_keys, grad_values)


def solution(mesh):
    placed = (
        P(("slab", "ctx"), None),
        P(("slab", "ctx"), None),
        P(("slab", "ctx"), None),
        P(("slab", "ctx"), None),
        P(("slab", "ctx")),
    )
    return jax.shard_map(
        on_device,
        mesh=mesh,
        in_specs=placed,
        out_specs=(P(("slab", "ctx"), None), P(("slab", "ctx"), None), P(("slab", "ctx"), None)),
        check_vma=False,
    )
```

```python
import functools

import jax
import jax.numpy as jnp
from jax import lax
from jax.experimental import pallas as pl
from jax.experimental.pallas import tpu as pltpu
from jax.sharding import PartitionSpec as P

HEAD_DIMENSION = 128
WINDOW_TOKENS = 1024
QPRE = 168
BLOCK_Q = 128
VPU_FACTOR = 5
PREFETCH = 2

NT_DIMS = (((1,), (1,)), ((), ()))
TN_DIMS = (((0,), (0,)), ((), ()))


def doc_shift(x, by):
    count = lax.axis_size("slab") * lax.axis_size("ctx")
    pairs = [(i, i + by) for i in range(count) if 0 <= i + by < count]
    return lax.ppermute(x, ("slab", "ctx"), pairs)


def attention_kernel(reach_ref, q_ref, do_ref, ko_ref, vo_ref, prev_ref, *refs):
    dq_ref, dko_ref, dvo_ref, dprev_ref, kext, vext, dkacc, dvacc = refs[-8:]
    rows = q_ref.shape[0]
    d = HEAD_DIMENSION
    w = WINDOW_TOKENS
    span = BLOCK_Q + w
    scale = jnp.float32(QPRE ** (-0.5))

    kext[0:w, :] = prev_ref[0]
    kext[w:w + rows, :] = ko_ref[...]
    vext[0:w, :] = prev_ref[1]
    vext[w:w + rows, :] = vo_ref[...]
    dkacc[...] = jnp.zeros_like(dkacc)
    dvacc[...] = jnp.zeros_like(dvacc)

    offsets = (lax.broadcasted_iota(jnp.int32, (BLOCK_Q, span), 1)
               - lax.broadcasted_iota(jnp.int32, (BLOCK_Q, span), 0))

    def body(b, carry):
        r0 = pl.multiple_of(b * BLOCK_Q, BLOCK_Q)
        q = q_ref[pl.ds(r0, BLOCK_Q), :]
        do = do_ref[pl.ds(r0, BLOCK_Q), :]
        q2 = jnp.concatenate([q[:, :d], q[:, d:]], axis=0)
        do2 = jnp.concatenate([do[:, :d], do[:, d:]], axis=0)
        kw = kext[pl.ds(r0, span), :]
        vw = vext[pl.ds(r0, span), :]
        reach = reach_ref[pl.ds(r0, BLOCK_Q), :]
        visible = (offsets <= w) & (offsets > w - reach)
        visible = jnp.concatenate([visible, visible], axis=0)
        s = lax.dot_general(q2, kw, NT_DIMS, preferred_element_type=jnp.float32)
        s = jnp.where(visible, s, -jnp.inf)
        top = jnp.max(s, axis=-1, keepdims=True)
        e = jnp.exp((s - top) * scale)
        total = jnp.sum(e, axis=-1, keepdims=True)
        p = e * (1.0 / total)
        dp = lax.dot_general(do2, vw, NT_DIMS, preferred_element_type=jnp.float32)
        delta = jnp.sum(p * dp, axis=-1, keepdims=True)
        ds = (scale * p * (dp - delta)).astype(jnp.bfloat16)
        pb = p.astype(jnp.bfloat16)
        dq2 = jnp.dot(ds, kw, preferred_element_type=jnp.float32)
        dq_ref[pl.ds(r0, BLOCK_Q), :] = jnp.concatenate(
            [dq2[:BLOCK_Q], dq2[BLOCK_Q:]], axis=1).astype(dq_ref.dtype)
        dk = lax.dot_general(ds, q2, TN_DIMS, preferred_element_type=jnp.float32)
        dv = lax.dot_general(pb, do2, TN_DIMS, preferred_element_type=jnp.float32)
        dkacc[pl.ds(r0, span), :] += dk
        dvacc[pl.ds(r0, span), :] += dv
        return carry

    lax.fori_loop(0, rows // BLOCK_Q, body, 0)
    dko_ref[...] = dkacc[w:w + rows, :]
    dvo_ref[...] = dvacc[w:w + rows, :]
    dprev_ref[0] = dkacc[0:w, :].astype(dprev_ref.dtype)
    dprev_ref[1] = dvacc[0:w, :].astype(dprev_ref.dtype)


def attention_head(g, reach_col, queries, output_gradient, keys, values, previous,
                   dq_buf, dk_buf, dv_buf):
    rows, q_width = queries.shape
    kv_width = keys.shape[1]
    d = HEAD_DIMENSION
    w = WINDOW_TOKENS
    q_spec = pl.BlockSpec((rows, 2 * d), lambda i: (0, g))
    own_spec = pl.BlockSpec((rows, d), lambda i: (0, g))
    prev_spec = pl.BlockSpec((2, w, d), lambda i: (0, 0, 0))
    any_spec = pl.BlockSpec(memory_space=pl.ANY)
    buffers = () if dq_buf is None else (dq_buf, dk_buf, dv_buf)
    flops = VPU_FACTOR * (rows // BLOCK_Q) * 5 * 2 * (2 * BLOCK_Q) * (BLOCK_Q + w) * d
    cost = pl.CostEstimate(
        flops=flops,
        transcendentals=rows * 2 * (BLOCK_Q + w),
        bytes_accessed=2 * (3 * rows * 2 * d + 2 * rows * d + 4 * w * d) + 4 * 2 * rows * d,
    )
    return pl.pallas_call(
        attention_kernel,
        grid=(1,),
        in_specs=[
            pl.BlockSpec((rows, 1), lambda i: (0, 0)),
            q_spec, q_spec, own_spec, own_spec, prev_spec,
        ] + [any_spec] * len(buffers),
        out_specs=[q_spec, own_spec, own_spec, prev_spec],
        out_shape=[
            jax.ShapeDtypeStruct((rows, q_width), jnp.bfloat16),
            jax.ShapeDtypeStruct((rows, kv_width), jnp.float32),
            jax.ShapeDtypeStruct((rows, kv_width), jnp.float32),
            jax.ShapeDtypeStruct((2, w, d), jnp.bfloat16),
        ],
        scratch_shapes=[
            pltpu.VMEM((w + rows, d), jnp.bfloat16),
            pltpu.VMEM((w + rows, d), jnp.bfloat16),
            pltpu.VMEM((w + rows, d), jnp.float32),
            pltpu.VMEM((w + rows, d), jnp.float32),
        ],
        input_output_aliases={6: 0, 7: 1, 8: 2} if buffers else {},
        compiler_params=pltpu.CompilerParams(dimension_semantics=("arbitrary",)),
        cost_estimate=cost,
    )(reach_col, queries, output_gradient, keys, values, previous, *buffers)


def on_device(queries, keys, values, output_gradient, reach):
    rows, q_width = queries.shape
    kv_width = keys.shape[1]
    heads = kv_width // HEAD_DIMENSION
    d = HEAD_DIMENSION
    w = WINDOW_TOKENS
    reach_col = reach.reshape(rows, 1)
    dq_buf = dk_buf = dv_buf = None
    sends = [jnp.stack([keys[rows - w:, g * d:(g + 1) * d], values[rows - w:, g * d:(g + 1) * d]])
             for g in range(heads)]
    arrived = {g: doc_shift(sends[g], 1) for g in range(min(PREFETCH + 1, heads))}
    returned = []
    for g in range(heads):
        ahead = g + PREFETCH
        if g >= 1 and ahead < heads:
            gated, dq_buf = lax.optimization_barrier((sends[ahead], dq_buf))
            arrived[ahead] = doc_shift(gated, 1)
        dq_buf, dk_buf, dv_buf, dprev = attention_head(
            g, reach_col, queries, output_gradient, keys, values, arrived.pop(g),
            dq_buf, dk_buf, dv_buf)
        returned.append(doc_shift(dprev, -1))
    incoming = jnp.concatenate(returned, axis=-1).astype(jnp.float32)
    if rows > w:
        incoming = jnp.concatenate(
            [jnp.zeros((2, rows - w, kv_width), jnp.float32), incoming], axis=1)
    grad_keys = (dk_buf + incoming[0]).astype(jnp.bfloat16)
    grad_values = (dv_buf + incoming[1]).astype(jnp.bfloat16)
    return (dq_buf, grad_keys, grad_values)


def solution(mesh):
    placed = (
        P(("slab", "ctx"), None),
        P(("slab", "ctx"), None),
        P(("slab", "ctx"), None),
        P(("slab", "ctx"), None),
        P(("slab", "ctx")),
    )
    return jax.shard_map(
        on_device,
        mesh=mesh,
        in_specs=placed,
        out_specs=(P(("slab", "ctx"), None), P(("slab", "ctx"), None), P(("slab", "ctx"), None)),
        check_vma=False,
    )
```

```python
import functools

import jax
import jax.numpy as jnp
from jax import lax
from jax.experimental import pallas as pl
from jax.experimental.pallas import tpu as pltpu
from jax.sharding import PartitionSpec as P

HEAD_DIMENSION = 128
WINDOW_TOKENS = 1024
QPRE = 168
BLOCK_Q = 128
VPU_FACTOR = 5
PREFETCH = 2
FINISH_LAG = 2

NT_DIMS = (((1,), (1,)), ((), ()))
TN_DIMS = (((0,), (0,)), ((), ()))


def doc_shift(x, by):
    count = lax.axis_size("slab") * lax.axis_size("ctx")
    pairs = [(i, i + by) for i in range(count) if 0 <= i + by < count]
    return lax.ppermute(x, ("slab", "ctx"), pairs)


def attention_kernel(finish, reach_ref, q_ref, do_ref, ko_ref, vo_ref, prev_ref, *refs):
    kext, vext, dkacc, dvacc = refs[-4:]
    if finish:
        dko_old, dvo_old, back_old = refs[:3]
        dq_ref, dko_ref, dvo_ref, dprev_ref, gk_ref, gv_ref = refs[-10:-4]
    else:
        dq_ref, dko_ref, dvo_ref, dprev_ref = refs[-8:-4]
    rows = q_ref.shape[0]
    d = HEAD_DIMENSION
    w = WINDOW_TOKENS
    span = BLOCK_Q + w
    scale = jnp.float32(QPRE ** (-0.5))

    kext[0:w, :] = prev_ref[0]
    kext[w:w + rows, :] = ko_ref[...]
    vext[0:w, :] = prev_ref[1]
    vext[w:w + rows, :] = vo_ref[...]
    dkacc[...] = jnp.zeros_like(dkacc)
    dvacc[...] = jnp.zeros_like(dvacc)

    offsets = (lax.broadcasted_iota(jnp.int32, (BLOCK_Q, span), 1)
               - lax.broadcasted_iota(jnp.int32, (BLOCK_Q, span), 0))

    def body(b, carry):
        r0 = pl.multiple_of(b * BLOCK_Q, BLOCK_Q)
        q = q_ref[pl.ds(r0, BLOCK_Q), :]
        do = do_ref[pl.ds(r0, BLOCK_Q), :]
        q2 = jnp.concatenate([q[:, :d], q[:, d:]], axis=0)
        do2 = jnp.concatenate([do[:, :d], do[:, d:]], axis=0)
        kw = kext[pl.ds(r0, span), :]
        vw = vext[pl.ds(r0, span), :]
        reach = reach_ref[pl.ds(r0, BLOCK_Q), :]
        visible = (offsets <= w) & (offsets > w - reach)
        visible = jnp.concatenate([visible, visible], axis=0)
        s = lax.dot_general(q2, kw, NT_DIMS, preferred_element_type=jnp.float32)
        s = jnp.where(visible, s, -jnp.inf)
        top = jnp.max(s, axis=-1, keepdims=True)
        e = jnp.exp((s - top) * scale)
        total = jnp.sum(e, axis=-1, keepdims=True)
        p = e * (1.0 / total)
        dp = lax.dot_general(do2, vw, NT_DIMS, preferred_element_type=jnp.float32)
        delta = jnp.sum(p * dp, axis=-1, keepdims=True)
        ds = (scale * p * (dp - delta)).astype(jnp.bfloat16)
        pb = p.astype(jnp.bfloat16)
        dq2 = jnp.dot(ds, kw, preferred_element_type=jnp.float32)
        dq_ref[pl.ds(r0, BLOCK_Q), :] = jnp.concatenate(
            [dq2[:BLOCK_Q], dq2[BLOCK_Q:]], axis=1).astype(dq_ref.dtype)
        dk = lax.dot_general(ds, q2, TN_DIMS, preferred_element_type=jnp.float32)
        dv = lax.dot_general(pb, do2, TN_DIMS, preferred_element_type=jnp.float32)
        dkacc[pl.ds(r0, span), :] += dk
        dvacc[pl.ds(r0, span), :] += dv
        return carry

    if finish:
        gk_ref[...] = dko_old[...].astype(gk_ref.dtype)
        gv_ref[...] = dvo_old[...].astype(gv_ref.dtype)
        gk_ref[rows - w:, :] = (dko_old[rows - w:, :]
                                + back_old[0].astype(jnp.float32)).astype(gk_ref.dtype)
        gv_ref[rows - w:, :] = (dvo_old[rows - w:, :]
                                + back_old[1].astype(jnp.float32)).astype(gv_ref.dtype)

    lax.fori_loop(0, rows // BLOCK_Q, body, 0)
    dko_ref[...] = dkacc[w:w + rows, :]
    dvo_ref[...] = dvacc[w:w + rows, :]
    dprev_ref[0] = dkacc[0:w, :].astype(dprev_ref.dtype)
    dprev_ref[1] = dvacc[0:w, :].astype(dprev_ref.dtype)


def attention_head(g, reach_col, queries, output_gradient, keys, values, previous,
                   dq_buf, older, grad_bufs):
    rows, q_width = queries.shape
    kv_width = keys.shape[1]
    d = HEAD_DIMENSION
    w = WINDOW_TOKENS
    q_spec = pl.BlockSpec((rows, 2 * d), lambda i: (0, g))
    own_spec = pl.BlockSpec((rows, d), lambda i: (0, g))
    col_spec = pl.BlockSpec((rows, d), lambda i: (0, 0))
    prev_spec = pl.BlockSpec((2, w, d), lambda i: (0, 0, 0))
    any_spec = pl.BlockSpec(memory_space=pl.ANY)
    finish = older is not None
    in_specs = [pl.BlockSpec((rows, 1), lambda i: (0, 0)),
                q_spec, q_spec, own_spec, own_spec, prev_spec]
    operands = [reach_col, queries, output_gradient, keys, values, previous]
    out_specs = [q_spec, col_spec, col_spec, prev_spec]
    out_shape = [
        jax.ShapeDtypeStruct((rows, q_width), jnp.bfloat16),
        jax.ShapeDtypeStruct((rows, d), jnp.float32),
        jax.ShapeDtypeStruct((rows, d), jnp.float32),
        jax.ShapeDtypeStruct((2, w, d), jnp.bfloat16),
    ]
    aliases = {}
    if finish:
        h = older[0]
        in_specs += [col_spec, col_spec, prev_spec]
        operands += list(older[1:])
        old_spec = pl.BlockSpec((rows, d), lambda i: (0, h))
        out_specs += [old_spec, old_spec]
        out_shape += [jax.ShapeDtypeStruct((rows, kv_width), jnp.bfloat16)] * 2
    buffers = ([] if dq_buf is None else [(dq_buf, 0)]) + (
        [] if grad_bufs is None else [(grad_bufs[0], 4), (grad_bufs[1], 5)])
    for buf, out_index in buffers:
        aliases[len(operands)] = out_index
        in_specs.append(any_spec)
        operands.append(buf)
    flops = VPU_FACTOR * (rows // BLOCK_Q) * 5 * 2 * (2 * BLOCK_Q) * (BLOCK_Q + w) * d
    cost = pl.CostEstimate(
        flops=flops,
        transcendentals=rows * 2 * (BLOCK_Q + w),
        bytes_accessed=2 * (3 * rows * 2 * d + 2 * rows * d + 4 * w * d) + 4 * 2 * rows * d,
    )
    return pl.pallas_call(
        functools.partial(attention_kernel, finish),
        grid=(1,),
        in_specs=in_specs,
        out_specs=out_specs,
        out_shape=out_shape,
        scratch_shapes=[
            pltpu.VMEM((w + rows, d), jnp.bfloat16),
            pltpu.VMEM((w + rows, d), jnp.bfloat16),
            pltpu.VMEM((w + rows, d), jnp.float32),
            pltpu.VMEM((w + rows, d), jnp.float32),
        ],
        input_output_aliases=aliases,
        compiler_params=pltpu.CompilerParams(dimension_semantics=("arbitrary",)),
        cost_estimate=cost,
    )(*operands)


def finish_columns(grad, h, own, back):
    rows = own.shape[0]
    w = WINDOW_TOKENS
    d = HEAD_DIMENSION
    total = own.at[rows - w:].add(back.astype(jnp.float32)).astype(jnp.bfloat16)
    return lax.dynamic_update_slice(grad, total, (0, h * d))


def on_device(queries, keys, values, output_gradient, reach):
    rows, q_width = queries.shape
    kv_width = keys.shape[1]
    heads = kv_width // HEAD_DIMENSION
    d = HEAD_DIMENSION
    w = WINDOW_TOKENS
    reach_col = reach.reshape(rows, 1)
    sends = [jnp.stack([keys[rows - w:, g * d:(g + 1) * d], values[rows - w:, g * d:(g + 1) * d]])
             for g in range(heads)]
    arrived = {g: doc_shift(sends[g], 1) for g in range(min(PREFETCH + 1, heads))}
    dq_buf = None
    grad_bufs = None
    pending = []
    for g in range(heads):
        ahead = g + PREFETCH
        if g >= 1 and ahead < heads:
            gated, dq_buf = lax.optimization_barrier((sends[ahead], dq_buf))
            arrived[ahead] = doc_shift(gated, 1)
        older = pending.pop(0) if len(pending) >= FINISH_LAG else None
        outs = attention_head(
            g, reach_col, queries, output_gradient, keys, values, arrived.pop(g),
            dq_buf, older, grad_bufs)
        dq_buf, dk_own, dv_own, dprev = outs[:4]
        if older is not None:
            grad_bufs = tuple(outs[4:6])
        pending.append((g, dk_own, dv_own, doc_shift(dprev, -1)))
    if grad_bufs is None:
        grad_bufs = (jnp.zeros((rows, kv_width), jnp.bfloat16),) * 2
    grad_keys, grad_values = grad_bufs
    for h, dk_own, dv_own, back in pending:
        grad_keys = finish_columns(grad_keys, h, dk_own, back[0])
        grad_values = finish_columns(grad_values, h, dv_own, back[1])
    return (dq_buf, grad_keys, grad_values)


def solution(mesh):
    placed = (
        P(("slab", "ctx"), None),
        P(("slab", "ctx"), None),
        P(("slab", "ctx"), None),
        P(("slab", "ctx"), None),
        P(("slab", "ctx")),
    )
    return jax.shard_map(
        on_device,
        mesh=mesh,
        in_specs=placed,
        out_specs=(P(("slab", "ctx"), None), P(("slab", "ctx"), None), P(("slab", "ctx"), None)),
        check_vma=False,
    )
```

```python
import functools

import jax
import jax.numpy as jnp
from jax import lax
from jax.experimental import pallas as pl
from jax.experimental.pallas import tpu as pltpu
from jax.sharding import PartitionSpec as P

HEAD_DIMENSION = 128
WINDOW_TOKENS = 1024
QPRE = 168
BLOCK_Q = 128
VPU_FACTOR = 5
FINISH_LAG = 2

NT_DIMS = (((1,), (1,)), ((), ()))
TN_DIMS = (((0,), (0,)), ((), ()))


def doc_shift(x, by):
    count = lax.axis_size("slab") * lax.axis_size("ctx")
    pairs = [(i, i + by) for i in range(count) if 0 <= i + by < count]
    return lax.ppermute(x, ("slab", "ctx"), pairs)


def attention_kernel(finish, reach_ref, q_ref, do_ref, ko_ref, vo_ref, prev_ref, *refs):
    kext, vext, dkacc, dvacc = refs[-4:]
    if finish:
        dko_old, dvo_old, back_old = refs[:3]
        dq_ref, dko_ref, dvo_ref, dprev_ref, gk_ref, gv_ref = refs[-10:-4]
    else:
        dq_ref, dko_ref, dvo_ref, dprev_ref = refs[-8:-4]
    rows = q_ref.shape[0]
    d = HEAD_DIMENSION
    w = WINDOW_TOKENS
    span = BLOCK_Q + w
    scale = jnp.float32(QPRE ** (-0.5))

    kext[0:w, :] = prev_ref[0]
    kext[w:w + rows, :] = ko_ref[...]
    vext[0:w, :] = prev_ref[1]
    vext[w:w + rows, :] = vo_ref[...]
    dkacc[...] = jnp.zeros_like(dkacc)
    dvacc[...] = jnp.zeros_like(dvacc)

    offsets = (lax.broadcasted_iota(jnp.int32, (BLOCK_Q, span), 1)
               - lax.broadcasted_iota(jnp.int32, (BLOCK_Q, span), 0))

    def body(b, carry):
        r0 = pl.multiple_of(b * BLOCK_Q, BLOCK_Q)
        q = q_ref[pl.ds(r0, BLOCK_Q), :]
        do = do_ref[pl.ds(r0, BLOCK_Q), :]
        q2 = jnp.concatenate([q[:, :d], q[:, d:]], axis=0)
        do2 = jnp.concatenate([do[:, :d], do[:, d:]], axis=0)
        kw = kext[pl.ds(r0, span), :]
        vw = vext[pl.ds(r0, span), :]
        reach = reach_ref[pl.ds(r0, BLOCK_Q), :]
        visible = (offsets <= w) & (offsets > w - reach)
        visible = jnp.concatenate([visible, visible], axis=0)
        s = lax.dot_general(q2, kw, NT_DIMS, preferred_element_type=jnp.float32)
        s = jnp.where(visible, s, -jnp.inf)
        top = jnp.max(s, axis=-1, keepdims=True)
        e = jnp.exp((s - top) * scale)
        total = jnp.sum(e, axis=-1, keepdims=True)
        p = e * (1.0 / total)
        dp = lax.dot_general(do2, vw, NT_DIMS, preferred_element_type=jnp.float32)
        delta = jnp.sum(p * dp, axis=-1, keepdims=True)
        ds = (scale * p * (dp - delta)).astype(jnp.bfloat16)
        pb = p.astype(jnp.bfloat16)
        dq2 = jnp.dot(ds, kw, preferred_element_type=jnp.float32)
        dq_ref[pl.ds(r0, BLOCK_Q), :] = jnp.concatenate(
            [dq2[:BLOCK_Q], dq2[BLOCK_Q:]], axis=1).astype(dq_ref.dtype)
        dk = lax.dot_general(ds, q2, TN_DIMS, preferred_element_type=jnp.float32)
        dv = lax.dot_general(pb, do2, TN_DIMS, preferred_element_type=jnp.float32)
        dkacc[pl.ds(r0, span), :] += dk
        dvacc[pl.ds(r0, span), :] += dv
        return carry

    if finish:
        gk_ref[...] = dko_old[...].astype(gk_ref.dtype)
        gv_ref[...] = dvo_old[...].astype(gv_ref.dtype)
        gk_ref[rows - w:, :] = (dko_old[rows - w:, :]
                                + back_old[0].astype(jnp.float32)).astype(gk_ref.dtype)
        gv_ref[rows - w:, :] = (dvo_old[rows - w:, :]
                                + back_old[1].astype(jnp.float32)).astype(gv_ref.dtype)

    lax.fori_loop(0, rows // BLOCK_Q, body, 0)
    dko_ref[...] = dkacc[w:w + rows, :]
    dvo_ref[...] = dvacc[w:w + rows, :]
    dprev_ref[0] = dkacc[0:w, :].astype(dprev_ref.dtype)
    dprev_ref[1] = dvacc[0:w, :].astype(dprev_ref.dtype)


def attention_head(g, reach_col, queries, output_gradient, keys, values, previous,
                   dq_buf, older, grad_bufs):
    rows, q_width = queries.shape
    kv_width = keys.shape[1]
    d = HEAD_DIMENSION
    w = WINDOW_TOKENS
    q_spec = pl.BlockSpec((rows, 2 * d), lambda i: (0, g))
    own_spec = pl.BlockSpec((rows, d), lambda i: (0, g))
    col_spec = pl.BlockSpec((rows, d), lambda i: (0, 0))
    prev_spec = pl.BlockSpec((2, w, d), lambda i: (0, 0, 0))
    any_spec = pl.BlockSpec(memory_space=pl.ANY)
    finish = older is not None
    in_specs = [pl.BlockSpec((rows, 1), lambda i: (0, 0)),
                q_spec, q_spec, own_spec, own_spec, prev_spec]
    operands = [reach_col, queries, output_gradient, keys, values, previous]
    out_specs = [q_spec, col_spec, col_spec, prev_spec]
    out_shape = [
        jax.ShapeDtypeStruct((rows, q_width), jnp.bfloat16),
        jax.ShapeDtypeStruct((rows, d), jnp.float32),
        jax.ShapeDtypeStruct((rows, d), jnp.float32),
        jax.ShapeDtypeStruct((2, w, d), jnp.bfloat16),
    ]
    aliases = {}
    if finish:
        h = older[0]
        in_specs += [col_spec, col_spec, prev_spec]
        operands += list(older[1:])
        old_spec = pl.BlockSpec((rows, d), lambda i: (0, h))
        out_specs += [old_spec, old_spec]
        out_shape += [jax.ShapeDtypeStruct((rows, kv_width), jnp.bfloat16)] * 2
    buffers = ([] if dq_buf is None else [(dq_buf, 0)]) + (
        [] if grad_bufs is None else [(grad_bufs[0], 4), (grad_bufs[1], 5)])
    for buf, out_index in buffers:
        aliases[len(operands)] = out_index
        in_specs.append(any_spec)
        operands.append(buf)
    flops = VPU_FACTOR * (rows // BLOCK_Q) * 5 * 2 * (2 * BLOCK_Q) * (BLOCK_Q + w) * d
    cost = pl.CostEstimate(
        flops=flops,
        transcendentals=rows * 2 * (BLOCK_Q + w),
        bytes_accessed=2 * (3 * rows * 2 * d + 2 * rows * d + 4 * w * d) + 4 * 2 * rows * d,
    )
    return pl.pallas_call(
        functools.partial(attention_kernel, finish),
        grid=(1,),
        in_specs=in_specs,
        out_specs=out_specs,
        out_shape=out_shape,
        scratch_shapes=[
            pltpu.VMEM((w + rows, d), jnp.bfloat16),
            pltpu.VMEM((w + rows, d), jnp.bfloat16),
            pltpu.VMEM((w + rows, d), jnp.float32),
            pltpu.VMEM((w + rows, d), jnp.float32),
        ],
        input_output_aliases=aliases,
        compiler_params=pltpu.CompilerParams(dimension_semantics=("arbitrary",)),
        cost_estimate=cost,
    )(*operands)


def finish_columns(grad, h, own, back):
    rows = own.shape[0]
    w = WINDOW_TOKENS
    d = HEAD_DIMENSION
    total = own.at[rows - w:].add(back.astype(jnp.float32)).astype(jnp.bfloat16)
    return lax.dynamic_update_slice(grad, total, (0, h * d))


def on_device(queries, keys, values, output_gradient, reach):
    rows, q_width = queries.shape
    kv_width = keys.shape[1]
    heads = kv_width // HEAD_DIMENSION
    d = HEAD_DIMENSION
    w = WINDOW_TOKENS
    reach_col = reach.reshape(rows, 1)
    sends = [jnp.stack([keys[rows - w:, g * d:(g + 1) * d], values[rows - w:, g * d:(g + 1) * d]])
             for g in range(heads)]
    arrived = {0: doc_shift(sends[0], 1)}
    dq_buf = None
    grad_bufs = None
    pending = []
    for g in range(heads):
        if g + 1 < heads:
            gated, arrived[g] = lax.optimization_barrier((sends[g + 1], arrived[g]))
            arrived[g + 1] = doc_shift(gated, 1)
        older = pending.pop(0) if len(pending) >= FINISH_LAG else None
        outs = attention_head(
            g, reach_col, queries, output_gradient, keys, values, arrived.pop(g),
            dq_buf, older, grad_bufs)
        dq_buf, dk_own, dv_own, dprev = outs[:4]
        if older is not None:
            grad_bufs = tuple(outs[4:6])
        pending.append((g, dk_own, dv_own, doc_shift(dprev, -1)))
    if grad_bufs is None:
        grad_bufs = (jnp.zeros((rows, kv_width), jnp.bfloat16),) * 2
    grad_keys, grad_values = grad_bufs
    for h, dk_own, dv_own, back in pending:
        grad_keys = finish_columns(grad_keys, h, dk_own, back[0])
        grad_values = finish_columns(grad_values, h, dv_own, back[1])
    return (dq_buf, grad_keys, grad_values)


def solution(mesh):
    placed = (
        P(("slab", "ctx"), None),
        P(("slab", "ctx"), None),
        P(("slab", "ctx"), None),
        P(("slab", "ctx"), None),
        P(("slab", "ctx")),
    )
    return jax.shard_map(
        on_device,
        mesh=mesh,
        in_specs=placed,
        out_specs=(P(("slab", "ctx"), None), P(("slab", "ctx"), None), P(("slab", "ctx"), None)),
        check_vma=False,
    )
```

```python
import functools

import jax
import jax.numpy as jnp
from jax import lax
from jax.experimental import pallas as pl
from jax.experimental.pallas import tpu as pltpu
from jax.sharding import PartitionSpec as P

HEAD_DIMENSION = 128
WINDOW_TOKENS = 1024
QPRE = 168
BLOCK_Q = 128
VPU_FACTOR = 5
HEADS_PER_CALL = 2
FINISH_LAG = 2

NT_DIMS = (((1,), (1,)), ((), ()))
TN_DIMS = (((0,), (0,)), ((), ()))


def doc_shift(x, by):
    count = lax.axis_size("slab") * lax.axis_size("ctx")
    pairs = [(i, i + by) for i in range(count) if 0 <= i + by < count]
    return lax.ppermute(x, ("slab", "ctx"), pairs)


def attention_kernel(finish, reach_ref, q_ref, do_ref, ko_ref, vo_ref, prev_ref, *refs):
    kext, vext, dkacc, dvacc = refs[-4:]
    if finish:
        dko_old, dvo_old, back_old = refs[:3]
        dq_ref, dko_ref, dvo_ref, dprev_ref, gk_ref, gv_ref = refs[-10:-4]
    else:
        dq_ref, dko_ref, dvo_ref, dprev_ref = refs[-8:-4]
    rows = q_ref.shape[0]
    d = HEAD_DIMENSION
    w = WINDOW_TOKENS
    span = BLOCK_Q + w
    scale = jnp.float32(QPRE ** (-0.5))

    kext[0:w, :] = prev_ref[0]
    kext[w:w + rows, :] = ko_ref[...]
    vext[0:w, :] = prev_ref[1]
    vext[w:w + rows, :] = vo_ref[...]
    dkacc[...] = jnp.zeros_like(dkacc)
    dvacc[...] = jnp.zeros_like(dvacc)

    offsets = (lax.broadcasted_iota(jnp.int32, (BLOCK_Q, span), 1)
               - lax.broadcasted_iota(jnp.int32, (BLOCK_Q, span), 0))

    def body(b, carry):
        r0 = pl.multiple_of(b * BLOCK_Q, BLOCK_Q)
        q = q_ref[pl.ds(r0, BLOCK_Q), :]
        do = do_ref[pl.ds(r0, BLOCK_Q), :]
        q2 = jnp.concatenate([q[:, :d], q[:, d:]], axis=0)
        do2 = jnp.concatenate([do[:, :d], do[:, d:]], axis=0)
        kw = kext[pl.ds(r0, span), :]
        vw = vext[pl.ds(r0, span), :]
        reach = reach_ref[pl.ds(r0, BLOCK_Q), :]
        visible = (offsets <= w) & (offsets > w - reach)
        visible = jnp.concatenate([visible, visible], axis=0)
        s = lax.dot_general(q2, kw, NT_DIMS, preferred_element_type=jnp.float32)
        s = jnp.where(visible, s, -jnp.inf)
        top = jnp.max(s, axis=-1, keepdims=True)
        e = jnp.exp((s - top) * scale)
        total = jnp.sum(e, axis=-1, keepdims=True)
        p = e * (1.0 / total)
        dp = lax.dot_general(do2, vw, NT_DIMS, preferred_element_type=jnp.float32)
        delta = jnp.sum(p * dp, axis=-1, keepdims=True)
        ds = (scale * p * (dp - delta)).astype(jnp.bfloat16)
        pb = p.astype(jnp.bfloat16)
        dq2 = jnp.dot(ds, kw, preferred_element_type=jnp.float32)
        dq_ref[pl.ds(r0, BLOCK_Q), :] = jnp.concatenate(
            [dq2[:BLOCK_Q], dq2[BLOCK_Q:]], axis=1).astype(dq_ref.dtype)
        dk = lax.dot_general(ds, q2, TN_DIMS, preferred_element_type=jnp.float32)
        dv = lax.dot_general(pb, do2, TN_DIMS, preferred_element_type=jnp.float32)
        dkacc[pl.ds(r0, span), :] += dk
        dvacc[pl.ds(r0, span), :] += dv
        return carry

    if finish:
        gk_ref[...] = dko_old[...].astype(gk_ref.dtype)
        gv_ref[...] = dvo_old[...].astype(gv_ref.dtype)
        gk_ref[rows - w:, :] = (dko_old[rows - w:, :]
                                + back_old[0].astype(jnp.float32)).astype(gk_ref.dtype)
        gv_ref[rows - w:, :] = (dvo_old[rows - w:, :]
                                + back_old[1].astype(jnp.float32)).astype(gv_ref.dtype)

    lax.fori_loop(0, rows // BLOCK_Q, body, 0)
    dko_ref[...] = dkacc[w:w + rows, :]
    dvo_ref[...] = dvacc[w:w + rows, :]
    dprev_ref[0] = dkacc[0:w, :].astype(dprev_ref.dtype)
    dprev_ref[1] = dvacc[0:w, :].astype(dprev_ref.dtype)


def attention_head(g, reach_col, queries, output_gradient, keys, values, previous,
                   dq_buf, older, grad_bufs):
    rows, q_width = queries.shape
    kv_width = keys.shape[1]
    d = HEAD_DIMENSION
    w = WINDOW_TOKENS
    n = HEADS_PER_CALL
    q_spec = pl.BlockSpec((rows, 2 * d), lambda i: (0, g * n + i))
    own_spec = pl.BlockSpec((rows, d), lambda i: (0, g * n + i))
    col_spec = pl.BlockSpec((rows, d), lambda i: (0, i))
    prev_spec = pl.BlockSpec((2, w, d), lambda i: (0, 0, i))
    any_spec = pl.BlockSpec(memory_space=pl.ANY)
    finish = older is not None
    in_specs = [pl.BlockSpec((rows, 1), lambda i: (0, 0)),
                q_spec, q_spec, own_spec, own_spec, prev_spec]
    operands = [reach_col, queries, output_gradient, keys, values, previous]
    out_specs = [q_spec, col_spec, col_spec, prev_spec]
    out_shape = [
        jax.ShapeDtypeStruct((rows, q_width), jnp.bfloat16),
        jax.ShapeDtypeStruct((rows, n * d), jnp.float32),
        jax.ShapeDtypeStruct((rows, n * d), jnp.float32),
        jax.ShapeDtypeStruct((2, w, n * d), jnp.bfloat16),
    ]
    aliases = {}
    if finish:
        h = older[0]
        in_specs += [col_spec, col_spec, prev_spec]
        operands += list(older[1:])
        old_spec = pl.BlockSpec((rows, d), lambda i: (0, h * n + i))
        out_specs += [old_spec, old_spec]
        out_shape += [jax.ShapeDtypeStruct((rows, kv_width), jnp.bfloat16)] * 2
    buffers = ([] if dq_buf is None else [(dq_buf, 0)]) + (
        [] if grad_bufs is None else [(grad_bufs[0], 4), (grad_bufs[1], 5)])
    for buf, out_index in buffers:
        aliases[len(operands)] = out_index
        in_specs.append(any_spec)
        operands.append(buf)
    flops = n * VPU_FACTOR * (rows // BLOCK_Q) * 5 * 2 * (2 * BLOCK_Q) * (BLOCK_Q + w) * d
    cost = pl.CostEstimate(
        flops=flops,
        transcendentals=n * rows * 2 * (BLOCK_Q + w),
        bytes_accessed=n * 2 * (3 * rows * 2 * d + 2 * rows * d + 4 * w * d) + 4 * 2 * rows * d,
    )
    return pl.pallas_call(
        functools.partial(attention_kernel, finish),
        grid=(n,),
        in_specs=in_specs,
        out_specs=out_specs,
        out_shape=out_shape,
        scratch_shapes=[
            pltpu.VMEM((w + rows, d), jnp.bfloat16),
            pltpu.VMEM((w + rows, d), jnp.bfloat16),
            pltpu.VMEM((w + rows, d), jnp.float32),
            pltpu.VMEM((w + rows, d), jnp.float32),
        ],
        input_output_aliases=aliases,
        compiler_params=pltpu.CompilerParams(dimension_semantics=("arbitrary",)),
        cost_estimate=cost,
    )(*operands)


def finish_columns(grad, h, own, back):
    rows = own.shape[0]
    w = WINDOW_TOKENS
    d = HEAD_DIMENSION
    total = own.at[rows - w:].add(back.astype(jnp.float32)).astype(jnp.bfloat16)
    return lax.dynamic_update_slice(grad, total, (0, h * HEADS_PER_CALL * d))


def on_device(queries, keys, values, output_gradient, reach):
    rows, q_width = queries.shape
    kv_width = keys.shape[1]
    d = HEAD_DIMENSION * HEADS_PER_CALL
    heads = kv_width // d
    w = WINDOW_TOKENS
    reach_col = reach.reshape(rows, 1)
    sends = [jnp.stack([keys[rows - w:, g * d:(g + 1) * d], values[rows - w:, g * d:(g + 1) * d]])
             for g in range(heads)]
    arrived = {0: doc_shift(sends[0], 1)}
    dq_buf = None
    grad_bufs = None
    pending = []
    for g in range(heads):
        if g + 1 < heads:
            gated, arrived[g] = lax.optimization_barrier((sends[g + 1], arrived[g]))
            arrived[g + 1] = doc_shift(gated, 1)
        older = pending.pop(0) if len(pending) >= FINISH_LAG else None
        outs = attention_head(
            g, reach_col, queries, output_gradient, keys, values, arrived.pop(g),
            dq_buf, older, grad_bufs)
        dq_buf, dk_own, dv_own, dprev = outs[:4]
        if older is not None:
            grad_bufs = tuple(outs[4:6])
        pending.append((g, dk_own, dv_own, doc_shift(dprev, -1)))
    if grad_bufs is None:
        grad_bufs = (jnp.zeros((rows, kv_width), jnp.bfloat16),) * 2
    grad_keys, grad_values = grad_bufs
    for h, dk_own, dv_own, back in pending:
        grad_keys = finish_columns(grad_keys, h, dk_own, back[0])
        grad_values = finish_columns(grad_values, h, dv_own, back[1])
    return (dq_buf, grad_keys, grad_values)


def solution(mesh):
    placed = (
        P(("slab", "ctx"), None),
        P(("slab", "ctx"), None),
        P(("slab", "ctx"), None),
        P(("slab", "ctx"), None),
        P(("slab", "ctx")),
    )
    return jax.shard_map(
        on_device,
        mesh=mesh,
        in_specs=placed,
        out_specs=(P(("slab", "ctx"), None), P(("slab", "ctx"), None), P(("slab", "ctx"), None)),
        check_vma=False,
    )
```

```python
import functools

import jax
import jax.numpy as jnp
from jax import lax
from jax.experimental import pallas as pl
from jax.experimental.pallas import tpu as pltpu
from jax.sharding import PartitionSpec as P

HEAD_DIMENSION = 128
WINDOW_TOKENS = 1024
QPRE = 168
BLOCK_Q = 128
VPU_FACTOR = 5
HEADS_PER_CALL = 2
SEND_DEPTH = 2
FINISH_LAG = 2

NT_DIMS = (((1,), (1,)), ((), ()))
TN_DIMS = (((0,), (0,)), ((), ()))


def doc_shift(x, by):
    count = lax.axis_size("slab") * lax.axis_size("ctx")
    pairs = [(i, i + by) for i in range(count) if 0 <= i + by < count]
    return lax.ppermute(x, ("slab", "ctx"), pairs)


def attention_kernel(finish, reach_ref, q_ref, do_ref, ko_ref, vo_ref, prev_ref, *refs):
    kext, vext, dkacc, dvacc = refs[-4:]
    if finish:
        dko_old, dvo_old, back_old = refs[:3]
        dq_ref, dko_ref, dvo_ref, dprev_ref, gk_ref, gv_ref = refs[-10:-4]
    else:
        dq_ref, dko_ref, dvo_ref, dprev_ref = refs[-8:-4]
    rows = q_ref.shape[0]
    d = HEAD_DIMENSION
    w = WINDOW_TOKENS
    span = BLOCK_Q + w
    scale = jnp.float32(QPRE ** (-0.5))

    kext[0:w, :] = prev_ref[0]
    kext[w:w + rows, :] = ko_ref[...]
    vext[0:w, :] = prev_ref[1]
    vext[w:w + rows, :] = vo_ref[...]
    dkacc[...] = jnp.zeros_like(dkacc)
    dvacc[...] = jnp.zeros_like(dvacc)

    offsets = (lax.broadcasted_iota(jnp.int32, (BLOCK_Q, span), 1)
               - lax.broadcasted_iota(jnp.int32, (BLOCK_Q, span), 0))

    def body(b, carry):
        r0 = pl.multiple_of(b * BLOCK_Q, BLOCK_Q)
        q = q_ref[pl.ds(r0, BLOCK_Q), :]
        do = do_ref[pl.ds(r0, BLOCK_Q), :]
        q2 = jnp.concatenate([q[:, :d], q[:, d:]], axis=0)
        do2 = jnp.concatenate([do[:, :d], do[:, d:]], axis=0)
        kw = kext[pl.ds(r0, span), :]
        vw = vext[pl.ds(r0, span), :]
        reach = reach_ref[pl.ds(r0, BLOCK_Q), :]
        visible = (offsets <= w) & (offsets > w - reach)
        visible = jnp.concatenate([visible, visible], axis=0)
        s = lax.dot_general(q2, kw, NT_DIMS, preferred_element_type=jnp.float32)
        s = jnp.where(visible, s, -jnp.inf)
        top = jnp.max(s, axis=-1, keepdims=True)
        e = jnp.exp((s - top) * scale)
        total = jnp.sum(e, axis=-1, keepdims=True)
        p = e * (1.0 / total)
        dp = lax.dot_general(do2, vw, NT_DIMS, preferred_element_type=jnp.float32)
        delta = jnp.sum(p * dp, axis=-1, keepdims=True)
        ds = (scale * p * (dp - delta)).astype(jnp.bfloat16)
        pb = p.astype(jnp.bfloat16)
        dq2 = jnp.dot(ds, kw, preferred_element_type=jnp.float32)
        dq_ref[pl.ds(r0, BLOCK_Q), :] = jnp.concatenate(
            [dq2[:BLOCK_Q], dq2[BLOCK_Q:]], axis=1).astype(dq_ref.dtype)
        dk = lax.dot_general(ds, q2, TN_DIMS, preferred_element_type=jnp.float32)
        dv = lax.dot_general(pb, do2, TN_DIMS, preferred_element_type=jnp.float32)
        dkacc[pl.ds(r0, span), :] += dk
        dvacc[pl.ds(r0, span), :] += dv
        return carry

    if finish:
        gk_ref[...] = dko_old[...].astype(gk_ref.dtype)
        gv_ref[...] = dvo_old[...].astype(gv_ref.dtype)
        gk_ref[rows - w:, :] = (dko_old[rows - w:, :]
                                + back_old[0].astype(jnp.float32)).astype(gk_ref.dtype)
        gv_ref[rows - w:, :] = (dvo_old[rows - w:, :]
                                + back_old[1].astype(jnp.float32)).astype(gv_ref.dtype)

    lax.fori_loop(0, rows // BLOCK_Q, body, 0)
    dko_ref[...] = dkacc[w:w + rows, :]
    dvo_ref[...] = dvacc[w:w + rows, :]
    dprev_ref[0] = dkacc[0:w, :].astype(dprev_ref.dtype)
    dprev_ref[1] = dvacc[0:w, :].astype(dprev_ref.dtype)


def attention_head(g, reach_col, queries, output_gradient, keys, values, previous,
                   dq_buf, older, grad_bufs):
    rows, q_width = queries.shape
    kv_width = keys.shape[1]
    d = HEAD_DIMENSION
    w = WINDOW_TOKENS
    n = HEADS_PER_CALL
    q_spec = pl.BlockSpec((rows, 2 * d), lambda i: (0, g * n + i))
    own_spec = pl.BlockSpec((rows, d), lambda i: (0, g * n + i))
    col_spec = pl.BlockSpec((rows, d), lambda i: (0, i))
    prev_spec = pl.BlockSpec((2, w, d), lambda i: (0, 0, i))
    any_spec = pl.BlockSpec(memory_space=pl.ANY)
    finish = older is not None
    in_specs = [pl.BlockSpec((rows, 1), lambda i: (0, 0)),
                q_spec, q_spec, own_spec, own_spec, prev_spec]
    operands = [reach_col, queries, output_gradient, keys, values, previous]
    out_specs = [q_spec, col_spec, col_spec, prev_spec]
    out_shape = [
        jax.ShapeDtypeStruct((rows, q_width), jnp.bfloat16),
        jax.ShapeDtypeStruct((rows, n * d), jnp.float32),
        jax.ShapeDtypeStruct((rows, n * d), jnp.float32),
        jax.ShapeDtypeStruct((2, w, n * d), jnp.bfloat16),
    ]
    aliases = {}
    if finish:
        h = older[0]
        in_specs += [col_spec, col_spec, prev_spec]
        operands += list(older[1:])
        old_spec = pl.BlockSpec((rows, d), lambda i: (0, h * n + i))
        out_specs += [old_spec, old_spec]
        out_shape += [jax.ShapeDtypeStruct((rows, kv_width), jnp.bfloat16)] * 2
    buffers = ([] if dq_buf is None else [(dq_buf, 0)]) + (
        [] if grad_bufs is None else [(grad_bufs[0], 4), (grad_bufs[1], 5)])
    for buf, out_index in buffers:
        aliases[len(operands)] = out_index
        in_specs.append(any_spec)
        operands.append(buf)
    flops = n * VPU_FACTOR * (rows // BLOCK_Q) * 5 * 2 * (2 * BLOCK_Q) * (BLOCK_Q + w) * d
    cost = pl.CostEstimate(
        flops=flops,
        transcendentals=n * rows * 2 * (BLOCK_Q + w),
        bytes_accessed=n * 2 * (3 * rows * 2 * d + 2 * rows * d + 4 * w * d) + 4 * 2 * rows * d,
    )
    return pl.pallas_call(
        functools.partial(attention_kernel, finish),
        grid=(n,),
        in_specs=in_specs,
        out_specs=out_specs,
        out_shape=out_shape,
        scratch_shapes=[
            pltpu.VMEM((w + rows, d), jnp.bfloat16),
            pltpu.VMEM((w + rows, d), jnp.bfloat16),
            pltpu.VMEM((w + rows, d), jnp.float32),
            pltpu.VMEM((w + rows, d), jnp.float32),
        ],
        input_output_aliases=aliases,
        compiler_params=pltpu.CompilerParams(dimension_semantics=("arbitrary",)),
        cost_estimate=cost,
    )(*operands)


def finish_columns(grad, h, own, back):
    rows = own.shape[0]
    w = WINDOW_TOKENS
    d = HEAD_DIMENSION
    total = own.at[rows - w:].add(back.astype(jnp.float32)).astype(jnp.bfloat16)
    return lax.dynamic_update_slice(grad, total, (0, h * HEADS_PER_CALL * d))


def on_device(queries, keys, values, output_gradient, reach):
    rows, q_width = queries.shape
    kv_width = keys.shape[1]
    d = HEAD_DIMENSION * HEADS_PER_CALL
    heads = kv_width // d
    w = WINDOW_TOKENS
    reach_col = reach.reshape(rows, 1)
    sends = [jnp.stack([keys[rows - w:, g * d:(g + 1) * d], values[rows - w:, g * d:(g + 1) * d]])
             for g in range(heads)]
    arrived = {0: doc_shift(sends[0], 1)}
    dq_buf = None
    grad_bufs = None
    pending = []
    for g in range(heads):
        for later in range(g + 1, min(g + SEND_DEPTH, heads - 1) + 1):
            if later not in arrived:
                gated, arrived[g] = lax.optimization_barrier((sends[later], arrived[g]))
                arrived[later] = doc_shift(gated, 1)
        older = pending.pop(0) if len(pending) >= FINISH_LAG else None
        outs = attention_head(
            g, reach_col, queries, output_gradient, keys, values, arrived.pop(g),
            dq_buf, older, grad_bufs)
        dq_buf, dk_own, dv_own, dprev = outs[:4]
        if older is not None:
            grad_bufs = tuple(outs[4:6])
        pending.append((g, dk_own, dv_own, doc_shift(dprev, -1)))
    if grad_bufs is None:
        grad_bufs = (jnp.zeros((rows, kv_width), jnp.bfloat16),) * 2
    grad_keys, grad_values = grad_bufs
    for h, dk_own, dv_own, back in pending:
        grad_keys = finish_columns(grad_keys, h, dk_own, back[0])
        grad_values = finish_columns(grad_values, h, dv_own, back[1])
    return (dq_buf, grad_keys, grad_values)


def solution(mesh):
    placed = (
        P(("slab", "ctx"), None),
        P(("slab", "ctx"), None),
        P(("slab", "ctx"), None),
        P(("slab", "ctx"), None),
        P(("slab", "ctx")),
    )
    return jax.shard_map(
        on_device,
        mesh=mesh,
        in_specs=placed,
        out_specs=(P(("slab", "ctx"), None), P(("slab", "ctx"), None), P(("slab", "ctx"), None)),
        check_vma=False,
    )
```

```python
import functools

import jax
import jax.numpy as jnp
from jax import lax
from jax.experimental import pallas as pl
from jax.experimental.pallas import tpu as pltpu
from jax.sharding import PartitionSpec as P

HEAD_DIMENSION = 128
WINDOW_TOKENS = 1024
QPRE = 168
BLOCK_Q = 128
VPU_FACTOR = 5
SEND_DEPTH = 2
FINISH_LAG = 2

NT_DIMS = (((1,), (1,)), ((), ()))
TN_DIMS = (((0,), (0,)), ((), ()))


def doc_shift(x, by):
    count = lax.axis_size("slab") * lax.axis_size("ctx")
    pairs = [(i, i + by) for i in range(count) if 0 <= i + by < count]
    return lax.ppermute(x, ("slab", "ctx"), pairs)


def attention_kernel(finish, reach_ref, q_ref, do_ref, ko_ref, vo_ref, prev_ref, *refs):
    kext, vext, dkacc, dvacc = refs[-4:]
    if finish:
        dko_old, dvo_old, back_old = refs[:3]
        dq_ref, dko_ref, dvo_ref, dprev_ref, gk_ref, gv_ref = refs[-10:-4]
    else:
        dq_ref, dko_ref, dvo_ref, dprev_ref = refs[-8:-4]
    rows = q_ref.shape[0]
    d = HEAD_DIMENSION
    w = WINDOW_TOKENS
    span = BLOCK_Q + w
    scale = jnp.float32(QPRE ** (-0.5))

    kext[0:w, :] = prev_ref[0]
    kext[w:w + rows, :] = ko_ref[...]
    vext[0:w, :] = prev_ref[1]
    vext[w:w + rows, :] = vo_ref[...]
    dkacc[...] = jnp.zeros_like(dkacc)
    dvacc[...] = jnp.zeros_like(dvacc)

    offsets = (lax.broadcasted_iota(jnp.int32, (BLOCK_Q, span), 1)
               - lax.broadcasted_iota(jnp.int32, (BLOCK_Q, span), 0))

    def body(b, carry):
        r0 = pl.multiple_of(b * BLOCK_Q, BLOCK_Q)
        q = q_ref[pl.ds(r0, BLOCK_Q), :]
        do = do_ref[pl.ds(r0, BLOCK_Q), :]
        q2 = jnp.concatenate([q[:, :d], q[:, d:]], axis=0)
        do2 = jnp.concatenate([do[:, :d], do[:, d:]], axis=0)
        kw = kext[pl.ds(r0, span), :]
        vw = vext[pl.ds(r0, span), :]
        reach = reach_ref[pl.ds(r0, BLOCK_Q), :]
        visible = (offsets <= w) & (offsets > w - reach)
        visible = jnp.concatenate([visible, visible], axis=0)
        s = lax.dot_general(q2, kw, NT_DIMS, preferred_element_type=jnp.float32)
        s = jnp.where(visible, s, -jnp.inf)
        top = jnp.max(s, axis=-1, keepdims=True)
        e = jnp.exp((s - top) * scale)
        total = jnp.sum(e, axis=-1, keepdims=True)
        p = e * (1.0 / total)
        dp = lax.dot_general(do2, vw, NT_DIMS, preferred_element_type=jnp.float32)
        delta = jnp.sum(p * dp, axis=-1, keepdims=True)
        ds = (scale * p * (dp - delta)).astype(jnp.bfloat16)
        pb = p.astype(jnp.bfloat16)
        dq2 = jnp.dot(ds, kw, preferred_element_type=jnp.float32)
        dq_ref[pl.ds(r0, BLOCK_Q), :] = jnp.concatenate(
            [dq2[:BLOCK_Q], dq2[BLOCK_Q:]], axis=1).astype(dq_ref.dtype)
        dk = lax.dot_general(ds, q2, TN_DIMS, preferred_element_type=jnp.float32)
        dv = lax.dot_general(pb, do2, TN_DIMS, preferred_element_type=jnp.float32)
        dkacc[pl.ds(r0, span), :] += dk
        dvacc[pl.ds(r0, span), :] += dv
        return carry

    if finish:
        @pl.when(pl.program_id(0) == 0)
        def _():
            gk_ref[...] = dko_old[...].astype(gk_ref.dtype)
            gv_ref[...] = dvo_old[...].astype(gv_ref.dtype)
            gk_ref[rows - w:, :] = (dko_old[rows - w:, :]
                                    + back_old[0].astype(jnp.float32)).astype(gk_ref.dtype)
            gv_ref[rows - w:, :] = (dvo_old[rows - w:, :]
                                    + back_old[1].astype(jnp.float32)).astype(gv_ref.dtype)

    lax.fori_loop(0, rows // BLOCK_Q, body, 0)
    dko_ref[...] = dkacc[w:w + rows, :]
    dvo_ref[...] = dvacc[w:w + rows, :]
    dprev_ref[0] = dkacc[0:w, :].astype(dprev_ref.dtype)
    dprev_ref[1] = dvacc[0:w, :].astype(dprev_ref.dtype)


def attention_head(group, reach_col, queries, output_gradient, keys, values, previous,
                   dq_buf, older, grad_bufs):
    rows, q_width = queries.shape
    kv_width = keys.shape[1]
    d = HEAD_DIMENSION
    w = WINDOW_TOKENS
    h0, n = group
    q_spec = pl.BlockSpec((rows, 2 * d), lambda i: (0, h0 + i))
    own_spec = pl.BlockSpec((rows, d), lambda i: (0, h0 + i))
    col_spec = pl.BlockSpec((rows, d), lambda i: (0, i))
    prev_spec = pl.BlockSpec((2, w, d), lambda i: (0, 0, i))
    any_spec = pl.BlockSpec(memory_space=pl.ANY)
    finish = older is not None
    in_specs = [pl.BlockSpec((rows, 1), lambda i: (0, 0)),
                q_spec, q_spec, own_spec, own_spec, prev_spec]
    operands = [reach_col, queries, output_gradient, keys, values, previous]
    out_specs = [q_spec, col_spec, col_spec, prev_spec]
    out_shape = [
        jax.ShapeDtypeStruct((rows, q_width), jnp.bfloat16),
        jax.ShapeDtypeStruct((rows, n * d), jnp.float32),
        jax.ShapeDtypeStruct((rows, n * d), jnp.float32),
        jax.ShapeDtypeStruct((2, w, n * d), jnp.bfloat16),
    ]
    aliases = {}
    if finish:
        old0, old_n = older[0]
        whole_spec = pl.BlockSpec((rows, old_n * d), lambda i: (0, 0))
        in_specs += [whole_spec, whole_spec, pl.BlockSpec((2, w, old_n * d), lambda i: (0, 0, 0))]
        operands += list(older[1:])
        old_spec = pl.BlockSpec((rows, old_n * d), lambda i: (0, old0 // old_n))
        out_specs += [old_spec, old_spec]
        out_shape += [jax.ShapeDtypeStruct((rows, kv_width), jnp.bfloat16)] * 2
    buffers = ([] if dq_buf is None else [(dq_buf, 0)]) + (
        [] if grad_bufs is None else [(grad_bufs[0], 4), (grad_bufs[1], 5)])
    for buf, out_index in buffers:
        aliases[len(operands)] = out_index
        in_specs.append(any_spec)
        operands.append(buf)
    flops = n * VPU_FACTOR * (rows // BLOCK_Q) * 5 * 2 * (2 * BLOCK_Q) * (BLOCK_Q + w) * d
    cost = pl.CostEstimate(
        flops=flops,
        transcendentals=n * rows * 2 * (BLOCK_Q + w),
        bytes_accessed=n * 2 * (3 * rows * 2 * d + 2 * rows * d + 4 * w * d) + 4 * 2 * rows * d,
    )
    return pl.pallas_call(
        functools.partial(attention_kernel, finish),
        name="attention_backward",
        grid=(n,),
        in_specs=in_specs,
        out_specs=out_specs,
        out_shape=out_shape,
        scratch_shapes=[
            pltpu.VMEM((w + rows, d), jnp.bfloat16),
            pltpu.VMEM((w + rows, d), jnp.bfloat16),
            pltpu.VMEM((w + rows, d), jnp.float32),
            pltpu.VMEM((w + rows, d), jnp.float32),
        ],
        input_output_aliases=aliases,
        compiler_params=pltpu.CompilerParams(dimension_semantics=("arbitrary",)),
        cost_estimate=cost,
    )(*operands)


def head_groups(heads):
    sizes = [1, 1] + [2] * ((heads - 4) // 2) + [1] * (heads - 2 - 2 * ((heads - 4) // 2))
    if heads < 4:
        sizes = [1] * heads
    starts = [sum(sizes[:i]) for i in range(len(sizes))]
    return list(zip(starts, sizes))


def finish_columns(grad, group, own, back):
    rows = own.shape[0]
    w = WINDOW_TOKENS
    d = HEAD_DIMENSION
    total = own.at[rows - w:].add(back.astype(jnp.float32)).astype(jnp.bfloat16)
    return lax.dynamic_update_slice(grad, total, (0, group[0] * d))


def on_device(queries, keys, values, output_gradient, reach):
    rows, q_width = queries.shape
    kv_width = keys.shape[1]
    d = HEAD_DIMENSION
    w = WINDOW_TOKENS
    groups = head_groups(kv_width // d)
    heads = len(groups)
    reach_col = reach.reshape(rows, 1)
    sends = [jnp.stack([keys[rows - w:, h0 * d:(h0 + n) * d], values[rows - w:, h0 * d:(h0 + n) * d]])
             for h0, n in groups]
    arrived = {0: doc_shift(sends[0], 1)}
    dq_buf = None
    grad_bufs = None
    pending = []
    for g in range(heads):
        for later in range(g + 1, min(g + SEND_DEPTH, heads - 1) + 1):
            if later not in arrived:
                gated, arrived[g] = lax.optimization_barrier((sends[later], arrived[g]))
                arrived[later] = doc_shift(gated, 1)
        older = pending.pop(0) if len(pending) >= FINISH_LAG else None
        outs = attention_head(
            groups[g], reach_col, queries, output_gradient, keys, values, arrived.pop(g),
            dq_buf, older, grad_bufs)
        dq_buf, dk_own, dv_own, dprev = outs[:4]
        if older is not None:
            grad_bufs = tuple(outs[4:6])
        pending.append((groups[g], dk_own, dv_own, doc_shift(dprev, -1)))
    if grad_bufs is None:
        grad_bufs = (jnp.zeros((rows, kv_width), jnp.bfloat16),) * 2
    grad_keys, grad_values = grad_bufs
    for h, dk_own, dv_own, back in pending:
        grad_keys = finish_columns(grad_keys, h, dk_own, back[0])
        grad_values = finish_columns(grad_values, h, dv_own, back[1])
    return (dq_buf, grad_keys, grad_values)


def solution(mesh):
    placed = (
        P(("slab", "ctx"), None),
        P(("slab", "ctx"), None),
        P(("slab", "ctx"), None),
        P(("slab", "ctx"), None),
        P(("slab", "ctx")),
    )
    return jax.shard_map(
        on_device,
        mesh=mesh,
        in_specs=placed,
        out_specs=(P(("slab", "ctx"), None), P(("slab", "ctx"), None), P(("slab", "ctx"), None)),
        check_vma=False,
    )
```

```python
import functools

import jax
import jax.numpy as jnp
from jax import lax
from jax.experimental import pallas as pl
from jax.experimental.pallas import tpu as pltpu
from jax.sharding import PartitionSpec as P

HEAD_DIMENSION = 128
WINDOW_TOKENS = 1024
QPRE = 168
BLOCK_Q = 128
VPU_FACTOR = 5
SEND_DEPTH = 2
FINISH_LAG = 1 << 30

NT_DIMS = (((1,), (1,)), ((), ()))
TN_DIMS = (((0,), (0,)), ((), ()))


def doc_shift(x, by):
    count = lax.axis_size("slab") * lax.axis_size("ctx")
    pairs = [(i, i + by) for i in range(count) if 0 <= i + by < count]
    return lax.ppermute(x, ("slab", "ctx"), pairs)


def attention_kernel(finish, reach_ref, q_ref, do_ref, ko_ref, vo_ref, prev_ref, *refs):
    kext, vext, dkacc, dvacc = refs[-4:]
    if finish:
        dko_old, dvo_old, back_old = refs[:3]
        dq_ref, dko_ref, dvo_ref, dprev_ref, gk_ref, gv_ref = refs[-10:-4]
    else:
        dq_ref, dko_ref, dvo_ref, dprev_ref = refs[-8:-4]
    rows = q_ref.shape[0]
    d = HEAD_DIMENSION
    w = WINDOW_TOKENS
    span = BLOCK_Q + w
    scale = jnp.float32(QPRE ** (-0.5))

    kext[0:w, :] = prev_ref[0]
    kext[w:w + rows, :] = ko_ref[...]
    vext[0:w, :] = prev_ref[1]
    vext[w:w + rows, :] = vo_ref[...]
    dkacc[...] = jnp.zeros_like(dkacc)
    dvacc[...] = jnp.zeros_like(dvacc)

    offsets = (lax.broadcasted_iota(jnp.int32, (BLOCK_Q, span), 1)
               - lax.broadcasted_iota(jnp.int32, (BLOCK_Q, span), 0))

    def body(b, carry):
        r0 = pl.multiple_of(b * BLOCK_Q, BLOCK_Q)
        q = q_ref[pl.ds(r0, BLOCK_Q), :]
        do = do_ref[pl.ds(r0, BLOCK_Q), :]
        q2 = jnp.concatenate([q[:, :d], q[:, d:]], axis=0)
        do2 = jnp.concatenate([do[:, :d], do[:, d:]], axis=0)
        kw = kext[pl.ds(r0, span), :]
        vw = vext[pl.ds(r0, span), :]
        reach = reach_ref[pl.ds(r0, BLOCK_Q), :]
        visible = (offsets <= w) & (offsets > w - reach)
        visible = jnp.concatenate([visible, visible], axis=0)
        s = lax.dot_general(q2, kw, NT_DIMS, preferred_element_type=jnp.float32)
        s = jnp.where(visible, s, -jnp.inf)
        top = jnp.max(s, axis=-1, keepdims=True)
        e = jnp.exp((s - top) * scale)
        total = jnp.sum(e, axis=-1, keepdims=True)
        p = e * (1.0 / total)
        dp = lax.dot_general(do2, vw, NT_DIMS, preferred_element_type=jnp.float32)
        delta = jnp.sum(p * dp, axis=-1, keepdims=True)
        ds = (scale * p * (dp - delta)).astype(jnp.bfloat16)
        pb = p.astype(jnp.bfloat16)
        dq2 = jnp.dot(ds, kw, preferred_element_type=jnp.float32)
        dq_ref[pl.ds(r0, BLOCK_Q), :] = jnp.concatenate(
            [dq2[:BLOCK_Q], dq2[BLOCK_Q:]], axis=1).astype(dq_ref.dtype)
        dk = lax.dot_general(ds, q2, TN_DIMS, preferred_element_type=jnp.float32)
        dv = lax.dot_general(pb, do2, TN_DIMS, preferred_element_type=jnp.float32)
        dkacc[pl.ds(r0, span), :] += dk
        dvacc[pl.ds(r0, span), :] += dv
        return carry

    if finish:
        @pl.when(pl.program_id(0) == 0)
        def _():
            gk_ref[...] = dko_old[...].astype(gk_ref.dtype)
            gv_ref[...] = dvo_old[...].astype(gv_ref.dtype)
            gk_ref[rows - w:, :] = (dko_old[rows - w:, :]
                                    + back_old[0].astype(jnp.float32)).astype(gk_ref.dtype)
            gv_ref[rows - w:, :] = (dvo_old[rows - w:, :]
                                    + back_old[1].astype(jnp.float32)).astype(gv_ref.dtype)

    lax.fori_loop(0, rows // BLOCK_Q, body, 0)
    dko_ref[...] = dkacc[w:w + rows, :]
    dvo_ref[...] = dvacc[w:w + rows, :]
    dprev_ref[0] = dkacc[0:w, :].astype(dprev_ref.dtype)
    dprev_ref[1] = dvacc[0:w, :].astype(dprev_ref.dtype)


def attention_head(group, reach_col, queries, output_gradient, keys, values, previous,
                   dq_buf, older, grad_bufs):
    rows, q_width = queries.shape
    kv_width = keys.shape[1]
    d = HEAD_DIMENSION
    w = WINDOW_TOKENS
    h0, n = group
    q_spec = pl.BlockSpec((rows, 2 * d), lambda i: (0, h0 + i))
    own_spec = pl.BlockSpec((rows, d), lambda i: (0, h0 + i))
    col_spec = pl.BlockSpec((rows, d), lambda i: (0, i))
    prev_spec = pl.BlockSpec((2, w, d), lambda i: (0, 0, i))
    any_spec = pl.BlockSpec(memory_space=pl.ANY)
    finish = older is not None
    in_specs = [pl.BlockSpec((rows, 1), lambda i: (0, 0)),
                q_spec, q_spec, own_spec, own_spec, prev_spec]
    operands = [reach_col, queries, output_gradient, keys, values, previous]
    out_specs = [q_spec, col_spec, col_spec, prev_spec]
    out_shape = [
        jax.ShapeDtypeStruct((rows, q_width), jnp.bfloat16),
        jax.ShapeDtypeStruct((rows, n * d), jnp.float32),
        jax.ShapeDtypeStruct((rows, n * d), jnp.float32),
        jax.ShapeDtypeStruct((2, w, n * d), jnp.bfloat16),
    ]
    aliases = {}
    if finish:
        old0, old_n = older[0]
        whole_spec = pl.BlockSpec((rows, old_n * d), lambda i: (0, 0))
        in_specs += [whole_spec, whole_spec, pl.BlockSpec((2, w, old_n * d), lambda i: (0, 0, 0))]
        operands += list(older[1:])
        old_spec = pl.BlockSpec((rows, old_n * d), lambda i: (0, old0 // old_n))
        out_specs += [old_spec, old_spec]
        out_shape += [jax.ShapeDtypeStruct((rows, kv_width), jnp.bfloat16)] * 2
    buffers = ([] if dq_buf is None else [(dq_buf, 0)]) + (
        [] if grad_bufs is None else [(grad_bufs[0], 4), (grad_bufs[1], 5)])
    for buf, out_index in buffers:
        aliases[len(operands)] = out_index
        in_specs.append(any_spec)
        operands.append(buf)
    flops = n * VPU_FACTOR * (rows // BLOCK_Q) * 5 * 2 * (2 * BLOCK_Q) * (BLOCK_Q + w) * d
    cost = pl.CostEstimate(
        flops=flops,
        transcendentals=n * rows * 2 * (BLOCK_Q + w),
        bytes_accessed=n * 2 * (3 * rows * 2 * d + 2 * rows * d + 4 * w * d) + 4 * 2 * rows * d,
    )
    return pl.pallas_call(
        functools.partial(attention_kernel, finish),
        name="attention_backward",
        grid=(n,),
        in_specs=in_specs,
        out_specs=out_specs,
        out_shape=out_shape,
        scratch_shapes=[
            pltpu.VMEM((w + rows, d), jnp.bfloat16),
            pltpu.VMEM((w + rows, d), jnp.bfloat16),
            pltpu.VMEM((w + rows, d), jnp.float32),
            pltpu.VMEM((w + rows, d), jnp.float32),
        ],
        input_output_aliases=aliases,
        compiler_params=pltpu.CompilerParams(dimension_semantics=("arbitrary",)),
        cost_estimate=cost,
    )(*operands)


def head_groups(heads):
    sizes = [1, 1] + [2] * ((heads - 4) // 2) + [1] * (heads - 2 - 2 * ((heads - 4) // 2))
    if heads < 4:
        sizes = [1] * heads
    starts = [sum(sizes[:i]) for i in range(len(sizes))]
    return list(zip(starts, sizes))


def finish_columns(grad, group, own, back):
    rows = own.shape[0]
    w = WINDOW_TOKENS
    d = HEAD_DIMENSION
    total = own.at[rows - w:].add(back.astype(jnp.float32)).astype(jnp.bfloat16)
    return lax.dynamic_update_slice(grad, total, (0, group[0] * d))


def on_device(queries, keys, values, output_gradient, reach):
    rows, q_width = queries.shape
    kv_width = keys.shape[1]
    d = HEAD_DIMENSION
    w = WINDOW_TOKENS
    groups = head_groups(kv_width // d)
    heads = len(groups)
    reach_col = reach.reshape(rows, 1)
    sends = [jnp.stack([keys[rows - w:, h0 * d:(h0 + n) * d], values[rows - w:, h0 * d:(h0 + n) * d]])
             for h0, n in groups]
    arrived = {0: doc_shift(sends[0], 1)}
    dq_buf = None
    grad_bufs = None
    pending = []
    for g in range(heads):
        for later in range(g + 1, min(g + SEND_DEPTH, heads - 1) + 1):
            if later not in arrived:
                gated, arrived[g] = lax.optimization_barrier((sends[later], arrived[g]))
                arrived[later] = doc_shift(gated, 1)
        older = pending.pop(0) if len(pending) >= FINISH_LAG else None
        outs = attention_head(
            groups[g], reach_col, queries, output_gradient, keys, values, arrived.pop(g),
            dq_buf, older, grad_bufs)
        dq_buf, dk_own, dv_own, dprev = outs[:4]
        if older is not None:
            grad_bufs = tuple(outs[4:6])
        pending.append((groups[g], dk_own, dv_own, doc_shift(dprev, -1)))
    if grad_bufs is None:
        grad_bufs = (jnp.zeros((rows, kv_width), jnp.bfloat16),) * 2
    grad_keys, grad_values = grad_bufs
    for h, dk_own, dv_own, back in pending:
        grad_keys = finish_columns(grad_keys, h, dk_own, back[0])
        grad_values = finish_columns(grad_values, h, dv_own, back[1])
    return (dq_buf, grad_keys, grad_values)


def solution(mesh):
    placed = (
        P(("slab", "ctx"), None),
        P(("slab", "ctx"), None),
        P(("slab", "ctx"), None),
        P(("slab", "ctx"), None),
        P(("slab", "ctx")),
    )
    return jax.shard_map(
        on_device,
        mesh=mesh,
        in_specs=placed,
        out_specs=(P(("slab", "ctx"), None), P(("slab", "ctx"), None), P(("slab", "ctx"), None)),
        check_vma=False,
    )
```

```python
import functools

import jax
import jax.numpy as jnp
from jax import lax
from jax.experimental import pallas as pl
from jax.experimental.pallas import tpu as pltpu
from jax.sharding import PartitionSpec as P

HEAD_DIMENSION = 128
WINDOW_TOKENS = 1024
QPRE = 168
BLOCK_Q = 128
VPU_FACTOR = 5
SEND_DEPTH = 2
FINISH_LAG = 2
GROUP_HEADS = 4

NT_DIMS = (((1,), (1,)), ((), ()))
TN_DIMS = (((0,), (0,)), ((), ()))


def doc_shift(x, by):
    count = lax.axis_size("slab") * lax.axis_size("ctx")
    pairs = [(i, i + by) for i in range(count) if 0 <= i + by < count]
    return lax.ppermute(x, ("slab", "ctx"), pairs)


def attention_kernel(finish, reach_ref, q_ref, do_ref, ko_ref, vo_ref, prev_ref, *refs):
    kext, vext, dkacc, dvacc = refs[-4:]
    if finish:
        dko_old, dvo_old, back_old = refs[:3]
        dq_ref, dko_ref, dvo_ref, dprev_ref, gk_ref, gv_ref = refs[-10:-4]
    else:
        dq_ref, dko_ref, dvo_ref, dprev_ref = refs[-8:-4]
    rows = q_ref.shape[0]
    d = HEAD_DIMENSION
    w = WINDOW_TOKENS
    span = BLOCK_Q + w
    scale = jnp.float32(QPRE ** (-0.5))

    kext[0:w, :] = prev_ref[0]
    kext[w:w + rows, :] = ko_ref[...]
    vext[0:w, :] = prev_ref[1]
    vext[w:w + rows, :] = vo_ref[...]
    dkacc[...] = jnp.zeros_like(dkacc)
    dvacc[...] = jnp.zeros_like(dvacc)

    offsets = (lax.broadcasted_iota(jnp.int32, (BLOCK_Q, span), 1)
               - lax.broadcasted_iota(jnp.int32, (BLOCK_Q, span), 0))

    def body(b, carry):
        r0 = pl.multiple_of(b * BLOCK_Q, BLOCK_Q)
        q = q_ref[pl.ds(r0, BLOCK_Q), :]
        do = do_ref[pl.ds(r0, BLOCK_Q), :]
        q2 = jnp.concatenate([q[:, :d], q[:, d:]], axis=0)
        do2 = jnp.concatenate([do[:, :d], do[:, d:]], axis=0)
        kw = kext[pl.ds(r0, span), :]
        vw = vext[pl.ds(r0, span), :]
        reach = reach_ref[pl.ds(r0, BLOCK_Q), :]
        visible = (offsets <= w) & (offsets > w - reach)
        visible = jnp.concatenate([visible, visible], axis=0)
        s = lax.dot_general(q2, kw, NT_DIMS, preferred_element_type=jnp.float32)
        s = jnp.where(visible, s, -jnp.inf)
        top = jnp.max(s, axis=-1, keepdims=True)
        e = jnp.exp((s - top) * scale)
        total = jnp.sum(e, axis=-1, keepdims=True)
        p = e * (1.0 / total)
        dp = lax.dot_general(do2, vw, NT_DIMS, preferred_element_type=jnp.float32)
        delta = jnp.sum(p * dp, axis=-1, keepdims=True)
        ds = (scale * p * (dp - delta)).astype(jnp.bfloat16)
        pb = p.astype(jnp.bfloat16)
        dq2 = jnp.dot(ds, kw, preferred_element_type=jnp.float32)
        dq_ref[pl.ds(r0, BLOCK_Q), :] = jnp.concatenate(
            [dq2[:BLOCK_Q], dq2[BLOCK_Q:]], axis=1).astype(dq_ref.dtype)
        dk = lax.dot_general(ds, q2, TN_DIMS, preferred_element_type=jnp.float32)
        dv = lax.dot_general(pb, do2, TN_DIMS, preferred_element_type=jnp.float32)
        dkacc[pl.ds(r0, span), :] += dk
        dvacc[pl.ds(r0, span), :] += dv
        return carry

    if finish:
        @pl.when(pl.program_id(0) == 0)
        def _():
            gk_ref[...] = dko_old[...].astype(gk_ref.dtype)
            gv_ref[...] = dvo_old[...].astype(gv_ref.dtype)
            gk_ref[rows - w:, :] = (dko_old[rows - w:, :]
                                    + back_old[0].astype(jnp.float32)).astype(gk_ref.dtype)
            gv_ref[rows - w:, :] = (dvo_old[rows - w:, :]
                                    + back_old[1].astype(jnp.float32)).astype(gv_ref.dtype)

    lax.fori_loop(0, rows // BLOCK_Q, body, 0)
    dko_ref[...] = dkacc[w:w + rows, :]
    dvo_ref[...] = dvacc[w:w + rows, :]
    dprev_ref[0] = dkacc[0:w, :].astype(dprev_ref.dtype)
    dprev_ref[1] = dvacc[0:w, :].astype(dprev_ref.dtype)


def attention_head(group, reach_col, queries, output_gradient, keys, values, previous,
                   dq_buf, older, grad_bufs):
    rows, q_width = queries.shape
    kv_width = keys.shape[1]
    d = HEAD_DIMENSION
    w = WINDOW_TOKENS
    h0, n = group
    q_spec = pl.BlockSpec((rows, 2 * d), lambda i: (0, h0 + i))
    own_spec = pl.BlockSpec((rows, d), lambda i: (0, h0 + i))
    col_spec = pl.BlockSpec((rows, d), lambda i: (0, i))
    prev_spec = pl.BlockSpec((2, w, d), lambda i: (0, 0, i))
    any_spec = pl.BlockSpec(memory_space=pl.ANY)
    finish = older is not None
    in_specs = [pl.BlockSpec((rows, 1), lambda i: (0, 0)),
                q_spec, q_spec, own_spec, own_spec, prev_spec]
    operands = [reach_col, queries, output_gradient, keys, values, previous]
    out_specs = [q_spec, col_spec, col_spec, prev_spec]
    out_shape = [
        jax.ShapeDtypeStruct((rows, q_width), jnp.bfloat16),
        jax.ShapeDtypeStruct((rows, n * d), jnp.float32),
        jax.ShapeDtypeStruct((rows, n * d), jnp.float32),
        jax.ShapeDtypeStruct((2, w, n * d), jnp.bfloat16),
    ]
    aliases = {}
    if finish:
        old0, old_n = older[0]
        whole_spec = pl.BlockSpec((rows, old_n * d), lambda i: (0, 0))
        in_specs += [whole_spec, whole_spec, pl.BlockSpec((2, w, old_n * d), lambda i: (0, 0, 0))]
        operands += list(older[1:])
        old_spec = pl.BlockSpec((rows, old_n * d), lambda i: (0, old0 // old_n))
        out_specs += [old_spec, old_spec]
        out_shape += [jax.ShapeDtypeStruct((rows, kv_width), jnp.bfloat16)] * 2
    buffers = ([] if dq_buf is None else [(dq_buf, 0)]) + (
        [] if grad_bufs is None else [(grad_bufs[0], 4), (grad_bufs[1], 5)])
    for buf, out_index in buffers:
        aliases[len(operands)] = out_index
        in_specs.append(any_spec)
        operands.append(buf)
    flops = n * VPU_FACTOR * (rows // BLOCK_Q) * 5 * 2 * (2 * BLOCK_Q) * (BLOCK_Q + w) * d
    cost = pl.CostEstimate(
        flops=flops,
        transcendentals=n * rows * 2 * (BLOCK_Q + w),
        bytes_accessed=n * 2 * (3 * rows * 2 * d + 2 * rows * d + 4 * w * d) + 4 * 2 * rows * d,
    )
    return pl.pallas_call(
        functools.partial(attention_kernel, finish),
        name="attention_backward",
        grid=(n,),
        in_specs=in_specs,
        out_specs=out_specs,
        out_shape=out_shape,
        scratch_shapes=[
            pltpu.VMEM((w + rows, d), jnp.bfloat16),
            pltpu.VMEM((w + rows, d), jnp.bfloat16),
            pltpu.VMEM((w + rows, d), jnp.float32),
            pltpu.VMEM((w + rows, d), jnp.float32),
        ],
        input_output_aliases=aliases,
        compiler_params=pltpu.CompilerParams(dimension_semantics=("arbitrary",)),
        cost_estimate=cost,
    )(*operands)


def head_groups(heads):
    size = GROUP_HEADS if heads % GROUP_HEADS == 0 else 1
    return [(h0, size) for h0 in range(0, heads, size)]


def finish_columns(grad, group, own, back):
    rows = own.shape[0]
    w = WINDOW_TOKENS
    d = HEAD_DIMENSION
    total = own.at[rows - w:].add(back.astype(jnp.float32)).astype(jnp.bfloat16)
    return lax.dynamic_update_slice(grad, total, (0, group[0] * d))


def on_device(queries, keys, values, output_gradient, reach):
    rows, q_width = queries.shape
    kv_width = keys.shape[1]
    d = HEAD_DIMENSION
    w = WINDOW_TOKENS
    groups = head_groups(kv_width // d)
    heads = len(groups)
    reach_col = reach.reshape(rows, 1)
    sends = [jnp.stack([keys[rows - w:, h0 * d:(h0 + n) * d], values[rows - w:, h0 * d:(h0 + n) * d]])
             for h0, n in groups]
    arrived = {0: doc_shift(sends[0], 1)}
    dq_buf = None
    grad_bufs = None
    pending = []
    for g in range(heads):
        for later in range(g + 1, min(g + SEND_DEPTH, heads - 1) + 1):
            if later not in arrived:
                gated, arrived[g] = lax.optimization_barrier((sends[later], arrived[g]))
                arrived[later] = doc_shift(gated, 1)
        older = pending.pop(0) if len(pending) >= FINISH_LAG else None
        outs = attention_head(
            groups[g], reach_col, queries, output_gradient, keys, values, arrived.pop(g),
            dq_buf, older, grad_bufs)
        dq_buf, dk_own, dv_own, dprev = outs[:4]
        if older is not None:
            grad_bufs = tuple(outs[4:6])
        pending.append((groups[g], dk_own, dv_own, doc_shift(dprev, -1)))
    if grad_bufs is None:
        grad_bufs = (jnp.zeros((rows, kv_width), jnp.bfloat16),) * 2
    grad_keys, grad_values = grad_bufs
    for h, dk_own, dv_own, back in pending:
        grad_keys = finish_columns(grad_keys, h, dk_own, back[0])
        grad_values = finish_columns(grad_values, h, dv_own, back[1])
    return (dq_buf, grad_keys, grad_values)


def solution(mesh):
    placed = (
        P(("slab", "ctx"), None),
        P(("slab", "ctx"), None),
        P(("slab", "ctx"), None),
        P(("slab", "ctx"), None),
        P(("slab", "ctx")),
    )
    return jax.shard_map(
        on_device,
        mesh=mesh,
        in_specs=placed,
        out_specs=(P(("slab", "ctx"), None), P(("slab", "ctx"), None), P(("slab", "ctx"), None)),
        check_vma=False,
    )
```

```python
import functools

import jax
import jax.numpy as jnp
from jax import lax
from jax.experimental import pallas as pl
from jax.experimental.pallas import tpu as pltpu
from jax.sharding import PartitionSpec as P

HEAD_DIMENSION = 128
WINDOW_TOKENS = 1024
QPRE = 168
BLOCK_Q = 128
VPU_FACTOR = 5
SEND_DEPTH = 2
FINISH_LAG = 2
GROUP_HEADS = 4

NT_DIMS = (((1,), (1,)), ((), ()))
TN_DIMS = (((0,), (0,)), ((), ()))


def doc_shift(x, by):
    count = lax.axis_size("slab") * lax.axis_size("ctx")
    pairs = [(i, i + by) for i in range(count) if 0 <= i + by < count]
    return lax.ppermute(x, ("slab", "ctx"), pairs)


def attention_kernel(finish, reach_ref, q_ref, do_ref, ko_ref, vo_ref, prev_ref, *refs):
    kext, vext, dkacc, dvacc, q_t, do_t = refs[-6:]
    if finish:
        dko_old, dvo_old, back_old = refs[:3]
        dq_ref, dko_ref, dvo_ref, dprev_ref, gk_ref, gv_ref = refs[-12:-6]
    else:
        dq_ref, dko_ref, dvo_ref, dprev_ref = refs[-10:-6]
    rows = q_ref.shape[0]
    d = HEAD_DIMENSION
    w = WINDOW_TOKENS
    span = BLOCK_Q + w
    scale = jnp.float32(QPRE ** (-0.5))

    kext[0:w, :] = prev_ref[0]
    kext[w:w + rows, :] = ko_ref[...]
    vext[0:w, :] = prev_ref[1]
    vext[w:w + rows, :] = vo_ref[...]
    dkacc[...] = jnp.zeros_like(dkacc)
    dvacc[...] = jnp.zeros_like(dvacc)
    q_t[...] = q_ref[...].astype(jnp.float32).T.astype(q_t.dtype)
    do_t[...] = do_ref[...].astype(jnp.float32).T.astype(do_t.dtype)

    offsets = (lax.broadcasted_iota(jnp.int32, (BLOCK_Q, span), 1)
               - lax.broadcasted_iota(jnp.int32, (BLOCK_Q, span), 0))

    def body(b, carry):
        r0 = pl.multiple_of(b * BLOCK_Q, BLOCK_Q)
        q = q_ref[pl.ds(r0, BLOCK_Q), :]
        do = do_ref[pl.ds(r0, BLOCK_Q), :]
        q2 = jnp.concatenate([q[:, :d], q[:, d:]], axis=0)
        do2 = jnp.concatenate([do[:, :d], do[:, d:]], axis=0)
        kw = kext[pl.ds(r0, span), :]
        vw = vext[pl.ds(r0, span), :]
        reach = reach_ref[pl.ds(r0, BLOCK_Q), :]
        visible = (offsets <= w) & (offsets > w - reach)
        visible = jnp.concatenate([visible, visible], axis=0)
        s = lax.dot_general(q2, kw, NT_DIMS, preferred_element_type=jnp.float32)
        s = jnp.where(visible, s, -jnp.inf)
        top = jnp.max(s, axis=-1, keepdims=True)
        e = jnp.exp((s - top) * scale)
        total = jnp.sum(e, axis=-1, keepdims=True)
        p = e * (1.0 / total)
        dp = lax.dot_general(do2, vw, NT_DIMS, preferred_element_type=jnp.float32)
        delta = jnp.sum(p * dp, axis=-1, keepdims=True)
        ds = (scale * p * (dp - delta)).astype(jnp.bfloat16)
        pb = p.astype(jnp.bfloat16)
        dq2 = jnp.dot(ds, kw, preferred_element_type=jnp.float32)
        dq_ref[pl.ds(r0, BLOCK_Q), :] = jnp.concatenate(
            [dq2[:BLOCK_Q], dq2[BLOCK_Q:]], axis=1).astype(dq_ref.dtype)
        q2t = jnp.concatenate([q_t[:d, pl.ds(r0, BLOCK_Q)], q_t[d:, pl.ds(r0, BLOCK_Q)]], axis=1)
        do2t = jnp.concatenate([do_t[:d, pl.ds(r0, BLOCK_Q)], do_t[d:, pl.ds(r0, BLOCK_Q)]], axis=1)
        dkacc[:, pl.ds(r0, span)] += jnp.dot(q2t, ds, preferred_element_type=jnp.float32)
        dvacc[:, pl.ds(r0, span)] += jnp.dot(do2t, pb, preferred_element_type=jnp.float32)
        return carry

    if finish:
        @pl.when(pl.program_id(0) == 0)
        def _():
            gk_ref[...] = dko_old[...].astype(gk_ref.dtype)
            gv_ref[...] = dvo_old[...].astype(gv_ref.dtype)
            gk_ref[rows - w:, :] = (dko_old[rows - w:, :]
                                    + back_old[0].astype(jnp.float32)).astype(gk_ref.dtype)
            gv_ref[rows - w:, :] = (dvo_old[rows - w:, :]
                                    + back_old[1].astype(jnp.float32)).astype(gv_ref.dtype)

    lax.fori_loop(0, rows // BLOCK_Q, body, 0)
    dko_ref[...] = dkacc[:, w:w + rows].T
    dvo_ref[...] = dvacc[:, w:w + rows].T
    dprev_ref[0] = dkacc[:, 0:w].T.astype(dprev_ref.dtype)
    dprev_ref[1] = dvacc[:, 0:w].T.astype(dprev_ref.dtype)


def attention_head(group, reach_col, queries, output_gradient, keys, values, previous,
                   dq_buf, older, grad_bufs):
    rows, q_width = queries.shape
    kv_width = keys.shape[1]
    d = HEAD_DIMENSION
    w = WINDOW_TOKENS
    h0, n = group
    q_spec = pl.BlockSpec((rows, 2 * d), lambda i: (0, h0 + i))
    own_spec = pl.BlockSpec((rows, d), lambda i: (0, h0 + i))
    col_spec = pl.BlockSpec((rows, d), lambda i: (0, i))
    prev_spec = pl.BlockSpec((2, w, d), lambda i: (0, 0, i))
    any_spec = pl.BlockSpec(memory_space=pl.ANY)
    finish = older is not None
    in_specs = [pl.BlockSpec((rows, 1), lambda i: (0, 0)),
                q_spec, q_spec, own_spec, own_spec, prev_spec]
    operands = [reach_col, queries, output_gradient, keys, values, previous]
    out_specs = [q_spec, col_spec, col_spec, prev_spec]
    out_shape = [
        jax.ShapeDtypeStruct((rows, q_width), jnp.bfloat16),
        jax.ShapeDtypeStruct((rows, n * d), jnp.float32),
        jax.ShapeDtypeStruct((rows, n * d), jnp.float32),
        jax.ShapeDtypeStruct((2, w, n * d), jnp.bfloat16),
    ]
    aliases = {}
    if finish:
        old0, old_n = older[0]
        whole_spec = pl.BlockSpec((rows, old_n * d), lambda i: (0, 0))
        in_specs += [whole_spec, whole_spec, pl.BlockSpec((2, w, old_n * d), lambda i: (0, 0, 0))]
        operands += list(older[1:])
        old_spec = pl.BlockSpec((rows, old_n * d), lambda i: (0, old0 // old_n))
        out_specs += [old_spec, old_spec]
        out_shape += [jax.ShapeDtypeStruct((rows, kv_width), jnp.bfloat16)] * 2
    buffers = ([] if dq_buf is None else [(dq_buf, 0)]) + (
        [] if grad_bufs is None else [(grad_bufs[0], 4), (grad_bufs[1], 5)])
    for buf, out_index in buffers:
        aliases[len(operands)] = out_index
        in_specs.append(any_spec)
        operands.append(buf)
    flops = n * VPU_FACTOR * (rows // BLOCK_Q) * 5 * 2 * (2 * BLOCK_Q) * (BLOCK_Q + w) * d
    cost = pl.CostEstimate(
        flops=flops,
        transcendentals=n * rows * 2 * (BLOCK_Q + w),
        bytes_accessed=n * 2 * (3 * rows * 2 * d + 2 * rows * d + 4 * w * d) + 4 * 2 * rows * d,
    )
    return pl.pallas_call(
        functools.partial(attention_kernel, finish),
        name="attention_backward",
        grid=(n,),
        in_specs=in_specs,
        out_specs=out_specs,
        out_shape=out_shape,
        scratch_shapes=[
            pltpu.VMEM((w + rows, d), jnp.bfloat16),
            pltpu.VMEM((w + rows, d), jnp.bfloat16),
            pltpu.VMEM((d, w + rows), jnp.float32),
            pltpu.VMEM((d, w + rows), jnp.float32),
            pltpu.VMEM((2 * d, rows), jnp.bfloat16),
            pltpu.VMEM((2 * d, rows), jnp.bfloat16),
        ],
        input_output_aliases=aliases,
        compiler_params=pltpu.CompilerParams(dimension_semantics=("arbitrary",)),
        cost_estimate=cost,
    )(*operands)


def head_groups(heads):
    size = GROUP_HEADS if heads % GROUP_HEADS == 0 else 1
    return [(h0, size) for h0 in range(0, heads, size)]


def finish_columns(grad, group, own, back):
    rows = own.shape[0]
    w = WINDOW_TOKENS
    d = HEAD_DIMENSION
    total = own.at[rows - w:].add(back.astype(jnp.float32)).astype(jnp.bfloat16)
    return lax.dynamic_update_slice(grad, total, (0, group[0] * d))


def on_device(queries, keys, values, output_gradient, reach):
    rows, q_width = queries.shape
    kv_width = keys.shape[1]
    d = HEAD_DIMENSION
    w = WINDOW_TOKENS
    groups = head_groups(kv_width // d)
    heads = len(groups)
    reach_col = reach.reshape(rows, 1)
    sends = [jnp.stack([keys[rows - w:, h0 * d:(h0 + n) * d], values[rows - w:, h0 * d:(h0 + n) * d]])
             for h0, n in groups]
    arrived = {0: doc_shift(sends[0], 1)}
    dq_buf = None
    grad_bufs = None
    pending = []
    for g in range(heads):
        for later in range(g + 1, min(g + SEND_DEPTH, heads - 1) + 1):
            if later not in arrived:
                gated, arrived[g] = lax.optimization_barrier((sends[later], arrived[g]))
                arrived[later] = doc_shift(gated, 1)
        older = pending.pop(0) if len(pending) >= FINISH_LAG else None
        outs = attention_head(
            groups[g], reach_col, queries, output_gradient, keys, values, arrived.pop(g),
            dq_buf, older, grad_bufs)
        dq_buf, dk_own, dv_own, dprev = outs[:4]
        if older is not None:
            grad_bufs = tuple(outs[4:6])
        pending.append((groups[g], dk_own, dv_own, doc_shift(dprev, -1)))
    if grad_bufs is None:
        grad_bufs = (jnp.zeros((rows, kv_width), jnp.bfloat16),) * 2
    grad_keys, grad_values = grad_bufs
    for h, dk_own, dv_own, back in pending:
        grad_keys = finish_columns(grad_keys, h, dk_own, back[0])
        grad_values = finish_columns(grad_values, h, dv_own, back[1])
    return (dq_buf, grad_keys, grad_values)


def solution(mesh):
    placed = (
        P(("slab", "ctx"), None),
        P(("slab", "ctx"), None),
        P(("slab", "ctx"), None),
        P(("slab", "ctx"), None),
        P(("slab", "ctx")),
    )
    return jax.shard_map(
        on_device,
        mesh=mesh,
        in_specs=placed,
        out_specs=(P(("slab", "ctx"), None), P(("slab", "ctx"), None), P(("slab", "ctx"), None)),
        check_vma=False,
    )
```

```python
import functools

import jax
import jax.numpy as jnp
from jax import lax
from jax.experimental import pallas as pl
from jax.experimental.pallas import tpu as pltpu
from jax.sharding import PartitionSpec as P

HEAD_DIMENSION = 128
WINDOW_TOKENS = 1024
QPRE = 168
BLOCK_Q = 128
VPU_FACTOR = 5
SEND_DEPTH = 2
FINISH_LAG = 2
GROUP_HEADS = 4

NT_DIMS = (((1,), (1,)), ((), ()))
TN_DIMS = (((0,), (0,)), ((), ()))


def doc_shift(x, by):
    count = lax.axis_size("slab") * lax.axis_size("ctx")
    pairs = [(i, i + by) for i in range(count) if 0 <= i + by < count]
    return lax.ppermute(x, ("slab", "ctx"), pairs)


def attention_kernel(finish, reach_ref, q_ref, do_ref, ko_ref, vo_ref, prev_ref, *refs):
    kext, vext, dkacc, dvacc, q_t, do_t = refs[-6:]
    if finish:
        dko_old, dvo_old, back_old = refs[:3]
        dq_ref, dko_ref, dvo_ref, dprev_ref, gk_ref, gv_ref = refs[-12:-6]
    else:
        dq_ref, dko_ref, dvo_ref, dprev_ref = refs[-10:-6]
    rows = q_ref.shape[0]
    d = HEAD_DIMENSION
    w = WINDOW_TOKENS
    span = BLOCK_Q + w
    scale = jnp.float32(QPRE ** (-0.5))

    kext[0:w, :] = prev_ref[0]
    kext[w:w + rows, :] = ko_ref[...]
    vext[0:w, :] = prev_ref[1]
    vext[w:w + rows, :] = vo_ref[...]
    dkacc[...] = jnp.zeros_like(dkacc)
    dvacc[...] = jnp.zeros_like(dvacc)
    q_t[...] = q_ref[...].astype(jnp.float32).T.astype(q_t.dtype)
    do_t[...] = do_ref[...].astype(jnp.float32).T.astype(do_t.dtype)

    offsets = (lax.broadcasted_iota(jnp.int32, (BLOCK_Q, span), 1)
               - lax.broadcasted_iota(jnp.int32, (BLOCK_Q, span), 0))

    def body(b, carry):
        r0 = pl.multiple_of(b * BLOCK_Q, BLOCK_Q)
        q = q_ref[pl.ds(r0, BLOCK_Q), :]
        do = do_ref[pl.ds(r0, BLOCK_Q), :]
        q2 = jnp.concatenate([q[:, :d], q[:, d:]], axis=0)
        do2 = jnp.concatenate([do[:, :d], do[:, d:]], axis=0)
        kw = kext[pl.ds(r0, span), :]
        vw = vext[pl.ds(r0, span), :]
        reach = reach_ref[pl.ds(r0, BLOCK_Q), :]
        visible = (offsets <= w) & (offsets > w - reach)
        visible = jnp.concatenate([visible, visible], axis=0)
        s = lax.dot_general(q2, kw, NT_DIMS, preferred_element_type=jnp.float32)
        s = jnp.where(visible, s, -jnp.inf)
        top = jnp.max(s, axis=-1, keepdims=True)
        e = jnp.exp((s - top) * scale)
        total = jnp.sum(e, axis=-1, keepdims=True)
        p = e * (1.0 / total)
        dp = lax.dot_general(do2, vw, NT_DIMS, preferred_element_type=jnp.float32)
        delta = jnp.sum(p * dp, axis=-1, keepdims=True)
        ds = (scale * p * (dp - delta)).astype(jnp.bfloat16)
        pb = p.astype(jnp.bfloat16)
        dq2 = jnp.dot(ds, kw, preferred_element_type=jnp.float32)
        dq_ref[pl.ds(r0, BLOCK_Q), :] = jnp.concatenate(
            [dq2[:BLOCK_Q], dq2[BLOCK_Q:]], axis=1).astype(dq_ref.dtype)
        q2t = jnp.concatenate([q_t[:d, pl.ds(r0, BLOCK_Q)], q_t[d:, pl.ds(r0, BLOCK_Q)]], axis=1)
        do2t = jnp.concatenate([do_t[:d, pl.ds(r0, BLOCK_Q)], do_t[d:, pl.ds(r0, BLOCK_Q)]], axis=1)
        dkacc[:, pl.ds(r0, span)] += jnp.dot(q2t, ds, preferred_element_type=jnp.float32)
        dvacc[:, pl.ds(r0, span)] += jnp.dot(do2t, pb, preferred_element_type=jnp.float32)
        return carry

    if finish:
        @pl.when(pl.program_id(0) == 0)
        def _():
            gk_ref[...] = dko_old[...].astype(gk_ref.dtype)
            gv_ref[...] = dvo_old[...].astype(gv_ref.dtype)
            gk_ref[rows - w:, :] = (dko_old[rows - w:, :]
                                    + back_old[0].astype(jnp.float32)).astype(gk_ref.dtype)
            gv_ref[rows - w:, :] = (dvo_old[rows - w:, :]
                                    + back_old[1].astype(jnp.float32)).astype(gv_ref.dtype)

    lax.fori_loop(0, rows // BLOCK_Q, body, 0)
    dko_ref[...] = dkacc[:, w:w + rows].T
    dvo_ref[...] = dvacc[:, w:w + rows].T
    dprev_ref[0] = dkacc[:, 0:w].T.astype(dprev_ref.dtype)
    dprev_ref[1] = dvacc[:, 0:w].T.astype(dprev_ref.dtype)


def attention_head(group, reach_col, queries, output_gradient, keys, values, previous,
                   dq_buf, older, grad_bufs):
    rows, q_width = queries.shape
    kv_width = keys.shape[1]
    d = HEAD_DIMENSION
    w = WINDOW_TOKENS
    h0, n = group
    q_spec = pl.BlockSpec((rows, 2 * d), lambda i: (0, h0 + i))
    own_spec = pl.BlockSpec((rows, d), lambda i: (0, h0 + i))
    col_spec = pl.BlockSpec((rows, d), lambda i: (0, i))
    prev_spec = pl.BlockSpec((2, w, d), lambda i: (0, 0, i))
    any_spec = pl.BlockSpec(memory_space=pl.ANY)
    finish = older is not None
    in_specs = [pl.BlockSpec((rows, 1), lambda i: (0, 0)),
                q_spec, q_spec, own_spec, own_spec, prev_spec]
    operands = [reach_col, queries, output_gradient, keys, values, previous]
    out_specs = [q_spec, col_spec, col_spec, prev_spec]
    out_shape = [
        jax.ShapeDtypeStruct((rows, q_width), jnp.bfloat16),
        jax.ShapeDtypeStruct((rows, n * d), jnp.float32),
        jax.ShapeDtypeStruct((rows, n * d), jnp.float32),
        jax.ShapeDtypeStruct((2, w, n * d), jnp.bfloat16),
    ]
    aliases = {}
    if finish:
        old0, old_n = older[0]
        whole_spec = pl.BlockSpec((rows, old_n * d), lambda i: (0, 0))
        in_specs += [whole_spec, whole_spec, pl.BlockSpec((2, w, old_n * d), lambda i: (0, 0, 0))]
        operands += list(older[1:])
        old_spec = pl.BlockSpec((rows, old_n * d), lambda i: (0, old0 // old_n))
        out_specs += [old_spec, old_spec]
        out_shape += [jax.ShapeDtypeStruct((rows, kv_width), jnp.bfloat16)] * 2
    buffers = ([] if dq_buf is None else [(dq_buf, 0)]) + (
        [] if grad_bufs is None else [(grad_bufs[0], 4), (grad_bufs[1], 5)])
    for buf, out_index in buffers:
        aliases[len(operands)] = out_index
        in_specs.append(any_spec)
        operands.append(buf)
    flops = n * VPU_FACTOR * (rows // BLOCK_Q) * 5 * 2 * (2 * BLOCK_Q) * (BLOCK_Q + w) * d
    cost = pl.CostEstimate(
        flops=flops,
        transcendentals=n * rows * 2 * (BLOCK_Q + w),
        bytes_accessed=n * 2 * (3 * rows * 2 * d + 2 * rows * d + 4 * w * d) + 4 * 2 * rows * d,
    )
    return pl.pallas_call(
        functools.partial(attention_kernel, finish),
        name="attention_backward",
        grid=(n,),
        in_specs=in_specs,
        out_specs=out_specs,
        out_shape=out_shape,
        scratch_shapes=[
            pltpu.VMEM((w + rows, d), jnp.bfloat16),
            pltpu.VMEM((w + rows, d), jnp.bfloat16),
            pltpu.VMEM((d, w + rows), jnp.float32),
            pltpu.VMEM((d, w + rows), jnp.float32),
            pltpu.VMEM((2 * d, rows), jnp.bfloat16),
            pltpu.VMEM((2 * d, rows), jnp.bfloat16),
        ],
        input_output_aliases=aliases,
        compiler_params=pltpu.CompilerParams(dimension_semantics=("arbitrary",)),
        cost_estimate=cost,
    )(*operands)


def head_groups(heads):
    if heads % GROUP_HEADS or heads < 2 * GROUP_HEADS:
        return [(h0, 1) for h0 in range(heads)]
    half = GROUP_HEADS // 2
    sizes = [half] + [GROUP_HEADS] * (heads // GROUP_HEADS - 1) + [half]
    starts = [sum(sizes[:i]) for i in range(len(sizes))]
    return list(zip(starts, sizes))


def finish_columns(grad, group, own, back):
    rows = own.shape[0]
    w = WINDOW_TOKENS
    d = HEAD_DIMENSION
    total = own.at[rows - w:].add(back.astype(jnp.float32)).astype(jnp.bfloat16)
    return lax.dynamic_update_slice(grad, total, (0, group[0] * d))


def on_device(queries, keys, values, output_gradient, reach):
    rows, q_width = queries.shape
    kv_width = keys.shape[1]
    d = HEAD_DIMENSION
    w = WINDOW_TOKENS
    groups = head_groups(kv_width // d)
    heads = len(groups)
    reach_col = reach.reshape(rows, 1)
    sends = [jnp.stack([keys[rows - w:, h0 * d:(h0 + n) * d], values[rows - w:, h0 * d:(h0 + n) * d]])
             for h0, n in groups]
    arrived = {0: doc_shift(sends[0], 1)}
    dq_buf = None
    grad_bufs = None
    pending = []
    for g in range(heads):
        for later in range(g + 1, min(g + SEND_DEPTH, heads - 1) + 1):
            if later not in arrived:
                gated, arrived[g] = lax.optimization_barrier((sends[later], arrived[g]))
                arrived[later] = doc_shift(gated, 1)
        aligned = bool(pending) and pending[0][0][0] % pending[0][0][1] == 0
        older = pending.pop(0) if len(pending) >= FINISH_LAG and aligned else None
        outs = attention_head(
            groups[g], reach_col, queries, output_gradient, keys, values, arrived.pop(g),
            dq_buf, older, grad_bufs)
        dq_buf, dk_own, dv_own, dprev = outs[:4]
        if older is not None:
            grad_bufs = tuple(outs[4:6])
        pending.append((groups[g], dk_own, dv_own, doc_shift(dprev, -1)))
    if grad_bufs is None:
        grad_bufs = (jnp.zeros((rows, kv_width), jnp.bfloat16),) * 2
    grad_keys, grad_values = grad_bufs
    for h, dk_own, dv_own, back in pending:
        grad_keys = finish_columns(grad_keys, h, dk_own, back[0])
        grad_values = finish_columns(grad_values, h, dv_own, back[1])
    return (dq_buf, grad_keys, grad_values)


def solution(mesh):
    placed = (
        P(("slab", "ctx"), None),
        P(("slab", "ctx"), None),
        P(("slab", "ctx"), None),
        P(("slab", "ctx"), None),
        P(("slab", "ctx")),
    )
    return jax.shard_map(
        on_device,
        mesh=mesh,
        in_specs=placed,
        out_specs=(P(("slab", "ctx"), None), P(("slab", "ctx"), None), P(("slab", "ctx"), None)),
        check_vma=False,
    )
```

```python
import functools

import jax
import jax.numpy as jnp
from jax import lax
from jax.experimental import pallas as pl
from jax.experimental.pallas import tpu as pltpu
from jax.sharding import PartitionSpec as P

HEAD_DIMENSION = 128
WINDOW_TOKENS = 1024
QPRE = 168
BLOCK_Q = 128
VPU_FACTOR = 5
SEND_DEPTH = 2
FINISH_LAG = 2
GROUP_HEADS = 4

NT_DIMS = (((1,), (1,)), ((), ()))
TN_DIMS = (((0,), (0,)), ((), ()))


def doc_shift(x, by):
    count = lax.axis_size("slab") * lax.axis_size("ctx")
    pairs = [(i, i + by) for i in range(count) if 0 <= i + by < count]
    return lax.ppermute(x, ("slab", "ctx"), pairs)


def attention_kernel(finish, reach_ref, q_ref, do_ref, ko_ref, vo_ref, prev_ref, *refs):
    kext, vext, dkacc, dvacc, q_t, do_t = refs[-6:]
    if finish:
        dko_old, dvo_old, back_old = refs[:3]
        dq_ref, dko_ref, dvo_ref, dprev_ref, gk_ref, gv_ref = refs[-12:-6]
    else:
        dq_ref, dko_ref, dvo_ref, dprev_ref = refs[-10:-6]
    rows = q_ref.shape[0]
    d = HEAD_DIMENSION
    w = WINDOW_TOKENS
    span = BLOCK_Q + w
    scale = jnp.float32(QPRE ** (-0.5))

    kext[0:w, :] = prev_ref[0]
    kext[w:w + rows, :] = ko_ref[...]
    vext[0:w, :] = prev_ref[1]
    vext[w:w + rows, :] = vo_ref[...]
    dkacc[...] = jnp.zeros_like(dkacc)
    dvacc[...] = jnp.zeros_like(dvacc)
    q_t[...] = q_ref[...].astype(jnp.float32).T.astype(q_t.dtype)
    do_t[...] = do_ref[...].astype(jnp.float32).T.astype(do_t.dtype)

    offsets = (lax.broadcasted_iota(jnp.int32, (BLOCK_Q, span), 1)
               - lax.broadcasted_iota(jnp.int32, (BLOCK_Q, span), 0))

    def body(b, carry):
        r0 = pl.multiple_of(b * BLOCK_Q, BLOCK_Q)
        q = q_ref[pl.ds(r0, BLOCK_Q), :]
        do = do_ref[pl.ds(r0, BLOCK_Q), :]
        q2 = jnp.concatenate([q[:, :d], q[:, d:]], axis=0)
        do2 = jnp.concatenate([do[:, :d], do[:, d:]], axis=0)
        kw = kext[pl.ds(r0, span), :]
        vw = vext[pl.ds(r0, span), :]
        reach = reach_ref[pl.ds(r0, BLOCK_Q), :]
        visible = (offsets <= w) & (offsets > w - reach)
        s = lax.dot_general(q2, kw, NT_DIMS, preferred_element_type=jnp.float32)
        s = jnp.where(visible[None], s.reshape(2, BLOCK_Q, span), -jnp.inf).reshape(2 * BLOCK_Q, span)
        top = jnp.max(s, axis=-1, keepdims=True)
        e = jnp.exp((s - top) * scale)
        total = jnp.sum(e, axis=-1, keepdims=True)
        p = e * (1.0 / total)
        dp = lax.dot_general(do2, vw, NT_DIMS, preferred_element_type=jnp.float32)
        delta = jnp.sum(p * dp, axis=-1, keepdims=True)
        ds = (scale * p * (dp - delta)).astype(jnp.bfloat16)
        pb = p.astype(jnp.bfloat16)
        dq2 = jnp.dot(ds, kw, preferred_element_type=jnp.float32)
        dq_ref[pl.ds(r0, BLOCK_Q), :] = jnp.concatenate(
            [dq2[:BLOCK_Q], dq2[BLOCK_Q:]], axis=1).astype(dq_ref.dtype)
        q2t = jnp.concatenate([q_t[:d, pl.ds(r0, BLOCK_Q)], q_t[d:, pl.ds(r0, BLOCK_Q)]], axis=1)
        do2t = jnp.concatenate([do_t[:d, pl.ds(r0, BLOCK_Q)], do_t[d:, pl.ds(r0, BLOCK_Q)]], axis=1)
        dkacc[:, pl.ds(r0, span)] += jnp.dot(q2t, ds, preferred_element_type=jnp.float32)
        dvacc[:, pl.ds(r0, span)] += jnp.dot(do2t, pb, preferred_element_type=jnp.float32)
        return carry

    if finish:
        @pl.when(pl.program_id(0) == 0)
        def _():
            gk_ref[...] = dko_old[...].astype(gk_ref.dtype)
            gv_ref[...] = dvo_old[...].astype(gv_ref.dtype)
            gk_ref[rows - w:, :] = (dko_old[rows - w:, :]
                                    + back_old[0].astype(jnp.float32)).astype(gk_ref.dtype)
            gv_ref[rows - w:, :] = (dvo_old[rows - w:, :]
                                    + back_old[1].astype(jnp.float32)).astype(gv_ref.dtype)

    lax.fori_loop(0, rows // BLOCK_Q, body, 0)
    dko_ref[...] = dkacc[:, w:w + rows].T
    dvo_ref[...] = dvacc[:, w:w + rows].T
    dprev_ref[0] = dkacc[:, 0:w].T.astype(dprev_ref.dtype)
    dprev_ref[1] = dvacc[:, 0:w].T.astype(dprev_ref.dtype)


def attention_head(group, reach_col, queries, output_gradient, keys, values, previous,
                   dq_buf, older, grad_bufs):
    rows, q_width = queries.shape
    kv_width = keys.shape[1]
    d = HEAD_DIMENSION
    w = WINDOW_TOKENS
    h0, n = group
    q_spec = pl.BlockSpec((rows, 2 * d), lambda i: (0, h0 + i))
    own_spec = pl.BlockSpec((rows, d), lambda i: (0, h0 + i))
    col_spec = pl.BlockSpec((rows, d), lambda i: (0, i))
    prev_spec = pl.BlockSpec((2, w, d), lambda i: (0, 0, i))
    any_spec = pl.BlockSpec(memory_space=pl.ANY)
    finish = older is not None
    in_specs = [pl.BlockSpec((rows, 1), lambda i: (0, 0)),
                q_spec, q_spec, own_spec, own_spec, prev_spec]
    operands = [reach_col, queries, output_gradient, keys, values, previous]
    out_specs = [q_spec, col_spec, col_spec, prev_spec]
    out_shape = [
        jax.ShapeDtypeStruct((rows, q_width), jnp.bfloat16),
        jax.ShapeDtypeStruct((rows, n * d), jnp.float32),
        jax.ShapeDtypeStruct((rows, n * d), jnp.float32),
        jax.ShapeDtypeStruct((2, w, n * d), jnp.bfloat16),
    ]
    aliases = {}
    if finish:
        old0, old_n = older[0]
        whole_spec = pl.BlockSpec((rows, old_n * d), lambda i: (0, 0))
        in_specs += [whole_spec, whole_spec, pl.BlockSpec((2, w, old_n * d), lambda i: (0, 0, 0))]
        operands += list(older[1:])
        old_spec = pl.BlockSpec((rows, old_n * d), lambda i: (0, old0 // old_n))
        out_specs += [old_spec, old_spec]
        out_shape += [jax.ShapeDtypeStruct((rows, kv_width), jnp.bfloat16)] * 2
    buffers = ([] if dq_buf is None else [(dq_buf, 0)]) + (
        [] if grad_bufs is None else [(grad_bufs[0], 4), (grad_bufs[1], 5)])
    for buf, out_index in buffers:
        aliases[len(operands)] = out_index
        in_specs.append(any_spec)
        operands.append(buf)
    flops = n * VPU_FACTOR * (rows // BLOCK_Q) * 5 * 2 * (2 * BLOCK_Q) * (BLOCK_Q + w) * d
    cost = pl.CostEstimate(
        flops=flops,
        transcendentals=n * rows * 2 * (BLOCK_Q + w),
        bytes_accessed=n * 2 * (3 * rows * 2 * d + 2 * rows * d + 4 * w * d) + 4 * 2 * rows * d,
    )
    return pl.pallas_call(
        functools.partial(attention_kernel, finish),
        name="attention_backward",
        grid=(n,),
        in_specs=in_specs,
        out_specs=out_specs,
        out_shape=out_shape,
        scratch_shapes=[
            pltpu.VMEM((w + rows, d), jnp.bfloat16),
            pltpu.VMEM((w + rows, d), jnp.bfloat16),
            pltpu.VMEM((d, w + rows), jnp.float32),
            pltpu.VMEM((d, w + rows), jnp.float32),
            pltpu.VMEM((2 * d, rows), jnp.bfloat16),
            pltpu.VMEM((2 * d, rows), jnp.bfloat16),
        ],
        input_output_aliases=aliases,
        compiler_params=pltpu.CompilerParams(dimension_semantics=("arbitrary",)),
        cost_estimate=cost,
    )(*operands)


def head_groups(heads):
    size = GROUP_HEADS if heads % GROUP_HEADS == 0 else 1
    return [(h0, size) for h0 in range(0, heads, size)]


def finish_columns(grad, group, own, back):
    rows = own.shape[0]
    w = WINDOW_TOKENS
    d = HEAD_DIMENSION
    total = own.at[rows - w:].add(back.astype(jnp.float32)).astype(jnp.bfloat16)
    return lax.dynamic_update_slice(grad, total, (0, group[0] * d))


def on_device(queries, keys, values, output_gradient, reach):
    rows, q_width = queries.shape
    kv_width = keys.shape[1]
    d = HEAD_DIMENSION
    w = WINDOW_TOKENS
    groups = head_groups(kv_width // d)
    heads = len(groups)
    reach_col = reach.reshape(rows, 1)
    sends = [jnp.stack([keys[rows - w:, h0 * d:(h0 + n) * d], values[rows - w:, h0 * d:(h0 + n) * d]])
             for h0, n in groups]
    arrived = {0: doc_shift(sends[0], 1)}
    dq_buf = None
    grad_bufs = None
    pending = []
    for g in range(heads):
        for later in range(g + 1, min(g + SEND_DEPTH, heads - 1) + 1):
            if later not in arrived:
                gated, arrived[g] = lax.optimization_barrier((sends[later], arrived[g]))
                arrived[later] = doc_shift(gated, 1)
        older = pending.pop(0) if len(pending) >= FINISH_LAG else None
        outs = attention_head(
            groups[g], reach_col, queries, output_gradient, keys, values, arrived.pop(g),
            dq_buf, older, grad_bufs)
        dq_buf, dk_own, dv_own, dprev = outs[:4]
        if older is not None:
            grad_bufs = tuple(outs[4:6])
        pending.append((groups[g], dk_own, dv_own, doc_shift(dprev, -1)))
    if grad_bufs is None:
        grad_bufs = (jnp.zeros((rows, kv_width), jnp.bfloat16),) * 2
    grad_keys, grad_values = grad_bufs
    for h, dk_own, dv_own, back in pending:
        grad_keys = finish_columns(grad_keys, h, dk_own, back[0])
        grad_values = finish_columns(grad_values, h, dv_own, back[1])
    return (dq_buf, grad_keys, grad_values)


def solution(mesh):
    placed = (
        P(("slab", "ctx"), None),
        P(("slab", "ctx"), None),
        P(("slab", "ctx"), None),
        P(("slab", "ctx"), None),
        P(("slab", "ctx")),
    )
    return jax.shard_map(
        on_device,
        mesh=mesh,
        in_specs=placed,
        out_specs=(P(("slab", "ctx"), None), P(("slab", "ctx"), None), P(("slab", "ctx"), None)),
        check_vma=False,
    )
```

```python
import functools

import jax
import jax.numpy as jnp
from jax import lax
from jax.experimental import pallas as pl
from jax.experimental.pallas import tpu as pltpu
from jax.sharding import PartitionSpec as P

HEAD_DIMENSION = 128
WINDOW_TOKENS = 1024
QPRE = 168
BLOCK_Q = 256
VPU_FACTOR = 5
SEND_DEPTH = 2
FINISH_LAG = 2
GROUP_HEADS = 4

NT_DIMS = (((1,), (1,)), ((), ()))
TN_DIMS = (((0,), (0,)), ((), ()))


def doc_shift(x, by):
    count = lax.axis_size("slab") * lax.axis_size("ctx")
    pairs = [(i, i + by) for i in range(count) if 0 <= i + by < count]
    return lax.ppermute(x, ("slab", "ctx"), pairs)


def attention_kernel(finish, reach_ref, q_ref, do_ref, ko_ref, vo_ref, prev_ref, *refs):
    kext, vext, dkacc, dvacc, q_t, do_t = refs[-6:]
    if finish:
        dko_old, dvo_old, back_old = refs[:3]
        dq_ref, dko_ref, dvo_ref, dprev_ref, gk_ref, gv_ref = refs[-12:-6]
    else:
        dq_ref, dko_ref, dvo_ref, dprev_ref = refs[-10:-6]
    rows = q_ref.shape[0]
    d = HEAD_DIMENSION
    w = WINDOW_TOKENS
    span = BLOCK_Q + w
    scale = jnp.float32(QPRE ** (-0.5))

    kext[0:w, :] = prev_ref[0]
    kext[w:w + rows, :] = ko_ref[...]
    vext[0:w, :] = prev_ref[1]
    vext[w:w + rows, :] = vo_ref[...]
    dkacc[...] = jnp.zeros_like(dkacc)
    dvacc[...] = jnp.zeros_like(dvacc)
    q_t[...] = q_ref[...].astype(jnp.float32).T.astype(q_t.dtype)
    do_t[...] = do_ref[...].astype(jnp.float32).T.astype(do_t.dtype)

    offsets = (lax.broadcasted_iota(jnp.int32, (BLOCK_Q, span), 1)
               - lax.broadcasted_iota(jnp.int32, (BLOCK_Q, span), 0))

    def body(b, carry):
        r0 = pl.multiple_of(b * BLOCK_Q, BLOCK_Q)
        q = q_ref[pl.ds(r0, BLOCK_Q), :]
        do = do_ref[pl.ds(r0, BLOCK_Q), :]
        q2 = jnp.concatenate([q[:, :d], q[:, d:]], axis=0)
        do2 = jnp.concatenate([do[:, :d], do[:, d:]], axis=0)
        kw = kext[pl.ds(r0, span), :]
        vw = vext[pl.ds(r0, span), :]
        reach = reach_ref[pl.ds(r0, BLOCK_Q), :]
        visible = (offsets <= w) & (offsets > w - reach)
        s = lax.dot_general(q2, kw, NT_DIMS, preferred_element_type=jnp.float32)
        s = jnp.where(visible[None], s.reshape(2, BLOCK_Q, span), -jnp.inf).reshape(2 * BLOCK_Q, span)
        top = jnp.max(s, axis=-1, keepdims=True)
        e = jnp.exp((s - top) * scale)
        total = jnp.sum(e, axis=-1, keepdims=True)
        p = e * (1.0 / total)
        dp = lax.dot_general(do2, vw, NT_DIMS, preferred_element_type=jnp.float32)
        delta = jnp.sum(p * dp, axis=-1, keepdims=True)
        ds = (scale * p * (dp - delta)).astype(jnp.bfloat16)
        pb = p.astype(jnp.bfloat16)
        dq2 = jnp.dot(ds, kw, preferred_element_type=jnp.float32)
        dq_ref[pl.ds(r0, BLOCK_Q), :] = jnp.concatenate(
            [dq2[:BLOCK_Q], dq2[BLOCK_Q:]], axis=1).astype(dq_ref.dtype)
        q2t = jnp.concatenate([q_t[:d, pl.ds(r0, BLOCK_Q)], q_t[d:, pl.ds(r0, BLOCK_Q)]], axis=1)
        do2t = jnp.concatenate([do_t[:d, pl.ds(r0, BLOCK_Q)], do_t[d:, pl.ds(r0, BLOCK_Q)]], axis=1)
        dkacc[:, pl.ds(r0, span)] += jnp.dot(q2t, ds, preferred_element_type=jnp.float32)
        dvacc[:, pl.ds(r0, span)] += jnp.dot(do2t, pb, preferred_element_type=jnp.float32)
        return carry

    if finish:
        @pl.when(pl.program_id(0) == 0)
        def _():
            gk_ref[...] = dko_old[...].astype(gk_ref.dtype)
            gv_ref[...] = dvo_old[...].astype(gv_ref.dtype)
            gk_ref[rows - w:, :] = (dko_old[rows - w:, :]
                                    + back_old[0].astype(jnp.float32)).astype(gk_ref.dtype)
            gv_ref[rows - w:, :] = (dvo_old[rows - w:, :]
                                    + back_old[1].astype(jnp.float32)).astype(gv_ref.dtype)

    lax.fori_loop(0, rows // BLOCK_Q, body, 0)
    dko_ref[...] = dkacc[:, w:w + rows].T
    dvo_ref[...] = dvacc[:, w:w + rows].T
    dprev_ref[0] = dkacc[:, 0:w].T.astype(dprev_ref.dtype)
    dprev_ref[1] = dvacc[:, 0:w].T.astype(dprev_ref.dtype)


def attention_head(group, reach_col, queries, output_gradient, keys, values, previous,
                   dq_buf, older, grad_bufs):
    rows, q_width = queries.shape
    kv_width = keys.shape[1]
    d = HEAD_DIMENSION
    w = WINDOW_TOKENS
    h0, n = group
    q_spec = pl.BlockSpec((rows, 2 * d), lambda i: (0, h0 + i))
    own_spec = pl.BlockSpec((rows, d), lambda i: (0, h0 + i))
    col_spec = pl.BlockSpec((rows, d), lambda i: (0, i))
    prev_spec = pl.BlockSpec((2, w, d), lambda i: (0, 0, i))
    any_spec = pl.BlockSpec(memory_space=pl.ANY)
    finish = older is not None
    in_specs = [pl.BlockSpec((rows, 1), lambda i: (0, 0)),
                q_spec, q_spec, own_spec, own_spec, prev_spec]
    operands = [reach_col, queries, output_gradient, keys, values, previous]
    out_specs = [q_spec, col_spec, col_spec, prev_spec]
    out_shape = [
        jax.ShapeDtypeStruct((rows, q_width), jnp.bfloat16),
        jax.ShapeDtypeStruct((rows, n * d), jnp.float32),
        jax.ShapeDtypeStruct((rows, n * d), jnp.float32),
        jax.ShapeDtypeStruct((2, w, n * d), jnp.bfloat16),
    ]
    aliases = {}
    if finish:
        old0, old_n = older[0]
        whole_spec = pl.BlockSpec((rows, old_n * d), lambda i: (0, 0))
        in_specs += [whole_spec, whole_spec, pl.BlockSpec((2, w, old_n * d), lambda i: (0, 0, 0))]
        operands += list(older[1:])
        old_spec = pl.BlockSpec((rows, old_n * d), lambda i: (0, old0 // old_n))
        out_specs += [old_spec, old_spec]
        out_shape += [jax.ShapeDtypeStruct((rows, kv_width), jnp.bfloat16)] * 2
    buffers = ([] if dq_buf is None else [(dq_buf, 0)]) + (
        [] if grad_bufs is None else [(grad_bufs[0], 4), (grad_bufs[1], 5)])
    for buf, out_index in buffers:
        aliases[len(operands)] = out_index
        in_specs.append(any_spec)
        operands.append(buf)
    flops = n * VPU_FACTOR * (rows // BLOCK_Q) * 5 * 2 * (2 * BLOCK_Q) * (BLOCK_Q + w) * d
    cost = pl.CostEstimate(
        flops=flops,
        transcendentals=n * rows * 2 * (BLOCK_Q + w),
        bytes_accessed=n * 2 * (3 * rows * 2 * d + 2 * rows * d + 4 * w * d) + 4 * 2 * rows * d,
    )
    return pl.pallas_call(
        functools.partial(attention_kernel, finish),
        name="attention_backward",
        grid=(n,),
        in_specs=in_specs,
        out_specs=out_specs,
        out_shape=out_shape,
        scratch_shapes=[
            pltpu.VMEM((w + rows, d), jnp.bfloat16),
            pltpu.VMEM((w + rows, d), jnp.bfloat16),
            pltpu.VMEM((d, w + rows), jnp.float32),
            pltpu.VMEM((d, w + rows), jnp.float32),
            pltpu.VMEM((2 * d, rows), jnp.bfloat16),
            pltpu.VMEM((2 * d, rows), jnp.bfloat16),
        ],
        input_output_aliases=aliases,
        compiler_params=pltpu.CompilerParams(dimension_semantics=("arbitrary",)),
        cost_estimate=cost,
    )(*operands)


def head_groups(heads):
    size = GROUP_HEADS if heads % GROUP_HEADS == 0 else 1
    return [(h0, size) for h0 in range(0, heads, size)]


def finish_columns(grad, group, own, back):
    rows = own.shape[0]
    w = WINDOW_TOKENS
    d = HEAD_DIMENSION
    total = own.at[rows - w:].add(back.astype(jnp.float32)).astype(jnp.bfloat16)
    return lax.dynamic_update_slice(grad, total, (0, group[0] * d))


def on_device(queries, keys, values, output_gradient, reach):
    rows, q_width = queries.shape
    kv_width = keys.shape[1]
    d = HEAD_DIMENSION
    w = WINDOW_TOKENS
    groups = head_groups(kv_width // d)
    heads = len(groups)
    reach_col = reach.reshape(rows, 1)
    sends = [jnp.stack([keys[rows - w:, h0 * d:(h0 + n) * d], values[rows - w:, h0 * d:(h0 + n) * d]])
             for h0, n in groups]
    arrived = {0: doc_shift(sends[0], 1)}
    dq_buf = None
    grad_bufs = None
    pending = []
    for g in range(heads):
        for later in range(g + 1, min(g + SEND_DEPTH, heads - 1) + 1):
            if later not in arrived:
                gated, arrived[g] = lax.optimization_barrier((sends[later], arrived[g]))
                arrived[later] = doc_shift(gated, 1)
        older = pending.pop(0) if len(pending) >= FINISH_LAG else None
        outs = attention_head(
            groups[g], reach_col, queries, output_gradient, keys, values, arrived.pop(g),
            dq_buf, older, grad_bufs)
        dq_buf, dk_own, dv_own, dprev = outs[:4]
        if older is not None:
            grad_bufs = tuple(outs[4:6])
        pending.append((groups[g], dk_own, dv_own, doc_shift(dprev, -1)))
    if grad_bufs is None:
        grad_bufs = (jnp.zeros((rows, kv_width), jnp.bfloat16),) * 2
    grad_keys, grad_values = grad_bufs
    for h, dk_own, dv_own, back in pending:
        grad_keys = finish_columns(grad_keys, h, dk_own, back[0])
        grad_values = finish_columns(grad_values, h, dv_own, back[1])
    return (dq_buf, grad_keys, grad_values)


def solution(mesh):
    placed = (
        P(("slab", "ctx"), None),
        P(("slab", "ctx"), None),
        P(("slab", "ctx"), None),
        P(("slab", "ctx"), None),
        P(("slab", "ctx")),
    )
    return jax.shard_map(
        on_device,
        mesh=mesh,
        in_specs=placed,
        out_specs=(P(("slab", "ctx"), None), P(("slab", "ctx"), None), P(("slab", "ctx"), None)),
        check_vma=False,
    )
```

```python
import functools

import jax
import jax.numpy as jnp
from jax import lax
from jax.experimental import pallas as pl
from jax.experimental.pallas import tpu as pltpu
from jax.sharding import PartitionSpec as P

HEAD_DIMENSION = 128
WINDOW_TOKENS = 1024
QPRE = 168
BLOCK_Q = 256
VPU_FACTOR = 5
SEND_DEPTH = 2
FINISH_LAG = 2
GROUP_HEADS = 4

NT_DIMS = (((1,), (1,)), ((), ()))
TN_DIMS = (((0,), (0,)), ((), ()))


def doc_shift(x, by):
    count = lax.axis_size("slab") * lax.axis_size("ctx")
    pairs = [(i, i + by) for i in range(count) if 0 <= i + by < count]
    return lax.ppermute(x, ("slab", "ctx"), pairs)


def attention_kernel(finish, reach_ref, q_ref, do_ref, ko_ref, vo_ref, prev_ref, q_t, do_t,
                     *refs):
    kext, vext, dkacc, dvacc = refs[-4:]
    if finish:
        dko_old, dvo_old, back_old = refs[:3]
        dq_ref, dko_ref, dvo_ref, dprev_ref, gk_ref, gv_ref = refs[-10:-4]
    else:
        dq_ref, dko_ref, dvo_ref, dprev_ref = refs[-8:-4]
    rows = q_ref.shape[0]
    d = HEAD_DIMENSION
    w = WINDOW_TOKENS
    span = BLOCK_Q + w
    scale = jnp.float32(QPRE ** (-0.5))

    kext[0:w, :] = prev_ref[0]
    kext[w:w + rows, :] = ko_ref[...]
    vext[0:w, :] = prev_ref[1]
    vext[w:w + rows, :] = vo_ref[...]
    dkacc[...] = jnp.zeros_like(dkacc)
    dvacc[...] = jnp.zeros_like(dvacc)

    offsets = (lax.broadcasted_iota(jnp.int32, (BLOCK_Q, span), 1)
               - lax.broadcasted_iota(jnp.int32, (BLOCK_Q, span), 0))

    def body(b, carry):
        r0 = pl.multiple_of(b * BLOCK_Q, BLOCK_Q)
        q = q_ref[pl.ds(r0, BLOCK_Q), :]
        do = do_ref[pl.ds(r0, BLOCK_Q), :]
        q2 = jnp.concatenate([q[:, :d], q[:, d:]], axis=0)
        do2 = jnp.concatenate([do[:, :d], do[:, d:]], axis=0)
        kw = kext[pl.ds(r0, span), :]
        vw = vext[pl.ds(r0, span), :]
        reach = reach_ref[pl.ds(r0, BLOCK_Q), :]
        visible = (offsets <= w) & (offsets > w - reach)
        s = lax.dot_general(q2, kw, NT_DIMS, preferred_element_type=jnp.float32)
        s = jnp.where(visible[None], s.reshape(2, BLOCK_Q, span), -jnp.inf).reshape(2 * BLOCK_Q, span)
        top = jnp.max(s, axis=-1, keepdims=True)
        e = jnp.exp((s - top) * scale)
        total = jnp.sum(e, axis=-1, keepdims=True)
        p = e * (1.0 / total)
        dp = lax.dot_general(do2, vw, NT_DIMS, preferred_element_type=jnp.float32)
        delta = jnp.sum(p * dp, axis=-1, keepdims=True)
        ds = (scale * p * (dp - delta)).astype(jnp.bfloat16)
        pb = p.astype(jnp.bfloat16)
        dq2 = jnp.dot(ds, kw, preferred_element_type=jnp.float32)
        dq_ref[pl.ds(r0, BLOCK_Q), :] = jnp.concatenate(
            [dq2[:BLOCK_Q], dq2[BLOCK_Q:]], axis=1).astype(dq_ref.dtype)
        q2t = jnp.concatenate([q_t[:d, pl.ds(r0, BLOCK_Q)], q_t[d:, pl.ds(r0, BLOCK_Q)]], axis=1)
        do2t = jnp.concatenate([do_t[:d, pl.ds(r0, BLOCK_Q)], do_t[d:, pl.ds(r0, BLOCK_Q)]], axis=1)
        dkacc[:, pl.ds(r0, span)] += jnp.dot(q2t, ds, preferred_element_type=jnp.float32)
        dvacc[:, pl.ds(r0, span)] += jnp.dot(do2t, pb, preferred_element_type=jnp.float32)
        return carry

    if finish:
        @pl.when(pl.program_id(0) == 0)
        def _():
            gk_ref[...] = dko_old[...].astype(gk_ref.dtype)
            gv_ref[...] = dvo_old[...].astype(gv_ref.dtype)
            gk_ref[rows - w:, :] = (dko_old[rows - w:, :]
                                    + back_old[0].astype(jnp.float32)).astype(gk_ref.dtype)
            gv_ref[rows - w:, :] = (dvo_old[rows - w:, :]
                                    + back_old[1].astype(jnp.float32)).astype(gv_ref.dtype)

    lax.fori_loop(0, rows // BLOCK_Q, body, 0)
    dko_ref[...] = dkacc[:, w:w + rows].T
    dvo_ref[...] = dvacc[:, w:w + rows].T
    dprev_ref[0] = dkacc[:, 0:w].T.astype(dprev_ref.dtype)
    dprev_ref[1] = dvacc[:, 0:w].T.astype(dprev_ref.dtype)


def attention_head(group, reach_col, queries, output_gradient, queries_t, gradient_t,
                   keys, values, previous, dq_buf, older, grad_bufs):
    rows, q_width = queries.shape
    kv_width = keys.shape[1]
    d = HEAD_DIMENSION
    w = WINDOW_TOKENS
    h0, n = group
    q_spec = pl.BlockSpec((rows, 2 * d), lambda i: (0, h0 + i))
    own_spec = pl.BlockSpec((rows, d), lambda i: (0, h0 + i))
    col_spec = pl.BlockSpec((rows, d), lambda i: (0, i))
    prev_spec = pl.BlockSpec((2, w, d), lambda i: (0, 0, i))
    any_spec = pl.BlockSpec(memory_space=pl.ANY)
    finish = older is not None
    t_spec = pl.BlockSpec((2 * d, rows), lambda i: (h0 + i, 0))
    in_specs = [pl.BlockSpec((rows, 1), lambda i: (0, 0)),
                q_spec, q_spec, own_spec, own_spec, prev_spec, t_spec, t_spec]
    operands = [reach_col, queries, output_gradient, keys, values, previous,
                queries_t, gradient_t]
    out_specs = [q_spec, col_spec, col_spec, prev_spec]
    out_shape = [
        jax.ShapeDtypeStruct((rows, q_width), jnp.bfloat16),
        jax.ShapeDtypeStruct((rows, n * d), jnp.float32),
        jax.ShapeDtypeStruct((rows, n * d), jnp.float32),
        jax.ShapeDtypeStruct((2, w, n * d), jnp.bfloat16),
    ]
    aliases = {}
    if finish:
        old0, old_n = older[0]
        whole_spec = pl.BlockSpec((rows, old_n * d), lambda i: (0, 0))
        in_specs += [whole_spec, whole_spec, pl.BlockSpec((2, w, old_n * d), lambda i: (0, 0, 0))]
        operands += list(older[1:])
        old_spec = pl.BlockSpec((rows, old_n * d), lambda i: (0, old0 // old_n))
        out_specs += [old_spec, old_spec]
        out_shape += [jax.ShapeDtypeStruct((rows, kv_width), jnp.bfloat16)] * 2
    buffers = ([] if dq_buf is None else [(dq_buf, 0)]) + (
        [] if grad_bufs is None else [(grad_bufs[0], 4), (grad_bufs[1], 5)])
    for buf, out_index in buffers:
        aliases[len(operands)] = out_index
        in_specs.append(any_spec)
        operands.append(buf)
    flops = n * VPU_FACTOR * (rows // BLOCK_Q) * 5 * 2 * (2 * BLOCK_Q) * (BLOCK_Q + w) * d
    cost = pl.CostEstimate(
        flops=flops,
        transcendentals=n * rows * 2 * (BLOCK_Q + w),
        bytes_accessed=n * 2 * (3 * rows * 2 * d + 2 * rows * d + 4 * w * d) + 4 * 2 * rows * d,
    )
    return pl.pallas_call(
        functools.partial(attention_kernel, finish),
        name="attention_backward",
        grid=(n,),
        in_specs=in_specs,
        out_specs=out_specs,
        out_shape=out_shape,
        scratch_shapes=[
            pltpu.VMEM((w + rows, d), jnp.bfloat16),
            pltpu.VMEM((w + rows, d), jnp.bfloat16),
            pltpu.VMEM((d, w + rows), jnp.float32),
            pltpu.VMEM((d, w + rows), jnp.float32),
        ],
        input_output_aliases=aliases,
        compiler_params=pltpu.CompilerParams(dimension_semantics=("arbitrary",)),
        cost_estimate=cost,
    )(*operands)


def head_groups(heads):
    size = GROUP_HEADS if heads % GROUP_HEADS == 0 else 1
    return [(h0, size) for h0 in range(0, heads, size)]


def finish_columns(grad, group, own, back):
    rows = own.shape[0]
    w = WINDOW_TOKENS
    d = HEAD_DIMENSION
    total = own.at[rows - w:].add(back.astype(jnp.float32)).astype(jnp.bfloat16)
    return lax.dynamic_update_slice(grad, total, (0, group[0] * d))


def on_device(queries, keys, values, output_gradient, reach):
    rows, q_width = queries.shape
    kv_width = keys.shape[1]
    d = HEAD_DIMENSION
    w = WINDOW_TOKENS
    groups = head_groups(kv_width // d)
    heads = len(groups)
    reach_col = reach.reshape(rows, 1)
    queries_t = queries.T
    gradient_t = output_gradient.T
    sends = [jnp.stack([keys[rows - w:, h0 * d:(h0 + n) * d], values[rows - w:, h0 * d:(h0 + n) * d]])
             for h0, n in groups]
    arrived = {0: doc_shift(sends[0], 1)}
    dq_buf = None
    grad_bufs = None
    pending = []
    for g in range(heads):
        for later in range(g + 1, min(g + SEND_DEPTH, heads - 1) + 1):
            if later not in arrived:
                gated, arrived[g] = lax.optimization_barrier((sends[later], arrived[g]))
                arrived[later] = doc_shift(gated, 1)
        older = pending.pop(0) if len(pending) >= FINISH_LAG else None
        outs = attention_head(
            groups[g], reach_col, queries, output_gradient, queries_t, gradient_t, keys, values, arrived.pop(g),
            dq_buf, older, grad_bufs)
        dq_buf, dk_own, dv_own, dprev = outs[:4]
        if older is not None:
            grad_bufs = tuple(outs[4:6])
        pending.append((groups[g], dk_own, dv_own, doc_shift(dprev, -1)))
    if grad_bufs is None:
        grad_bufs = (jnp.zeros((rows, kv_width), jnp.bfloat16),) * 2
    grad_keys, grad_values = grad_bufs
    for h, dk_own, dv_own, back in pending:
        grad_keys = finish_columns(grad_keys, h, dk_own, back[0])
        grad_values = finish_columns(grad_values, h, dv_own, back[1])
    return (dq_buf, grad_keys, grad_values)


def solution(mesh):
    placed = (
        P(("slab", "ctx"), None),
        P(("slab", "ctx"), None),
        P(("slab", "ctx"), None),
        P(("slab", "ctx"), None),
        P(("slab", "ctx")),
    )
    return jax.shard_map(
        on_device,
        mesh=mesh,
        in_specs=placed,
        out_specs=(P(("slab", "ctx"), None), P(("slab", "ctx"), None), P(("slab", "ctx"), None)),
        check_vma=False,
    )
```

```python
import functools

import jax
import jax.numpy as jnp
from jax import lax
from jax.experimental import pallas as pl
from jax.experimental.pallas import tpu as pltpu
from jax.sharding import PartitionSpec as P

HEAD_DIMENSION = 128
WINDOW_TOKENS = 1024
QPRE = 168
BLOCK_Q = 512
VPU_FACTOR = 5
SEND_DEPTH = 2
FINISH_LAG = 2
GROUP_HEADS = 4

NT_DIMS = (((1,), (1,)), ((), ()))
TN_DIMS = (((0,), (0,)), ((), ()))


def doc_shift(x, by):
    count = lax.axis_size("slab") * lax.axis_size("ctx")
    pairs = [(i, i + by) for i in range(count) if 0 <= i + by < count]
    return lax.ppermute(x, ("slab", "ctx"), pairs)


def attention_kernel(finish, reach_ref, q_ref, do_ref, ko_ref, vo_ref, prev_ref, q_t, do_t,
                     *refs):
    kext, vext, dkacc, dvacc = refs[-4:]
    if finish:
        dko_old, dvo_old, back_old = refs[:3]
        dq_ref, dko_ref, dvo_ref, dprev_ref, gk_ref, gv_ref = refs[-10:-4]
    else:
        dq_ref, dko_ref, dvo_ref, dprev_ref = refs[-8:-4]
    rows = q_ref.shape[0]
    d = HEAD_DIMENSION
    w = WINDOW_TOKENS
    span = BLOCK_Q + w
    scale = jnp.float32(QPRE ** (-0.5))

    kext[0:w, :] = prev_ref[0]
    kext[w:w + rows, :] = ko_ref[...]
    vext[0:w, :] = prev_ref[1]
    vext[w:w + rows, :] = vo_ref[...]
    dkacc[...] = jnp.zeros_like(dkacc)
    dvacc[...] = jnp.zeros_like(dvacc)

    offsets = (lax.broadcasted_iota(jnp.int32, (BLOCK_Q, span), 1)
               - lax.broadcasted_iota(jnp.int32, (BLOCK_Q, span), 0))

    def body(b, carry):
        r0 = pl.multiple_of(b * BLOCK_Q, BLOCK_Q)
        q = q_ref[pl.ds(r0, BLOCK_Q), :]
        do = do_ref[pl.ds(r0, BLOCK_Q), :]
        q2 = jnp.concatenate([q[:, :d], q[:, d:]], axis=0)
        do2 = jnp.concatenate([do[:, :d], do[:, d:]], axis=0)
        kw = kext[pl.ds(r0, span), :]
        vw = vext[pl.ds(r0, span), :]
        reach = reach_ref[pl.ds(r0, BLOCK_Q), :]
        visible = (offsets <= w) & (offsets > w - reach)
        s = lax.dot_general(q2, kw, NT_DIMS, preferred_element_type=jnp.float32)
        s = jnp.where(visible[None], s.reshape(2, BLOCK_Q, span), -jnp.inf).reshape(2 * BLOCK_Q, span)
        top = jnp.max(s, axis=-1, keepdims=True)
        e = jnp.exp((s - top) * scale)
        total = jnp.sum(e, axis=-1, keepdims=True)
        p = e * (1.0 / total)
        dp = lax.dot_general(do2, vw, NT_DIMS, preferred_element_type=jnp.float32)
        delta = jnp.sum(p * dp, axis=-1, keepdims=True)
        ds = (scale * p * (dp - delta)).astype(jnp.bfloat16)
        pb = p.astype(jnp.bfloat16)
        dq2 = jnp.dot(ds, kw, preferred_element_type=jnp.float32)
        dq_ref[pl.ds(r0, BLOCK_Q), :] = jnp.concatenate(
            [dq2[:BLOCK_Q], dq2[BLOCK_Q:]], axis=1).astype(dq_ref.dtype)
        q2t = jnp.concatenate([q_t[:d, pl.ds(r0, BLOCK_Q)], q_t[d:, pl.ds(r0, BLOCK_Q)]], axis=1)
        do2t = jnp.concatenate([do_t[:d, pl.ds(r0, BLOCK_Q)], do_t[d:, pl.ds(r0, BLOCK_Q)]], axis=1)
        dkacc[:, pl.ds(r0, span)] += jnp.dot(q2t, ds, preferred_element_type=jnp.float32)
        dvacc[:, pl.ds(r0, span)] += jnp.dot(do2t, pb, preferred_element_type=jnp.float32)
        return carry

    if finish:
        @pl.when(pl.program_id(0) == 0)
        def _():
            gk_ref[...] = dko_old[...].astype(gk_ref.dtype)
            gv_ref[...] = dvo_old[...].astype(gv_ref.dtype)
            gk_ref[rows - w:, :] = (dko_old[rows - w:, :]
                                    + back_old[0].astype(jnp.float32)).astype(gk_ref.dtype)
            gv_ref[rows - w:, :] = (dvo_old[rows - w:, :]
                                    + back_old[1].astype(jnp.float32)).astype(gv_ref.dtype)

    lax.fori_loop(0, rows // BLOCK_Q, body, 0)
    dko_ref[...] = dkacc[:, w:w + rows].T
    dvo_ref[...] = dvacc[:, w:w + rows].T
    dprev_ref[0] = dkacc[:, 0:w].T.astype(dprev_ref.dtype)
    dprev_ref[1] = dvacc[:, 0:w].T.astype(dprev_ref.dtype)


def attention_head(group, reach_col, queries, output_gradient, queries_t, gradient_t,
                   keys, values, previous, dq_buf, older, grad_bufs):
    rows, q_width = queries.shape
    kv_width = keys.shape[1]
    d = HEAD_DIMENSION
    w = WINDOW_TOKENS
    h0, n = group
    q_spec = pl.BlockSpec((rows, 2 * d), lambda i: (0, h0 + i))
    own_spec = pl.BlockSpec((rows, d), lambda i: (0, h0 + i))
    col_spec = pl.BlockSpec((rows, d), lambda i: (0, i))
    prev_spec = pl.BlockSpec((2, w, d), lambda i: (0, 0, i))
    any_spec = pl.BlockSpec(memory_space=pl.ANY)
    finish = older is not None
    t_spec = pl.BlockSpec((2 * d, rows), lambda i: (h0 + i, 0))
    in_specs = [pl.BlockSpec((rows, 1), lambda i: (0, 0)),
                q_spec, q_spec, own_spec, own_spec, prev_spec, t_spec, t_spec]
    operands = [reach_col, queries, output_gradient, keys, values, previous,
                queries_t, gradient_t]
    out_specs = [q_spec, col_spec, col_spec, prev_spec]
    out_shape = [
        jax.ShapeDtypeStruct((rows, q_width), jnp.bfloat16),
        jax.ShapeDtypeStruct((rows, n * d), jnp.float32),
        jax.ShapeDtypeStruct((rows, n * d), jnp.float32),
        jax.ShapeDtypeStruct((2, w, n * d), jnp.bfloat16),
    ]
    aliases = {}
    if finish:
        old0, old_n = older[0]
        whole_spec = pl.BlockSpec((rows, old_n * d), lambda i: (0, 0))
        in_specs += [whole_spec, whole_spec, pl.BlockSpec((2, w, old_n * d), lambda i: (0, 0, 0))]
        operands += list(older[1:])
        old_spec = pl.BlockSpec((rows, old_n * d), lambda i: (0, old0 // old_n))
        out_specs += [old_spec, old_spec]
        out_shape += [jax.ShapeDtypeStruct((rows, kv_width), jnp.bfloat16)] * 2
    buffers = ([] if dq_buf is None else [(dq_buf, 0)]) + (
        [] if grad_bufs is None else [(grad_bufs[0], 4), (grad_bufs[1], 5)])
    for buf, out_index in buffers:
        aliases[len(operands)] = out_index
        in_specs.append(any_spec)
        operands.append(buf)
    flops = n * VPU_FACTOR * (rows // BLOCK_Q) * 5 * 2 * (2 * BLOCK_Q) * (BLOCK_Q + w) * d
    cost = pl.CostEstimate(
        flops=flops,
        transcendentals=n * rows * 2 * (BLOCK_Q + w),
        bytes_accessed=n * 2 * (3 * rows * 2 * d + 2 * rows * d + 4 * w * d) + 4 * 2 * rows * d,
    )
    return pl.pallas_call(
        functools.partial(attention_kernel, finish),
        name="attention_backward",
        grid=(n,),
        in_specs=in_specs,
        out_specs=out_specs,
        out_shape=out_shape,
        scratch_shapes=[
            pltpu.VMEM((w + rows, d), jnp.bfloat16),
            pltpu.VMEM((w + rows, d), jnp.bfloat16),
            pltpu.VMEM((d, w + rows), jnp.float32),
            pltpu.VMEM((d, w + rows), jnp.float32),
        ],
        input_output_aliases=aliases,
        compiler_params=pltpu.CompilerParams(dimension_semantics=("arbitrary",)),
        cost_estimate=cost,
    )(*operands)


def head_groups(heads):
    size = GROUP_HEADS if heads % GROUP_HEADS == 0 else 1
    return [(h0, size) for h0 in range(0, heads, size)]


def finish_columns(grad, group, own, back):
    rows = own.shape[0]
    w = WINDOW_TOKENS
    d = HEAD_DIMENSION
    total = own.at[rows - w:].add(back.astype(jnp.float32)).astype(jnp.bfloat16)
    return lax.dynamic_update_slice(grad, total, (0, group[0] * d))


def on_device(queries, keys, values, output_gradient, reach):
    rows, q_width = queries.shape
    kv_width = keys.shape[1]
    d = HEAD_DIMENSION
    w = WINDOW_TOKENS
    groups = head_groups(kv_width // d)
    heads = len(groups)
    reach_col = reach.reshape(rows, 1)
    queries_t = queries.T
    gradient_t = output_gradient.T
    sends = [jnp.stack([keys[rows - w:, h0 * d:(h0 + n) * d], values[rows - w:, h0 * d:(h0 + n) * d]])
             for h0, n in groups]
    arrived = {0: doc_shift(sends[0], 1)}
    dq_buf = None
    grad_bufs = None
    pending = []
    for g in range(heads):
        for later in range(g + 1, min(g + SEND_DEPTH, heads - 1) + 1):
            if later not in arrived:
                gated, arrived[g] = lax.optimization_barrier((sends[later], arrived[g]))
                arrived[later] = doc_shift(gated, 1)
        older = pending.pop(0) if len(pending) >= FINISH_LAG else None
        outs = attention_head(
            groups[g], reach_col, queries, output_gradient, queries_t, gradient_t, keys, values, arrived.pop(g),
            dq_buf, older, grad_bufs)
        dq_buf, dk_own, dv_own, dprev = outs[:4]
        if older is not None:
            grad_bufs = tuple(outs[4:6])
        pending.append((groups[g], dk_own, dv_own, doc_shift(dprev, -1)))
    if grad_bufs is None:
        grad_bufs = (jnp.zeros((rows, kv_width), jnp.bfloat16),) * 2
    grad_keys, grad_values = grad_bufs
    for h, dk_own, dv_own, back in pending:
        grad_keys = finish_columns(grad_keys, h, dk_own, back[0])
        grad_values = finish_columns(grad_values, h, dv_own, back[1])
    return (dq_buf, grad_keys, grad_values)


def solution(mesh):
    placed = (
        P(("slab", "ctx"), None),
        P(("slab", "ctx"), None),
        P(("slab", "ctx"), None),
        P(("slab", "ctx"), None),
        P(("slab", "ctx")),
    )
    return jax.shard_map(
        on_device,
        mesh=mesh,
        in_specs=placed,
        out_specs=(P(("slab", "ctx"), None), P(("slab", "ctx"), None), P(("slab", "ctx"), None)),
        check_vma=False,
    )
```

```python
import functools

import jax
import jax.numpy as jnp
from jax import lax
from jax.experimental import pallas as pl
from jax.experimental.pallas import tpu as pltpu
from jax.sharding import PartitionSpec as P

HEAD_DIMENSION = 128
WINDOW_TOKENS = 1024
QPRE = 168
BLOCK_Q = 256
VPU_FACTOR = 5
SEND_DEPTH = 2
FINISH_LAG = 2
GROUP_HEADS = 4

NT_DIMS = (((1,), (1,)), ((), ()))
TN_DIMS = (((0,), (0,)), ((), ()))


def doc_shift(x, by):
    count = lax.axis_size("slab") * lax.axis_size("ctx")
    pairs = [(i, i + by) for i in range(count) if 0 <= i + by < count]
    return lax.ppermute(x, ("slab", "ctx"), pairs)


def attention_kernel(finish, reach_ref, q_ref, do_ref, ko_ref, vo_ref, kp_ref, vp_ref, q_t, do_t,
                     *refs):
    kext, vext, dkacc, dvacc = refs[-4:]
    if finish:
        dko_old, dvo_old, back_old = refs[:3]
        dq_ref, dko_ref, dvo_ref, dprev_ref, gk_ref, gv_ref = refs[-10:-4]
    else:
        dq_ref, dko_ref, dvo_ref, dprev_ref = refs[-8:-4]
    rows = q_ref.shape[0]
    d = HEAD_DIMENSION
    w = WINDOW_TOKENS
    span = BLOCK_Q + w
    scale = jnp.float32(QPRE ** (-0.5))

    kext[0:w, :] = kp_ref[...]
    kext[w:w + rows, :] = ko_ref[...]
    vext[0:w, :] = vp_ref[...]
    vext[w:w + rows, :] = vo_ref[...]
    dkacc[...] = jnp.zeros_like(dkacc)
    dvacc[...] = jnp.zeros_like(dvacc)

    offsets = (lax.broadcasted_iota(jnp.int32, (BLOCK_Q, span), 1)
               - lax.broadcasted_iota(jnp.int32, (BLOCK_Q, span), 0))

    def body(b, carry):
        r0 = pl.multiple_of(b * BLOCK_Q, BLOCK_Q)
        q = q_ref[pl.ds(r0, BLOCK_Q), :]
        do = do_ref[pl.ds(r0, BLOCK_Q), :]
        q2 = jnp.concatenate([q[:, :d], q[:, d:]], axis=0)
        do2 = jnp.concatenate([do[:, :d], do[:, d:]], axis=0)
        kw = kext[pl.ds(r0, span), :]
        vw = vext[pl.ds(r0, span), :]
        reach = reach_ref[pl.ds(r0, BLOCK_Q), :]
        visible = (offsets <= w) & (offsets > w - reach)
        s = lax.dot_general(q2, kw, NT_DIMS, preferred_element_type=jnp.float32)
        s = jnp.where(visible[None], s.reshape(2, BLOCK_Q, span), -jnp.inf).reshape(2 * BLOCK_Q, span)
        top = jnp.max(s, axis=-1, keepdims=True)
        e = jnp.exp((s - top) * scale)
        total = jnp.sum(e, axis=-1, keepdims=True)
        p = e * (1.0 / total)
        dp = lax.dot_general(do2, vw, NT_DIMS, preferred_element_type=jnp.float32)
        delta = jnp.sum(p * dp, axis=-1, keepdims=True)
        ds = (scale * p * (dp - delta)).astype(jnp.bfloat16)
        pb = p.astype(jnp.bfloat16)
        dq2 = jnp.dot(ds, kw, preferred_element_type=jnp.float32)
        dq_ref[pl.ds(r0, BLOCK_Q), :] = jnp.concatenate(
            [dq2[:BLOCK_Q], dq2[BLOCK_Q:]], axis=1).astype(dq_ref.dtype)
        q2t = jnp.concatenate([q_t[:d, pl.ds(r0, BLOCK_Q)], q_t[d:, pl.ds(r0, BLOCK_Q)]], axis=1)
        do2t = jnp.concatenate([do_t[:d, pl.ds(r0, BLOCK_Q)], do_t[d:, pl.ds(r0, BLOCK_Q)]], axis=1)
        dkacc[:, pl.ds(r0, span)] += jnp.dot(q2t, ds, preferred_element_type=jnp.float32)
        dvacc[:, pl.ds(r0, span)] += jnp.dot(do2t, pb, preferred_element_type=jnp.float32)
        return carry

    if finish:
        @pl.when(pl.program_id(0) == 0)
        def _():
            gk_ref[...] = dko_old[...].astype(gk_ref.dtype)
            gv_ref[...] = dvo_old[...].astype(gv_ref.dtype)
            gk_ref[rows - w:, :] = (dko_old[rows - w:, :]
                                    + back_old[0].astype(jnp.float32)).astype(gk_ref.dtype)
            gv_ref[rows - w:, :] = (dvo_old[rows - w:, :]
                                    + back_old[1].astype(jnp.float32)).astype(gv_ref.dtype)

    lax.fori_loop(0, rows // BLOCK_Q, body, 0)
    dko_ref[...] = dkacc[:, w:w + rows].T
    dvo_ref[...] = dvacc[:, w:w + rows].T
    dprev_ref[0] = dkacc[:, 0:w].T.astype(dprev_ref.dtype)
    dprev_ref[1] = dvacc[:, 0:w].T.astype(dprev_ref.dtype)


def attention_head(group, reach_col, queries, output_gradient, queries_t, gradient_t,
                   keys, values, previous, dq_buf, older, grad_bufs):
    rows, q_width = queries.shape
    kv_width = keys.shape[1]
    d = HEAD_DIMENSION
    w = WINDOW_TOKENS
    h0, n = group
    q_spec = pl.BlockSpec((rows, 2 * d), lambda i: (0, h0 + i))
    own_spec = pl.BlockSpec((rows, d), lambda i: (0, h0 + i))
    col_spec = pl.BlockSpec((rows, d), lambda i: (0, i))
    prev_spec = pl.BlockSpec((2, w, d), lambda i: (0, 0, i))
    tail_spec = pl.BlockSpec((w, d), lambda i: (0, i))
    any_spec = pl.BlockSpec(memory_space=pl.ANY)
    finish = older is not None
    t_spec = pl.BlockSpec((2 * d, rows), lambda i: (h0 + i, 0))
    in_specs = [pl.BlockSpec((rows, 1), lambda i: (0, 0)),
                q_spec, q_spec, own_spec, own_spec, tail_spec, tail_spec, t_spec, t_spec]
    operands = [reach_col, queries, output_gradient, keys, values, previous[0], previous[1],
                queries_t, gradient_t]
    out_specs = [q_spec, col_spec, col_spec, prev_spec]
    out_shape = [
        jax.ShapeDtypeStruct((rows, q_width), jnp.bfloat16),
        jax.ShapeDtypeStruct((rows, n * d), jnp.float32),
        jax.ShapeDtypeStruct((rows, n * d), jnp.float32),
        jax.ShapeDtypeStruct((2, w, n * d), jnp.bfloat16),
    ]
    aliases = {}
    if finish:
        old0, old_n = older[0]
        whole_spec = pl.BlockSpec((rows, old_n * d), lambda i: (0, 0))
        in_specs += [whole_spec, whole_spec, pl.BlockSpec((2, w, old_n * d), lambda i: (0, 0, 0))]
        operands += list(older[1:])
        old_spec = pl.BlockSpec((rows, old_n * d), lambda i: (0, old0 // old_n))
        out_specs += [old_spec, old_spec]
        out_shape += [jax.ShapeDtypeStruct((rows, kv_width), jnp.bfloat16)] * 2
    buffers = ([] if dq_buf is None else [(dq_buf, 0)]) + (
        [] if grad_bufs is None else [(grad_bufs[0], 4), (grad_bufs[1], 5)])
    for buf, out_index in buffers:
        aliases[len(operands)] = out_index
        in_specs.append(any_spec)
        operands.append(buf)
    flops = n * VPU_FACTOR * (rows // BLOCK_Q) * 5 * 2 * (2 * BLOCK_Q) * (BLOCK_Q + w) * d
    cost = pl.CostEstimate(
        flops=flops,
        transcendentals=n * rows * 2 * (BLOCK_Q + w),
        bytes_accessed=n * 2 * (3 * rows * 2 * d + 2 * rows * d + 4 * w * d) + 4 * 2 * rows * d,
    )
    return pl.pallas_call(
        functools.partial(attention_kernel, finish),
        name="attention_backward",
        grid=(n,),
        in_specs=in_specs,
        out_specs=out_specs,
        out_shape=out_shape,
        scratch_shapes=[
            pltpu.VMEM((w + rows, d), jnp.bfloat16),
            pltpu.VMEM((w + rows, d), jnp.bfloat16),
            pltpu.VMEM((d, w + rows), jnp.float32),
            pltpu.VMEM((d, w + rows), jnp.float32),
        ],
        input_output_aliases=aliases,
        compiler_params=pltpu.CompilerParams(dimension_semantics=("arbitrary",)),
        cost_estimate=cost,
    )(*operands)


def head_groups(heads):
    size = GROUP_HEADS if heads % GROUP_HEADS == 0 else 1
    return [(h0, size) for h0 in range(0, heads, size)]


def finish_columns(grad, group, own, back):
    rows = own.shape[0]
    w = WINDOW_TOKENS
    d = HEAD_DIMENSION
    total = own.at[rows - w:].add(back.astype(jnp.float32)).astype(jnp.bfloat16)
    return lax.dynamic_update_slice(grad, total, (0, group[0] * d))


def on_device(queries, keys, values, output_gradient, reach):
    rows, q_width = queries.shape
    kv_width = keys.shape[1]
    d = HEAD_DIMENSION
    w = WINDOW_TOKENS
    groups = head_groups(kv_width // d)
    heads = len(groups)
    reach_col = reach.reshape(rows, 1)
    queries_t = queries.T
    gradient_t = output_gradient.T
    sends = [(keys[rows - w:, h0 * d:(h0 + n) * d], values[rows - w:, h0 * d:(h0 + n) * d])
             for h0, n in groups]
    arrived = {0: doc_shift(sends[0], 1)}
    dq_buf = None
    grad_bufs = None
    pending = []
    for g in range(heads):
        for later in range(g + 1, min(g + SEND_DEPTH, heads - 1) + 1):
            if later not in arrived:
                gated, arrived[g] = lax.optimization_barrier((sends[later], arrived[g]))
                arrived[later] = doc_shift(gated, 1)
        older = pending.pop(0) if len(pending) >= FINISH_LAG else None
        outs = attention_head(
            groups[g], reach_col, queries, output_gradient, queries_t, gradient_t, keys, values, arrived.pop(g),
            dq_buf, older, grad_bufs)
        dq_buf, dk_own, dv_own, dprev = outs[:4]
        if older is not None:
            grad_bufs = tuple(outs[4:6])
        pending.append((groups[g], dk_own, dv_own, doc_shift(dprev, -1)))
    if grad_bufs is None:
        grad_bufs = (jnp.zeros((rows, kv_width), jnp.bfloat16),) * 2
    grad_keys, grad_values = grad_bufs
    for h, dk_own, dv_own, back in pending:
        grad_keys = finish_columns(grad_keys, h, dk_own, back[0])
        grad_values = finish_columns(grad_values, h, dv_own, back[1])
    return (dq_buf, grad_keys, grad_values)


def solution(mesh):
    placed = (
        P(("slab", "ctx"), None),
        P(("slab", "ctx"), None),
        P(("slab", "ctx"), None),
        P(("slab", "ctx"), None),
        P(("slab", "ctx")),
    )
    return jax.shard_map(
        on_device,
        mesh=mesh,
        in_specs=placed,
        out_specs=(P(("slab", "ctx"), None), P(("slab", "ctx"), None), P(("slab", "ctx"), None)),
        check_vma=False,
    )
```

```python
import functools

import jax
import jax.numpy as jnp
from jax import lax
from jax.experimental import pallas as pl
from jax.experimental.pallas import tpu as pltpu
from jax.sharding import PartitionSpec as P

HEAD_DIMENSION = 128
WINDOW_TOKENS = 1024
QPRE = 168
LOG2_E = 1.4426950408889634
BLOCK_Q = 256
VPU_FACTOR = 5
SEND_DEPTH = 2
FINISH_LAG = 2
GROUP_HEADS = 4

NT_DIMS = (((1,), (1,)), ((), ()))
TN_DIMS = (((0,), (0,)), ((), ()))


def doc_shift(x, by):
    count = lax.axis_size("slab") * lax.axis_size("ctx")
    pairs = [(i, i + by) for i in range(count) if 0 <= i + by < count]
    return lax.ppermute(x, ("slab", "ctx"), pairs)


def attention_kernel(finish, reach_ref, q_ref, do_ref, ko_ref, vo_ref, prev_ref, q_t, do_t,
                     *refs):
    kext, vext, dkacc, dvacc = refs[-4:]
    if finish:
        dko_old, dvo_old, back_old = refs[:3]
        dq_ref, dko_ref, dvo_ref, dprev_ref, gk_ref, gv_ref = refs[-10:-4]
    else:
        dq_ref, dko_ref, dvo_ref, dprev_ref = refs[-8:-4]
    rows = q_ref.shape[0]
    d = HEAD_DIMENSION
    w = WINDOW_TOKENS
    span = BLOCK_Q + w
    scale = jnp.float32(QPRE ** (-0.5))

    kext[0:w, :] = prev_ref[0]
    kext[w:w + rows, :] = ko_ref[...]
    vext[0:w, :] = prev_ref[1]
    vext[w:w + rows, :] = vo_ref[...]
    dkacc[...] = jnp.zeros_like(dkacc)
    dvacc[...] = jnp.zeros_like(dvacc)

    offsets = (lax.broadcasted_iota(jnp.int32, (BLOCK_Q, span), 1)
               - lax.broadcasted_iota(jnp.int32, (BLOCK_Q, span), 0))

    def body(b, carry):
        r0 = pl.multiple_of(b * BLOCK_Q, BLOCK_Q)
        q = q_ref[pl.ds(r0, BLOCK_Q), :]
        do = do_ref[pl.ds(r0, BLOCK_Q), :]
        q2 = jnp.concatenate([q[:, :d], q[:, d:]], axis=0)
        do2 = jnp.concatenate([do[:, :d], do[:, d:]], axis=0)
        kw = kext[pl.ds(r0, span), :]
        vw = vext[pl.ds(r0, span), :]
        reach = reach_ref[pl.ds(r0, BLOCK_Q), :]
        visible = (offsets <= w) & (offsets > w - reach)
        s = lax.dot_general(q2, kw, NT_DIMS, preferred_element_type=jnp.float32)
        s = jnp.where(visible[None], s.reshape(2, BLOCK_Q, span), -jnp.inf).reshape(2 * BLOCK_Q, span)
        top = jnp.max(s, axis=-1, keepdims=True)
        e = jnp.exp2((s - top) * (scale * LOG2_E))
        total = jnp.sum(e, axis=-1, keepdims=True)
        p = e * (1.0 / total)
        dp = lax.dot_general(do2, vw, NT_DIMS, preferred_element_type=jnp.float32)
        delta = jnp.sum(p * dp, axis=-1, keepdims=True)
        ds = (scale * p * (dp - delta)).astype(jnp.bfloat16)
        pb = p.astype(jnp.bfloat16)
        dq2 = jnp.dot(ds, kw, preferred_element_type=jnp.float32)
        dq_ref[pl.ds(r0, BLOCK_Q), :] = jnp.concatenate(
            [dq2[:BLOCK_Q], dq2[BLOCK_Q:]], axis=1).astype(dq_ref.dtype)
        q2t = jnp.concatenate([q_t[:d, pl.ds(r0, BLOCK_Q)], q_t[d:, pl.ds(r0, BLOCK_Q)]], axis=1)
        do2t = jnp.concatenate([do_t[:d, pl.ds(r0, BLOCK_Q)], do_t[d:, pl.ds(r0, BLOCK_Q)]], axis=1)
        dkacc[:, pl.ds(r0, span)] += jnp.dot(q2t, ds, preferred_element_type=jnp.float32)
        dvacc[:, pl.ds(r0, span)] += jnp.dot(do2t, pb, preferred_element_type=jnp.float32)
        return carry

    if finish:
        @pl.when(pl.program_id(0) == 0)
        def _():
            gk_ref[...] = dko_old[...].astype(gk_ref.dtype)
            gv_ref[...] = dvo_old[...].astype(gv_ref.dtype)
            gk_ref[rows - w:, :] = (dko_old[rows - w:, :]
                                    + back_old[0].astype(jnp.float32)).astype(gk_ref.dtype)
            gv_ref[rows - w:, :] = (dvo_old[rows - w:, :]
                                    + back_old[1].astype(jnp.float32)).astype(gv_ref.dtype)

    lax.fori_loop(0, rows // BLOCK_Q, body, 0)
    dko_ref[...] = dkacc[:, w:w + rows].T
    dvo_ref[...] = dvacc[:, w:w + rows].T
    dprev_ref[0] = dkacc[:, 0:w].T.astype(dprev_ref.dtype)
    dprev_ref[1] = dvacc[:, 0:w].T.astype(dprev_ref.dtype)


def attention_head(group, reach_col, queries, output_gradient, queries_t, gradient_t,
                   keys, values, previous, dq_buf, older, grad_bufs):
    rows, q_width = queries.shape
    kv_width = keys.shape[1]
    d = HEAD_DIMENSION
    w = WINDOW_TOKENS
    h0, n = group
    q_spec = pl.BlockSpec((rows, 2 * d), lambda i: (0, h0 + i))
    own_spec = pl.BlockSpec((rows, d), lambda i: (0, h0 + i))
    col_spec = pl.BlockSpec((rows, d), lambda i: (0, i))
    prev_spec = pl.BlockSpec((2, w, d), lambda i: (0, 0, i))
    any_spec = pl.BlockSpec(memory_space=pl.ANY)
    finish = older is not None
    t_spec = pl.BlockSpec((2 * d, rows), lambda i: (h0 + i, 0))
    in_specs = [pl.BlockSpec((rows, 1), lambda i: (0, 0)),
                q_spec, q_spec, own_spec, own_spec, prev_spec, t_spec, t_spec]
    operands = [reach_col, queries, output_gradient, keys, values, previous,
                queries_t, gradient_t]
    out_specs = [q_spec, col_spec, col_spec, prev_spec]
    out_shape = [
        jax.ShapeDtypeStruct((rows, q_width), jnp.bfloat16),
        jax.ShapeDtypeStruct((rows, n * d), jnp.float32),
        jax.ShapeDtypeStruct((rows, n * d), jnp.float32),
        jax.ShapeDtypeStruct((2, w, n * d), jnp.bfloat16),
    ]
    aliases = {}
    if finish:
        old0, old_n = older[0]
        whole_spec = pl.BlockSpec((rows, old_n * d), lambda i: (0, 0))
        in_specs += [whole_spec, whole_spec, pl.BlockSpec((2, w, old_n * d), lambda i: (0, 0, 0))]
        operands += list(older[1:])
        old_spec = pl.BlockSpec((rows, old_n * d), lambda i: (0, old0 // old_n))
        out_specs += [old_spec, old_spec]
        out_shape += [jax.ShapeDtypeStruct((rows, kv_width), jnp.bfloat16)] * 2
    buffers = ([] if dq_buf is None else [(dq_buf, 0)]) + (
        [] if grad_bufs is None else [(grad_bufs[0], 4), (grad_bufs[1], 5)])
    for buf, out_index in buffers:
        aliases[len(operands)] = out_index
        in_specs.append(any_spec)
        operands.append(buf)
    flops = n * VPU_FACTOR * (rows // BLOCK_Q) * 5 * 2 * (2 * BLOCK_Q) * (BLOCK_Q + w) * d
    cost = pl.CostEstimate(
        flops=flops,
        transcendentals=n * rows * 2 * (BLOCK_Q + w),
        bytes_accessed=n * 2 * (3 * rows * 2 * d + 2 * rows * d + 4 * w * d) + 4 * 2 * rows * d,
    )
    return pl.pallas_call(
        functools.partial(attention_kernel, finish),
        name="attention_backward",
        grid=(n,),
        in_specs=in_specs,
        out_specs=out_specs,
        out_shape=out_shape,
        scratch_shapes=[
            pltpu.VMEM((w + rows, d), jnp.bfloat16),
            pltpu.VMEM((w + rows, d), jnp.bfloat16),
            pltpu.VMEM((d, w + rows), jnp.float32),
            pltpu.VMEM((d, w + rows), jnp.float32),
        ],
        input_output_aliases=aliases,
        compiler_params=pltpu.CompilerParams(dimension_semantics=("arbitrary",)),
        cost_estimate=cost,
    )(*operands)


def head_groups(heads):
    size = GROUP_HEADS if heads % GROUP_HEADS == 0 else 1
    return [(h0, size) for h0 in range(0, heads, size)]


def finish_columns(grad, group, own, back):
    rows = own.shape[0]
    w = WINDOW_TOKENS
    d = HEAD_DIMENSION
    total = own.at[rows - w:].add(back.astype(jnp.float32)).astype(jnp.bfloat16)
    return lax.dynamic_update_slice(grad, total, (0, group[0] * d))


def on_device(queries, keys, values, output_gradient, reach):
    rows, q_width = queries.shape
    kv_width = keys.shape[1]
    d = HEAD_DIMENSION
    w = WINDOW_TOKENS
    groups = head_groups(kv_width // d)
    heads = len(groups)
    reach_col = reach.reshape(rows, 1)
    queries_t = queries.T
    gradient_t = output_gradient.T
    sends = [jnp.stack([keys[rows - w:, h0 * d:(h0 + n) * d], values[rows - w:, h0 * d:(h0 + n) * d]])
             for h0, n in groups]
    arrived = {0: doc_shift(sends[0], 1)}
    dq_buf = None
    grad_bufs = None
    pending = []
    for g in range(heads):
        for later in range(g + 1, min(g + SEND_DEPTH, heads - 1) + 1):
            if later not in arrived:
                gated, arrived[g] = lax.optimization_barrier((sends[later], arrived[g]))
                arrived[later] = doc_shift(gated, 1)
        older = pending.pop(0) if len(pending) >= FINISH_LAG else None
        outs = attention_head(
            groups[g], reach_col, queries, output_gradient, queries_t, gradient_t, keys, values, arrived.pop(g),
            dq_buf, older, grad_bufs)
        dq_buf, dk_own, dv_own, dprev = outs[:4]
        if older is not None:
            grad_bufs = tuple(outs[4:6])
        pending.append((groups[g], dk_own, dv_own, doc_shift(dprev, -1)))
    if grad_bufs is None:
        grad_bufs = (jnp.zeros((rows, kv_width), jnp.bfloat16),) * 2
    grad_keys, grad_values = grad_bufs
    for h, dk_own, dv_own, back in pending:
        grad_keys = finish_columns(grad_keys, h, dk_own, back[0])
        grad_values = finish_columns(grad_values, h, dv_own, back[1])
    return (dq_buf, grad_keys, grad_values)


def solution(mesh):
    placed = (
        P(("slab", "ctx"), None),
        P(("slab", "ctx"), None),
        P(("slab", "ctx"), None),
        P(("slab", "ctx"), None),
        P(("slab", "ctx")),
    )
    return jax.shard_map(
        on_device,
        mesh=mesh,
        in_specs=placed,
        out_specs=(P(("slab", "ctx"), None), P(("slab", "ctx"), None), P(("slab", "ctx"), None)),
        check_vma=False,
    )
```

```python
import functools

import jax
import jax.numpy as jnp
from jax import lax
from jax.experimental import pallas as pl
from jax.experimental.pallas import tpu as pltpu
from jax.sharding import PartitionSpec as P

HEAD_DIMENSION = 128
WINDOW_TOKENS = 1024
QPRE = 168
LOG2_E = 1.4426950408889634
BLOCK_Q = 256
VPU_FACTOR = 5
SEND_DEPTH = 2
FINISH_LAG = 2
GROUP_HEADS = 4

NT_DIMS = (((1,), (1,)), ((), ()))
TN_DIMS = (((0,), (0,)), ((), ()))


def doc_shift(x, by):
    count = lax.axis_size("slab") * lax.axis_size("ctx")
    pairs = [(i, i + by) for i in range(count) if 0 <= i + by < count]
    return lax.ppermute(x, ("slab", "ctx"), pairs)


def attention_kernel(finish, reach_ref, q_ref, do_ref, ko_ref, vo_ref, prev_ref, q_t, do_t,
                     *refs):
    kext, vext, dkacc, dvacc = refs[-4:]
    if finish:
        dko_old, dvo_old, back_old = refs[:3]
        dq_ref, dko_ref, dvo_ref, dprev_ref, gk_ref, gv_ref = refs[-10:-4]
    else:
        dq_ref, dko_ref, dvo_ref, dprev_ref = refs[-8:-4]
    rows = q_ref.shape[0]
    d = HEAD_DIMENSION
    w = WINDOW_TOKENS
    span = BLOCK_Q + w
    scale = jnp.float32(QPRE ** (-0.5))

    kext[0:w, :] = prev_ref[0]
    kext[w:w + rows, :] = ko_ref[...]
    vext[0:w, :] = prev_ref[1]
    vext[w:w + rows, :] = vo_ref[...]
    dkacc[...] = jnp.zeros_like(dkacc)
    dvacc[...] = jnp.zeros_like(dvacc)

    offsets = (lax.broadcasted_iota(jnp.int32, (BLOCK_Q, span), 1)
               - lax.broadcasted_iota(jnp.int32, (BLOCK_Q, span), 0))
    causal = offsets <= w

    def body(b, carry):
        r0 = pl.multiple_of(b * BLOCK_Q, BLOCK_Q)
        q = q_ref[pl.ds(r0, BLOCK_Q), :]
        do = do_ref[pl.ds(r0, BLOCK_Q), :]
        q2 = jnp.concatenate([q[:, :d], q[:, d:]], axis=0)
        do2 = jnp.concatenate([do[:, :d], do[:, d:]], axis=0)
        kw = kext[pl.ds(r0, span), :]
        vw = vext[pl.ds(r0, span), :]
        reach = reach_ref[pl.ds(r0, BLOCK_Q), :]
        visible = causal & (offsets > w - reach)
        s = lax.dot_general(q2, kw, NT_DIMS, preferred_element_type=jnp.float32)
        s = jnp.where(visible[None], s.reshape(2, BLOCK_Q, span), -jnp.inf).reshape(2 * BLOCK_Q, span)
        top = jnp.max(s, axis=-1, keepdims=True)
        e = jnp.exp2((s - top) * (scale * LOG2_E))
        total = jnp.sum(e, axis=-1, keepdims=True)
        p = e * (1.0 / total)
        dp = lax.dot_general(do2, vw, NT_DIMS, preferred_element_type=jnp.float32)
        delta = jnp.sum(p * dp, axis=-1, keepdims=True)
        ds = (scale * p * (dp - delta)).astype(jnp.bfloat16)
        pb = p.astype(jnp.bfloat16)
        dq2 = jnp.dot(ds, kw, preferred_element_type=jnp.float32)
        dq_ref[pl.ds(r0, BLOCK_Q), :] = jnp.concatenate(
            [dq2[:BLOCK_Q], dq2[BLOCK_Q:]], axis=1).astype(dq_ref.dtype)
        q2t = jnp.concatenate([q_t[:d, pl.ds(r0, BLOCK_Q)], q_t[d:, pl.ds(r0, BLOCK_Q)]], axis=1)
        do2t = jnp.concatenate([do_t[:d, pl.ds(r0, BLOCK_Q)], do_t[d:, pl.ds(r0, BLOCK_Q)]], axis=1)
        dkacc[:, pl.ds(r0, span)] += jnp.dot(q2t, ds, preferred_element_type=jnp.float32)
        dvacc[:, pl.ds(r0, span)] += jnp.dot(do2t, pb, preferred_element_type=jnp.float32)
        return carry

    if finish:
        @pl.when(pl.program_id(0) == 0)
        def _():
            gk_ref[...] = dko_old[...].astype(gk_ref.dtype)
            gv_ref[...] = dvo_old[...].astype(gv_ref.dtype)
            gk_ref[rows - w:, :] = (dko_old[rows - w:, :]
                                    + back_old[0].astype(jnp.float32)).astype(gk_ref.dtype)
            gv_ref[rows - w:, :] = (dvo_old[rows - w:, :]
                                    + back_old[1].astype(jnp.float32)).astype(gv_ref.dtype)

    lax.fori_loop(0, rows // BLOCK_Q, body, 0)
    dko_ref[...] = dkacc[:, w:w + rows].T
    dvo_ref[...] = dvacc[:, w:w + rows].T
    dprev_ref[0] = dkacc[:, 0:w].T.astype(dprev_ref.dtype)
    dprev_ref[1] = dvacc[:, 0:w].T.astype(dprev_ref.dtype)


def attention_head(group, reach_col, queries, output_gradient, queries_t, gradient_t,
                   keys, values, previous, dq_buf, older, grad_bufs):
    rows, q_width = queries.shape
    kv_width = keys.shape[1]
    d = HEAD_DIMENSION
    w = WINDOW_TOKENS
    h0, n = group
    q_spec = pl.BlockSpec((rows, 2 * d), lambda i: (0, h0 + i))
    own_spec = pl.BlockSpec((rows, d), lambda i: (0, h0 + i))
    col_spec = pl.BlockSpec((rows, d), lambda i: (0, i))
    prev_spec = pl.BlockSpec((2, w, d), lambda i: (0, 0, i))
    any_spec = pl.BlockSpec(memory_space=pl.ANY)
    finish = older is not None
    t_spec = pl.BlockSpec((2 * d, rows), lambda i: (h0 + i, 0))
    in_specs = [pl.BlockSpec((rows, 1), lambda i: (0, 0)),
                q_spec, q_spec, own_spec, own_spec, prev_spec, t_spec, t_spec]
    operands = [reach_col, queries, output_gradient, keys, values, previous,
                queries_t, gradient_t]
    out_specs = [q_spec, col_spec, col_spec, prev_spec]
    out_shape = [
        jax.ShapeDtypeStruct((rows, q_width), jnp.bfloat16),
        jax.ShapeDtypeStruct((rows, n * d), jnp.float32),
        jax.ShapeDtypeStruct((rows, n * d), jnp.float32),
        jax.ShapeDtypeStruct((2, w, n * d), jnp.bfloat16),
    ]
    aliases = {}
    if finish:
        old0, old_n = older[0]
        whole_spec = pl.BlockSpec((rows, old_n * d), lambda i: (0, 0))
        in_specs += [whole_spec, whole_spec, pl.BlockSpec((2, w, old_n * d), lambda i: (0, 0, 0))]
        operands += list(older[1:])
        old_spec = pl.BlockSpec((rows, old_n * d), lambda i: (0, old0 // old_n))
        out_specs += [old_spec, old_spec]
        out_shape += [jax.ShapeDtypeStruct((rows, kv_width), jnp.bfloat16)] * 2
    buffers = ([] if dq_buf is None else [(dq_buf, 0)]) + (
        [] if grad_bufs is None else [(grad_bufs[0], 4), (grad_bufs[1], 5)])
    for buf, out_index in buffers:
        aliases[len(operands)] = out_index
        in_specs.append(any_spec)
        operands.append(buf)
    flops = n * VPU_FACTOR * (rows // BLOCK_Q) * 5 * 2 * (2 * BLOCK_Q) * (BLOCK_Q + w) * d
    cost = pl.CostEstimate(
        flops=flops,
        transcendentals=n * rows * 2 * (BLOCK_Q + w),
        bytes_accessed=n * 2 * (3 * rows * 2 * d + 2 * rows * d + 4 * w * d) + 4 * 2 * rows * d,
    )
    return pl.pallas_call(
        functools.partial(attention_kernel, finish),
        name="attention_backward",
        grid=(n,),
        in_specs=in_specs,
        out_specs=out_specs,
        out_shape=out_shape,
        scratch_shapes=[
            pltpu.VMEM((w + rows, d), jnp.bfloat16),
            pltpu.VMEM((w + rows, d), jnp.bfloat16),
            pltpu.VMEM((d, w + rows), jnp.float32),
            pltpu.VMEM((d, w + rows), jnp.float32),
        ],
        input_output_aliases=aliases,
        compiler_params=pltpu.CompilerParams(dimension_semantics=("arbitrary",)),
        cost_estimate=cost,
    )(*operands)


def head_groups(heads):
    size = GROUP_HEADS if heads % GROUP_HEADS == 0 else 1
    return [(h0, size) for h0 in range(0, heads, size)]


def finish_columns(grad, group, own, back):
    rows = own.shape[0]
    w = WINDOW_TOKENS
    d = HEAD_DIMENSION
    total = own.at[rows - w:].add(back.astype(jnp.float32)).astype(jnp.bfloat16)
    return lax.dynamic_update_slice(grad, total, (0, group[0] * d))


def on_device(queries, keys, values, output_gradient, reach):
    rows, q_width = queries.shape
    kv_width = keys.shape[1]
    d = HEAD_DIMENSION
    w = WINDOW_TOKENS
    groups = head_groups(kv_width // d)
    heads = len(groups)
    reach_col = reach.reshape(rows, 1)
    queries_t = queries.T
    gradient_t = output_gradient.T
    sends = [jnp.stack([keys[rows - w:, h0 * d:(h0 + n) * d], values[rows - w:, h0 * d:(h0 + n) * d]])
             for h0, n in groups]
    arrived = {0: doc_shift(sends[0], 1)}
    dq_buf = None
    grad_bufs = None
    pending = []
    for g in range(heads):
        for later in range(g + 1, min(g + SEND_DEPTH, heads - 1) + 1):
            if later not in arrived:
                gated, arrived[g] = lax.optimization_barrier((sends[later], arrived[g]))
                arrived[later] = doc_shift(gated, 1)
        older = pending.pop(0) if len(pending) >= FINISH_LAG else None
        outs = attention_head(
            groups[g], reach_col, queries, output_gradient, queries_t, gradient_t, keys, values, arrived.pop(g),
            dq_buf, older, grad_bufs)
        dq_buf, dk_own, dv_own, dprev = outs[:4]
        if older is not None:
            grad_bufs = tuple(outs[4:6])
        pending.append((groups[g], dk_own, dv_own, doc_shift(dprev, -1)))
    if grad_bufs is None:
        grad_bufs = (jnp.zeros((rows, kv_width), jnp.bfloat16),) * 2
    grad_keys, grad_values = grad_bufs
    for h, dk_own, dv_own, back in pending:
        grad_keys = finish_columns(grad_keys, h, dk_own, back[0])
        grad_values = finish_columns(grad_values, h, dv_own, back[1])
    return (dq_buf, grad_keys, grad_values)


def solution(mesh):
    placed = (
        P(("slab", "ctx"), None),
        P(("slab", "ctx"), None),
        P(("slab", "ctx"), None),
        P(("slab", "ctx"), None),
        P(("slab", "ctx")),
    )
    return jax.shard_map(
        on_device,
        mesh=mesh,
        in_specs=placed,
        out_specs=(P(("slab", "ctx"), None), P(("slab", "ctx"), None), P(("slab", "ctx"), None)),
        check_vma=False,
    )
```

```python
import functools

import jax
import jax.numpy as jnp
from jax import lax
from jax.experimental import pallas as pl
from jax.experimental.pallas import tpu as pltpu
from jax.sharding import PartitionSpec as P

HEAD_DIMENSION = 128
WINDOW_TOKENS = 1024
QPRE = 168
LOG2_E = 1.4426950408889634
BLOCK_Q = 256
VPU_FACTOR = 5
SEND_DEPTH = 2
FINISH_LAG = 2
GROUP_HEADS = 4

NT_DIMS = (((1,), (1,)), ((), ()))
TN_DIMS = (((0,), (0,)), ((), ()))


def doc_shift(x, by):
    count = lax.axis_size("slab") * lax.axis_size("ctx")
    pairs = [(i, i + by) for i in range(count) if 0 <= i + by < count]
    return lax.ppermute(x, ("slab", "ctx"), pairs)


def attention_kernel(finish, reach_ref, q_ref, do_ref, ko_ref, vo_ref, prev_ref, q_t, do_t,
                     *refs):
    kext, vext, dkacc, dvacc = refs[-4:]
    if finish:
        dko_old, dvo_old, back_old = refs[:3]
        dq_ref, dko_ref, dvo_ref, dprev_ref, gk_ref, gv_ref = refs[-10:-4]
    else:
        dq_ref, dko_ref, dvo_ref, dprev_ref = refs[-8:-4]
    rows = q_ref.shape[0]
    d = HEAD_DIMENSION
    w = WINDOW_TOKENS
    span = BLOCK_Q + w
    scale = jnp.float32(QPRE ** (-0.5))

    kext[0:w, :] = prev_ref[0]
    kext[w:w + rows, :] = ko_ref[...]
    vext[0:w, :] = prev_ref[1]
    vext[w:w + rows, :] = vo_ref[...]
    dkacc[...] = jnp.zeros_like(dkacc)
    dvacc[...] = jnp.zeros_like(dvacc)

    offsets = (lax.broadcasted_iota(jnp.int32, (BLOCK_Q, span), 1)
               - lax.broadcasted_iota(jnp.int32, (BLOCK_Q, span), 0))

    def body(b, carry):
        r0 = pl.multiple_of(b * BLOCK_Q, BLOCK_Q)
        q = q_ref[pl.ds(r0, BLOCK_Q), :]
        do = do_ref[pl.ds(r0, BLOCK_Q), :]
        q2 = jnp.concatenate([q[:, :d], q[:, d:]], axis=0)
        do2 = jnp.concatenate([do[:, :d], do[:, d:]], axis=0)
        kw = kext[pl.ds(r0, span), :]
        vw = vext[pl.ds(r0, span), :]
        reach = reach_ref[pl.ds(r0, BLOCK_Q), :]
        visible = (offsets <= w) & (offsets > w - reach)
        s = lax.dot_general(q2, kw, NT_DIMS, preferred_element_type=jnp.float32)
        s = jnp.where(visible[None], s.reshape(2, BLOCK_Q, span), -jnp.inf).reshape(2 * BLOCK_Q, span)
        top = jnp.max(s, axis=-1, keepdims=True)
        e = jnp.exp2((s - top) * (scale * LOG2_E))
        total = jnp.sum(e, axis=-1, keepdims=True)
        p = e * (1.0 / total)
        dp = lax.dot_general(do2, vw, NT_DIMS, preferred_element_type=jnp.float32)
        delta = jnp.sum(p * dp, axis=-1, keepdims=True)
        ds = (scale * p * (dp - delta)).astype(jnp.bfloat16)
        pb = p.astype(jnp.bfloat16)
        dq2 = jnp.dot(ds, kw, preferred_element_type=jnp.float32)
        dq_ref[pl.ds(r0, BLOCK_Q), :] = jnp.concatenate(
            [dq2[:BLOCK_Q], dq2[BLOCK_Q:]], axis=1).astype(dq_ref.dtype)
        q2t = jnp.concatenate([q_t[:d, pl.ds(r0, BLOCK_Q)], q_t[d:, pl.ds(r0, BLOCK_Q)]], axis=1)
        do2t = jnp.concatenate([do_t[:d, pl.ds(r0, BLOCK_Q)], do_t[d:, pl.ds(r0, BLOCK_Q)]], axis=1)
        dkacc[:, pl.ds(r0, span)] += jnp.dot(q2t, ds, preferred_element_type=jnp.float32)
        dvacc[:, pl.ds(r0, span)] += jnp.dot(do2t, pb, preferred_element_type=jnp.float32)
        return carry

    if finish:
        @pl.when(pl.program_id(0) == 0)
        def _():
            gk_ref[...] = dko_old[...].astype(gk_ref.dtype)
            gv_ref[...] = dvo_old[...].astype(gv_ref.dtype)
            gk_ref[rows - w:, :] = (dko_old[rows - w:, :]
                                    + back_old[0].astype(jnp.float32)).astype(gk_ref.dtype)
            gv_ref[rows - w:, :] = (dvo_old[rows - w:, :]
                                    + back_old[1].astype(jnp.float32)).astype(gv_ref.dtype)

    lax.fori_loop(0, rows // BLOCK_Q, body, 0, unroll=True)
    dko_ref[...] = dkacc[:, w:w + rows].T
    dvo_ref[...] = dvacc[:, w:w + rows].T
    dprev_ref[0] = dkacc[:, 0:w].T.astype(dprev_ref.dtype)
    dprev_ref[1] = dvacc[:, 0:w].T.astype(dprev_ref.dtype)


def attention_head(group, reach_col, queries, output_gradient, queries_t, gradient_t,
                   keys, values, previous, dq_buf, older, grad_bufs):
    rows, q_width = queries.shape
    kv_width = keys.shape[1]
    d = HEAD_DIMENSION
    w = WINDOW_TOKENS
    h0, n = group
    q_spec = pl.BlockSpec((rows, 2 * d), lambda i: (0, h0 + i))
    own_spec = pl.BlockSpec((rows, d), lambda i: (0, h0 + i))
    col_spec = pl.BlockSpec((rows, d), lambda i: (0, i))
    prev_spec = pl.BlockSpec((2, w, d), lambda i: (0, 0, i))
    any_spec = pl.BlockSpec(memory_space=pl.ANY)
    finish = older is not None
    t_spec = pl.BlockSpec((2 * d, rows), lambda i: (h0 + i, 0))
    in_specs = [pl.BlockSpec((rows, 1), lambda i: (0, 0)),
                q_spec, q_spec, own_spec, own_spec, prev_spec, t_spec, t_spec]
    operands = [reach_col, queries, output_gradient, keys, values, previous,
                queries_t, gradient_t]
    out_specs = [q_spec, col_spec, col_spec, prev_spec]
    out_shape = [
        jax.ShapeDtypeStruct((rows, q_width), jnp.bfloat16),
        jax.ShapeDtypeStruct((rows, n * d), jnp.float32),
        jax.ShapeDtypeStruct((rows, n * d), jnp.float32),
        jax.ShapeDtypeStruct((2, w, n * d), jnp.bfloat16),
    ]
    aliases = {}
    if finish:
        old0, old_n = older[0]
        whole_spec = pl.BlockSpec((rows, old_n * d), lambda i: (0, 0))
        in_specs += [whole_spec, whole_spec, pl.BlockSpec((2, w, old_n * d), lambda i: (0, 0, 0))]
        operands += list(older[1:])
        old_spec = pl.BlockSpec((rows, old_n * d), lambda i: (0, old0 // old_n))
        out_specs += [old_spec, old_spec]
        out_shape += [jax.ShapeDtypeStruct((rows, kv_width), jnp.bfloat16)] * 2
    buffers = ([] if dq_buf is None else [(dq_buf, 0)]) + (
        [] if grad_bufs is None else [(grad_bufs[0], 4), (grad_bufs[1], 5)])
    for buf, out_index in buffers:
        aliases[len(operands)] = out_index
        in_specs.append(any_spec)
        operands.append(buf)
    flops = n * VPU_FACTOR * (rows // BLOCK_Q) * 5 * 2 * (2 * BLOCK_Q) * (BLOCK_Q + w) * d
    cost = pl.CostEstimate(
        flops=flops,
        transcendentals=n * rows * 2 * (BLOCK_Q + w),
        bytes_accessed=n * 2 * (3 * rows * 2 * d + 2 * rows * d + 4 * w * d) + 4 * 2 * rows * d,
    )
    return pl.pallas_call(
        functools.partial(attention_kernel, finish),
        name="attention_backward",
        grid=(n,),
        in_specs=in_specs,
        out_specs=out_specs,
        out_shape=out_shape,
        scratch_shapes=[
            pltpu.VMEM((w + rows, d), jnp.bfloat16),
            pltpu.VMEM((w + rows, d), jnp.bfloat16),
            pltpu.VMEM((d, w + rows), jnp.float32),
            pltpu.VMEM((d, w + rows), jnp.float32),
        ],
        input_output_aliases=aliases,
        compiler_params=pltpu.CompilerParams(dimension_semantics=("arbitrary",)),
        cost_estimate=cost,
    )(*operands)


def head_groups(heads):
    size = GROUP_HEADS if heads % GROUP_HEADS == 0 else 1
    return [(h0, size) for h0 in range(0, heads, size)]


def finish_columns(grad, group, own, back):
    rows = own.shape[0]
    w = WINDOW_TOKENS
    d = HEAD_DIMENSION
    total = own.at[rows - w:].add(back.astype(jnp.float32)).astype(jnp.bfloat16)
    return lax.dynamic_update_slice(grad, total, (0, group[0] * d))


def on_device(queries, keys, values, output_gradient, reach):
    rows, q_width = queries.shape
    kv_width = keys.shape[1]
    d = HEAD_DIMENSION
    w = WINDOW_TOKENS
    groups = head_groups(kv_width // d)
    heads = len(groups)
    reach_col = reach.reshape(rows, 1)
    queries_t = queries.T
    gradient_t = output_gradient.T
    sends = [jnp.stack([keys[rows - w:, h0 * d:(h0 + n) * d], values[rows - w:, h0 * d:(h0 + n) * d]])
             for h0, n in groups]
    arrived = {0: doc_shift(sends[0], 1)}
    dq_buf = None
    grad_bufs = None
    pending = []
    for g in range(heads):
        for later in range(g + 1, min(g + SEND_DEPTH, heads - 1) + 1):
            if later not in arrived:
                gated, arrived[g] = lax.optimization_barrier((sends[later], arrived[g]))
                arrived[later] = doc_shift(gated, 1)
        older = pending.pop(0) if len(pending) >= FINISH_LAG else None
        outs = attention_head(
            groups[g], reach_col, queries, output_gradient, queries_t, gradient_t, keys, values, arrived.pop(g),
            dq_buf, older, grad_bufs)
        dq_buf, dk_own, dv_own, dprev = outs[:4]
        if older is not None:
            grad_bufs = tuple(outs[4:6])
        pending.append((groups[g], dk_own, dv_own, doc_shift(dprev, -1)))
    if grad_bufs is None:
        grad_bufs = (jnp.zeros((rows, kv_width), jnp.bfloat16),) * 2
    grad_keys, grad_values = grad_bufs
    for h, dk_own, dv_own, back in pending:
        grad_keys = finish_columns(grad_keys, h, dk_own, back[0])
        grad_values = finish_columns(grad_values, h, dv_own, back[1])
    return (dq_buf, grad_keys, grad_values)


def solution(mesh):
    placed = (
        P(("slab", "ctx"), None),
        P(("slab", "ctx"), None),
        P(("slab", "ctx"), None),
        P(("slab", "ctx"), None),
        P(("slab", "ctx")),
    )
    return jax.shard_map(
        on_device,
        mesh=mesh,
        in_specs=placed,
        out_specs=(P(("slab", "ctx"), None), P(("slab", "ctx"), None), P(("slab", "ctx"), None)),
        check_vma=False,
    )
```

```python
import functools

import jax
import jax.numpy as jnp
from jax import lax
from jax.experimental import pallas as pl
from jax.experimental.pallas import tpu as pltpu
from jax.sharding import PartitionSpec as P

HEAD_DIMENSION = 128
WINDOW_TOKENS = 1024
QPRE = 168
LOG2_E = 1.4426950408889634
BLOCK_Q = 256
VPU_FACTOR = 5
SEND_DEPTH = 2
FINISH_LAG = 2
GROUP_HEADS = 4

NT_DIMS = (((1,), (1,)), ((), ()))
TN_DIMS = (((0,), (0,)), ((), ()))


def doc_shift(x, by):
    count = lax.axis_size("slab") * lax.axis_size("ctx")
    pairs = [(i, i + by) for i in range(count) if 0 <= i + by < count]
    return lax.ppermute(x, ("slab", "ctx"), pairs)


def attention_kernel(finish, reach_ref, q_ref, do_ref, ko_ref, vo_ref, prev_ref, q_t, do_t,
                     *refs):
    kext, vext, dkacc, dvacc = refs[-4:]
    if finish:
        dko_old, dvo_old, back_old = refs[:3]
        dq_ref, dko_ref, dvo_ref, dprev_ref, gk_ref, gv_ref = refs[-10:-4]
    else:
        dq_ref, dko_ref, dvo_ref, dprev_ref = refs[-8:-4]
    rows = q_ref.shape[0]
    d = HEAD_DIMENSION
    w = WINDOW_TOKENS
    span = BLOCK_Q + w
    scale = jnp.float32(QPRE ** (-0.5))

    kext[0:w, :] = prev_ref[0]
    kext[w:w + rows, :] = ko_ref[...]
    vext[0:w, :] = prev_ref[1]
    vext[w:w + rows, :] = vo_ref[...]
    dkacc[...] = jnp.zeros_like(dkacc)
    dvacc[...] = jnp.zeros_like(dvacc)

    offsets = (lax.broadcasted_iota(jnp.int32, (BLOCK_Q, span), 1)
               - lax.broadcasted_iota(jnp.int32, (BLOCK_Q, span), 0))

    def body(b, carry):
        r0 = pl.multiple_of(b * BLOCK_Q, BLOCK_Q)
        q = q_ref[pl.ds(r0, BLOCK_Q), :]
        do = do_ref[pl.ds(r0, BLOCK_Q), :]
        q2 = jnp.concatenate([q[:, :d], q[:, d:]], axis=0)
        do2 = jnp.concatenate([do[:, :d], do[:, d:]], axis=0)
        kw = kext[pl.ds(r0, span), :]
        vw = vext[pl.ds(r0, span), :]
        reach = reach_ref[pl.ds(r0, BLOCK_Q), :]
        visible = (offsets <= w) & (offsets > w - reach)
        s = lax.dot_general(q2, kw, NT_DIMS, preferred_element_type=jnp.float32)
        s = jnp.where(visible[None], s.reshape(2, BLOCK_Q, span), -jnp.inf).reshape(2 * BLOCK_Q, span)
        top = jnp.max(s, axis=-1, keepdims=True)
        e = jnp.exp2((s - top) * (scale * LOG2_E))
        total = jnp.sum(e, axis=-1, keepdims=True)
        p = e * (1.0 / total)
        dp = lax.dot_general(do2, vw, NT_DIMS, preferred_element_type=jnp.float32)
        delta = jnp.sum(p * dp, axis=-1, keepdims=True)
        ds = (scale * p * (dp - delta)).astype(jnp.bfloat16)
        pb = p.astype(jnp.bfloat16)
        dq2 = jnp.dot(ds, kw, preferred_element_type=jnp.float32)
        dq_ref[pl.ds(r0, BLOCK_Q), :d] = dq2[:BLOCK_Q].astype(dq_ref.dtype)
        dq_ref[pl.ds(r0, BLOCK_Q), d:] = dq2[BLOCK_Q:].astype(dq_ref.dtype)
        q2t = jnp.concatenate([q_t[:d, pl.ds(r0, BLOCK_Q)], q_t[d:, pl.ds(r0, BLOCK_Q)]], axis=1)
        do2t = jnp.concatenate([do_t[:d, pl.ds(r0, BLOCK_Q)], do_t[d:, pl.ds(r0, BLOCK_Q)]], axis=1)
        dkacc[:, pl.ds(r0, span)] += jnp.dot(q2t, ds, preferred_element_type=jnp.float32)
        dvacc[:, pl.ds(r0, span)] += jnp.dot(do2t, pb, preferred_element_type=jnp.float32)
        return carry

    if finish:
        @pl.when(pl.program_id(0) == 0)
        def _():
            gk_ref[...] = dko_old[...].astype(gk_ref.dtype)
            gv_ref[...] = dvo_old[...].astype(gv_ref.dtype)
            gk_ref[rows - w:, :] = (dko_old[rows - w:, :]
                                    + back_old[0].astype(jnp.float32)).astype(gk_ref.dtype)
            gv_ref[rows - w:, :] = (dvo_old[rows - w:, :]
                                    + back_old[1].astype(jnp.float32)).astype(gv_ref.dtype)

    lax.fori_loop(0, rows // BLOCK_Q, body, 0)
    dko_ref[...] = dkacc[:, w:w + rows].T
    dvo_ref[...] = dvacc[:, w:w + rows].T
    dprev_ref[0] = dkacc[:, 0:w].T.astype(dprev_ref.dtype)
    dprev_ref[1] = dvacc[:, 0:w].T.astype(dprev_ref.dtype)


def attention_head(group, reach_col, queries, output_gradient, queries_t, gradient_t,
                   keys, values, previous, dq_buf, older, grad_bufs):
    rows, q_width = queries.shape
    kv_width = keys.shape[1]
    d = HEAD_DIMENSION
    w = WINDOW_TOKENS
    h0, n = group
    q_spec = pl.BlockSpec((rows, 2 * d), lambda i: (0, h0 + i))
    own_spec = pl.BlockSpec((rows, d), lambda i: (0, h0 + i))
    col_spec = pl.BlockSpec((rows, d), lambda i: (0, i))
    prev_spec = pl.BlockSpec((2, w, d), lambda i: (0, 0, i))
    any_spec = pl.BlockSpec(memory_space=pl.ANY)
    finish = older is not None
    t_spec = pl.BlockSpec((2 * d, rows), lambda i: (h0 + i, 0))
    in_specs = [pl.BlockSpec((rows, 1), lambda i: (0, 0)),
                q_spec, q_spec, own_spec, own_spec, prev_spec, t_spec, t_spec]
    operands = [reach_col, queries, output_gradient, keys, values, previous,
                queries_t, gradient_t]
    out_specs = [q_spec, col_spec, col_spec, prev_spec]
    out_shape = [
        jax.ShapeDtypeStruct((rows, q_width), jnp.bfloat16),
        jax.ShapeDtypeStruct((rows, n * d), jnp.float32),
        jax.ShapeDtypeStruct((rows, n * d), jnp.float32),
        jax.ShapeDtypeStruct((2, w, n * d), jnp.bfloat16),
    ]
    aliases = {}
    if finish:
        old0, old_n = older[0]
        whole_spec = pl.BlockSpec((rows, old_n * d), lambda i: (0, 0))
        in_specs += [whole_spec, whole_spec, pl.BlockSpec((2, w, old_n * d), lambda i: (0, 0, 0))]
        operands += list(older[1:])
        old_spec = pl.BlockSpec((rows, old_n * d), lambda i: (0, old0 // old_n))
        out_specs += [old_spec, old_spec]
        out_shape += [jax.ShapeDtypeStruct((rows, kv_width), jnp.bfloat16)] * 2
    buffers = ([] if dq_buf is None else [(dq_buf, 0)]) + (
        [] if grad_bufs is None else [(grad_bufs[0], 4), (grad_bufs[1], 5)])
    for buf, out_index in buffers:
        aliases[len(operands)] = out_index
        in_specs.append(any_spec)
        operands.append(buf)
    flops = n * VPU_FACTOR * (rows // BLOCK_Q) * 5 * 2 * (2 * BLOCK_Q) * (BLOCK_Q + w) * d
    cost = pl.CostEstimate(
        flops=flops,
        transcendentals=n * rows * 2 * (BLOCK_Q + w),
        bytes_accessed=n * 2 * (3 * rows * 2 * d + 2 * rows * d + 4 * w * d) + 4 * 2 * rows * d,
    )
    return pl.pallas_call(
        functools.partial(attention_kernel, finish),
        name="attention_backward",
        grid=(n,),
        in_specs=in_specs,
        out_specs=out_specs,
        out_shape=out_shape,
        scratch_shapes=[
            pltpu.VMEM((w + rows, d), jnp.bfloat16),
            pltpu.VMEM((w + rows, d), jnp.bfloat16),
            pltpu.VMEM((d, w + rows), jnp.float32),
            pltpu.VMEM((d, w + rows), jnp.float32),
        ],
        input_output_aliases=aliases,
        compiler_params=pltpu.CompilerParams(dimension_semantics=("arbitrary",)),
        cost_estimate=cost,
    )(*operands)


def head_groups(heads):
    size = GROUP_HEADS if heads % GROUP_HEADS == 0 else 1
    return [(h0, size) for h0 in range(0, heads, size)]


def finish_columns(grad, group, own, back):
    rows = own.shape[0]
    w = WINDOW_TOKENS
    d = HEAD_DIMENSION
    total = own.at[rows - w:].add(back.astype(jnp.float32)).astype(jnp.bfloat16)
    return lax.dynamic_update_slice(grad, total, (0, group[0] * d))


def on_device(queries, keys, values, output_gradient, reach):
    rows, q_width = queries.shape
    kv_width = keys.shape[1]
    d = HEAD_DIMENSION
    w = WINDOW_TOKENS
    groups = head_groups(kv_width // d)
    heads = len(groups)
    reach_col = reach.reshape(rows, 1)
    queries_t = queries.T
    gradient_t = output_gradient.T
    sends = [jnp.stack([keys[rows - w:, h0 * d:(h0 + n) * d], values[rows - w:, h0 * d:(h0 + n) * d]])
             for h0, n in groups]
    arrived = {0: doc_shift(sends[0], 1)}
    dq_buf = None
    grad_bufs = None
    pending = []
    for g in range(heads):
        for later in range(g + 1, min(g + SEND_DEPTH, heads - 1) + 1):
            if later not in arrived:
                gated, arrived[g] = lax.optimization_barrier((sends[later], arrived[g]))
                arrived[later] = doc_shift(gated, 1)
        older = pending.pop(0) if len(pending) >= FINISH_LAG else None
        outs = attention_head(
            groups[g], reach_col, queries, output_gradient, queries_t, gradient_t, keys, values, arrived.pop(g),
            dq_buf, older, grad_bufs)
        dq_buf, dk_own, dv_own, dprev = outs[:4]
        if older is not None:
            grad_bufs = tuple(outs[4:6])
        pending.append((groups[g], dk_own, dv_own, doc_shift(dprev, -1)))
    if grad_bufs is None:
        grad_bufs = (jnp.zeros((rows, kv_width), jnp.bfloat16),) * 2
    grad_keys, grad_values = grad_bufs
    for h, dk_own, dv_own, back in pending:
        grad_keys = finish_columns(grad_keys, h, dk_own, back[0])
        grad_values = finish_columns(grad_values, h, dv_own, back[1])
    return (dq_buf, grad_keys, grad_values)


def solution(mesh):
    placed = (
        P(("slab", "ctx"), None),
        P(("slab", "ctx"), None),
        P(("slab", "ctx"), None),
        P(("slab", "ctx"), None),
        P(("slab", "ctx")),
    )
    return jax.shard_map(
        on_device,
        mesh=mesh,
        in_specs=placed,
        out_specs=(P(("slab", "ctx"), None), P(("slab", "ctx"), None), P(("slab", "ctx"), None)),
        check_vma=False,
    )
```
